256 devices in a mesh: req: 64 (over z, x, core), tp: 4 (over y).
Axes of the slice: x: 4, y: 4, z: 8, core: 2. Of those that a mesh axis runs over, the one named last changes fastest.
Arguments:
- hidden: bfloat16 [16384, 2048], P('req'), may hold values from -10.5 to 10.5
- lengths: int32 [64], replicated, may hold values from 1 to 1024, 16384 in all
- dealing: int32 [64], replicated, may hold values from 0 to 63, each once
- norm_gain: bfloat16 [2048], replicated, may hold values from 0.5 to 1.5
- w_query: bfloat16 [2048, 2048], P(None, 'tp'), may hold values from -0.125 to 0.125
- w_key: bfloat16 [2048, 1024], P(None, 'tp'), may hold values from -0.125 to 0.125
- w_value: bfloat16 [2048, 1024], P(None, 'tp'), may hold values from -0.125 to 0.125
- query_gain: bfloat16 [128], replicated, may hold values from 0.5 to 8
- key_gain: bfloat16 [128], replicated, may hold values from 0.5 to 8
- w_out: bfloat16 [2048, 2048], P(None, 'tp'), may hold values from -0.125 to 0.125
Outputs:
- hidden_out: bfloat16 [16384, 2048], P('req', 'tp')
- kv_cache: bfloat16 [2, 64, 1024, 1024], P(None, 'req', None, 'tp')
The draws below stay inside these ranges and needn't reach their ends.
Inputs may be any that keep to these rules, and one draw needn't show every extreme that they name: The lengths sum to 16384; the largest is exactly 1024. A permutation: dealt slot j, on device j of req, holds prompt dealing[j].
All inputs are finite; a program needn't handle non-finite values.
Results may differ from the reference program's by a relative error of at most 0.012.
The reference program's roundings to bfloat16 on the way count: a program that leaves them out, or rounds other values in their place, can miss the bound.
Values may be sent and summed in bfloat16 or wider, within the bound.
No kernel may reach another device: no remote copies, remote signals or barrier semaphores. Data moves between devices by JAX's collectives and lax.ppermute only.
A program may use at most 128 MiB of HBM per device.

```python
import math
import jax
import jax.numpy as jnp
import numpy as np
from jax import lax

D = 2048
QH = 16
KVH = 8
HD = 128
TOK_DEV = 256
PROMPTS = 64
TOKENS = 16384
SEQ = 1024
N_REQ = 64


def draw_hidden(key, part):
    noise_key = jax.random.fold_in(key, 101)
    return jnp.clip(jax.random.normal(noise_key, (TOKENS, D), jnp.float32), -4.0, 4.0).astype(jnp.bfloat16)


def draw_query_gain(key, part):
    gain_key = jax.random.fold_in(key, 201)
    return jax.random.uniform(gain_key, (HD,), jnp.float32, 0.5, 2.0).astype(jnp.bfloat16)


def draw_key_gain(key, part):
    gain_key = jax.random.fold_in(key, 202)
    return jax.random.uniform(gain_key, (HD,), jnp.float32, 0.5, 2.0).astype(jnp.bfloat16)


def levels(rng, extent, pieces, least, largest):
    factor_of = 1.0
    for position, blocks in pieces:
        steps = jax.random.uniform(jax.random.fold_in(jax.random.fold_in(rng, 6), position), (blocks,), jnp.float32, least / len(pieces), largest / len(pieces))
        factor_of = factor_of * jnp.repeat(jnp.exp(steps), extent[position] // blocks).reshape((-1,) + (1,) * (len(extent) - 1 - position))
    return factor_of


def profile(amount, total, bound, lean):
    weights = [(1 << 20) // math.isqrt(grade ** lean) + 1 for grade in range(2, amount + 1)]
    surplus, holding = total - bound - (amount - 1), [1] * (amount - 1)
    while surplus > 0:
        movable = [i for i in range(amount - 1) if holding[i] < bound]
        whole, budget = sum([weights[i] for i in movable]), surplus
        for i in movable:
            addition = min(bound - holding[i], max(1, budget * weights[i] // whole), surplus)
            holding[i] = holding[i] + addition
            surplus = surplus - addition
    return np.array([bound] + holding)


def ragged_sizes(own_key, count, total, bound, lean):
    if count == 2:
        one = jax.random.randint(own_key, (), max(1, total - bound), min(bound, total - 1) + 1)
        return jnp.stack([one, total - one])
    sizes = jnp.asarray(profile(count, total, bound, lean), jnp.int32)
    twos = (count - 1) // 2
    giver, taker = sizes[1:1 + 2 * twos:2], sizes[2:2 + 2 * twos:2]
    room = jnp.minimum(giver - 1, bound - taker)
    shifted = jax.random.randint(jax.random.fold_in(own_key, 1), (twos,), 0, 1 << 20) % (room + 1)
    sizes = sizes.at[1:1 + 2 * twos:2].set(giver - shifted).at[2:2 + 2 * twos:2].set(taker + shifted)
    return sizes[jax.random.permutation(jax.random.fold_in(own_key, 2), count)]


def scatter_about(stream_key, dims, width, most, shards=(), kind=jnp.bfloat16):
    values = jax.random.normal(stream_key, dims, jnp.float32) * width
    if len(shards) > 0:
        values = levels(stream_key, dims, shards, -0.22, 0.18) * values
    return jnp.clip(values, min=-most, max=most).astype(kind)


def setup_inputs(seed: int = 0) -> dict:
    key_list = jax.random.split(jax.random.key(seed), 11)
    hidden = draw_hidden(jax.random.fold_in(key_list[10], 71), 0)
    lengths = ragged_sizes(key_list[1], PROMPTS, TOKENS, SEQ, 1).astype(jnp.int32)
    dealing = jax.random.permutation(key_list[2], PROMPTS).astype(jnp.int32)
    norm_gain = jnp.clip(1.0 + 0.1 * jax.random.normal(key_list[3], (D,), jnp.float32), 0.5, 1.5).astype(jnp.bfloat16)
    w_query = scatter_about(key_list[4], (D, QH * HD), D ** -0.5, 0.125, ((1, 4),))
    w_key = scatter_about(key_list[5], (D, KVH * HD), D ** -0.5, 0.125, ((1, 4),))
    w_value = scatter_about(key_list[6], (D, KVH * HD), D ** -0.5, 0.125, ((1, 4),))
    query_gain = draw_query_gain(jax.random.fold_in(key_list[10], 71), 0)
    key_gain = draw_key_gain(jax.random.fold_in(key_list[10], 71), 0)
    w_out = scatter_about(key_list[9], (QH * HD, D), (QH * HD) ** -0.5, 0.125, ((1, 4),))
    return dict(hidden=hidden, lengths=lengths, dealing=dealing, norm_gain=norm_gain, w_query=w_query, w_key=w_key, w_value=w_value, query_gain=query_gain, key_gain=key_gain, w_out=w_out)


EPS = 1e-06
THETA = 1000000.0

def rms_rows(values, scale_gain):
    inv_rms = lax.rsqrt(lax.optimization_barrier(jnp.mean(values * values, axis=-1, keepdims=True)) + EPS)
    return values * inv_rms * scale_gain

def rotate(values, positions):
    features = values.shape[-1]
    half_width = features // 2
    frequency = THETA ** (-(jnp.arange(half_width).astype(jnp.float32) * 2.0) / features)
    angles = positions.astype(jnp.float32)[:, None] * frequency[None, :]
    cosine = jnp.cos(angles)[:, None, :]
    sine_part = jnp.sin(angles)[:, None, :]
    first_half = values[..., :half_width]
    second_half = values[..., half_width:]
    return jnp.concatenate([first_half * cosine - second_half * sine_part, second_half * cosine + first_half * sine_part], axis=-1)

def attend_slot(operands):
    query_slot, key_slot, value_slot, slot_length = operands
    group_size = QH // KVH
    queries = query_slot.reshape(SEQ, KVH, group_size, HD).astype(jnp.float32)
    keys_split = key_slot.reshape(SEQ, KVH, HD).astype(jnp.float32)
    values_split = value_slot.reshape(SEQ, KVH, HD).astype(jnp.float32)
    scores = jnp.einsum('qkgd,skd->kgqs', queries, keys_split) * HD ** (-0.5)
    offsets = jnp.arange(SEQ, dtype=jnp.int32)
    allowed = (offsets[None, :] <= offsets[:, None]) & (offsets[None, :] < slot_length)
    scores = jnp.where(allowed[None, None], scores, -jnp.inf)
    row_max = lax.optimization_barrier(jnp.max(scores, axis=-1, keepdims=True))
    weights = jnp.exp(scores - row_max)
    weights = (weights / lax.optimization_barrier(jnp.sum(weights, axis=-1, keepdims=True))).astype(jnp.bfloat16)
    mixture = jnp.einsum('kgqs,skd->qkgd', weights.astype(jnp.float32), values_split)
    return mixture.astype(jnp.bfloat16).reshape(SEQ, QH * HD)

def reference(hidden, lengths, dealing, norm_gain, w_query, w_key, w_value, query_gain, key_gain, w_out):
    prompt_ends = jnp.cumsum(lengths).astype(jnp.int32)
    starts = (prompt_ends - lengths).astype(jnp.int32)
    packed_ids = jnp.arange(TOKENS, dtype=jnp.int32)
    segment = lax.optimization_barrier(jnp.sum((packed_ids[:, None] >= prompt_ends[None, :]).astype(jnp.int32), axis=1)).astype(jnp.int32)
    positions = (packed_ids - starts[segment]).astype(jnp.int32)
    packed = hidden.reshape(N_REQ, TOK_DEV, D).transpose(1, 0, 2).reshape(TOKENS, D)
    normed = rms_rows(packed.astype(jnp.float32), norm_gain.astype(jnp.float32)).astype(jnp.bfloat16)
    query_rows = jnp.dot(normed, w_query, preferred_element_type=jnp.float32).reshape(TOKENS, QH, HD)
    key_rows = jnp.dot(normed, w_key, preferred_element_type=jnp.float32).reshape(TOKENS, KVH, HD)
    value_rows = jnp.dot(normed, w_value, preferred_element_type=jnp.float32).astype(jnp.bfloat16)
    query_rows = rotate(rms_rows(query_rows, query_gain.astype(jnp.float32)), positions).astype(jnp.bfloat16).reshape(TOKENS, QH * HD)
    key_rows = rotate(rms_rows(key_rows, key_gain.astype(jnp.float32)), positions).astype(jnp.bfloat16).reshape(TOKENS, KVH * HD)
    offsets = jnp.arange(SEQ, dtype=jnp.int32)
    slot_lengths = lengths[dealing].astype(jnp.int32)
    slot_starts = starts[dealing].astype(jnp.int32)
    is_valid = offsets[None, :] < slot_lengths[:, None]
    row_ids = jnp.where(is_valid, slot_starts[:, None] + offsets[None, :], 0).astype(jnp.int32)

    def pick(source_table):
        return jnp.where(is_valid[:, :, None], source_table[row_ids], jnp.zeros((), source_table.dtype))
    query_slots = pick(query_rows)
    key_slots = pick(key_rows)
    value_slots = pick(value_rows)
    mixture = lax.map(attend_slot, (query_slots, key_slots, value_slots, slot_lengths)).reshape(PROMPTS * SEQ, QH * HD)
    inverse = jnp.zeros((PROMPTS,), jnp.int32).at[dealing].set(jnp.arange(PROMPTS, dtype=jnp.int32))
    slot_rows = (inverse[segment] * SEQ + positions).astype(jnp.int32)
    attended_packed = mixture[slot_rows]
    attended = attended_packed.reshape(TOK_DEV, N_REQ, QH * HD).transpose(1, 0, 2).reshape(TOKENS, QH * HD)
    branch = lax.optimization_barrier(jnp.dot(attended, w_out, preferred_element_type=jnp.float32).astype(jnp.bfloat16))
    hidden_out = (hidden.astype(jnp.float32) + branch.astype(jnp.float32)).astype(jnp.bfloat16)
    kv_cache = jnp.stack([key_slots, value_slots])
    return (hidden_out, kv_cache)
```

```python
import jax
import jax.numpy as jnp
from jax import lax
from jax.sharding import PartitionSpec as P

EPS = 1e-06
THETA = 1000000.0


def rms_rows(values, scale_gain):
    inv_rms = lax.rsqrt(jnp.mean(values * values, axis=-1, keepdims=True) + EPS)
    return values * inv_rms * scale_gain


def rotate(values, positions):
    features = values.shape[-1]
    half_width = features // 2
    frequency = THETA ** (-(jnp.arange(half_width).astype(jnp.float32) * 2.0) / features)
    angles = positions.astype(jnp.float32)[:, None] * frequency[None, :]
    cosine = jnp.cos(angles)[:, None, :]
    sine_part = jnp.sin(angles)[:, None, :]
    first_half = values[..., :half_width]
    second_half = values[..., half_width:]
    return jnp.concatenate(
        [
            first_half * cosine - second_half * sine_part,
            second_half * cosine + first_half * sine_part,
        ],
        axis=-1,
    )


def project(normed, w_query, w_key, w_value, query_gain, key_gain, positions):
    head_dim = query_gain.shape[0]
    row_count = normed.shape[0]
    query_rows = jnp.dot(normed, w_query, preferred_element_type=jnp.float32).reshape(
        row_count, -1, head_dim
    )
    key_rows = jnp.dot(normed, w_key, preferred_element_type=jnp.float32).reshape(
        row_count, -1, head_dim
    )
    value_rows = jnp.dot(normed, w_value, preferred_element_type=jnp.float32).astype(jnp.bfloat16)
    query_rows = rotate(rms_rows(query_rows, query_gain.astype(jnp.float32)), positions).astype(
        jnp.bfloat16
    )
    key_rows = rotate(rms_rows(key_rows, key_gain.astype(jnp.float32)), positions).astype(
        jnp.bfloat16
    )
    return (query_rows.reshape(row_count, -1), key_rows.reshape(row_count, -1), value_rows)


def attend(query_slot, key_slot, value_slot, prompt_length, head_dim):
    slot_len, query_width = query_slot.shape
    kv_heads = key_slot.shape[1] // head_dim
    group_size = query_width // head_dim // kv_heads
    queries = query_slot.reshape(slot_len, kv_heads, group_size, head_dim)
    keys_split = key_slot.reshape(slot_len, kv_heads, head_dim)
    values_split = value_slot.reshape(slot_len, kv_heads, head_dim)
    scores = jnp.einsum(
        "qkgd,skd->kgqs", queries, keys_split, preferred_element_type=jnp.float32
    ) * head_dim ** (-0.5)
    offsets = jnp.arange(slot_len, dtype=jnp.int32)
    allowed = (offsets[None, :] <= offsets[:, None]) & (offsets[None, :] < prompt_length)
    scores = jnp.where(allowed[None, None], scores, -jnp.inf)
    row_max = jnp.max(scores, axis=-1, keepdims=True)
    weights = jnp.exp(scores - row_max)
    weights = (weights / jnp.sum(weights, axis=-1, keepdims=True)).astype(jnp.bfloat16)
    mixture = jnp.einsum(
        "kgqs,skd->qkgd", weights, values_split, preferred_element_type=jnp.float32
    )
    return mixture.astype(jnp.bfloat16).reshape(slot_len, query_width)


def on_device(
    hidden, lengths, dealing, norm_gain, w_query, w_key, w_value, query_gain, key_gain, w_out
):
    devices = lax.axis_size("req")
    home_index = lax.axis_index("req")
    slice_index = lax.axis_index("tp")
    tok_rows, features = hidden.shape
    head_dim = query_gain.shape[0]
    out_width = w_out.shape[1]
    q_width = w_query.shape[1]
    k_width = w_key.shape[1]
    slot_len = 4 * tok_rows
    capacity = slot_len // devices
    prompt_total = lengths.shape[0]
    prompt_ids = jnp.arange(prompt_total, dtype=jnp.int32)
    prompt_ends = jnp.cumsum(lengths)
    starts = prompt_ends - lengths
    packed_ids = jnp.arange(tok_rows, dtype=jnp.int32) * devices + home_index
    segment = jnp.sum((packed_ids[:, None] >= prompt_ends[None, :]).astype(jnp.int32), axis=1)
    seg_onehot = (segment[:, None] == prompt_ids[None, :]).astype(jnp.int32)
    positions = packed_ids - jnp.sum(seg_onehot * starts[None, :], axis=1)
    inverse = jnp.zeros((prompt_total,), jnp.int32).at[dealing].set(prompt_ids)
    deal_hot = (dealing[:, None] == prompt_ids[None, :]).astype(jnp.int32)
    dealt_starts = jnp.sum(deal_hot * starts[None, :], axis=1)
    dealt_lengths = jnp.sum(deal_hot * lengths[None, :], axis=1)
    first_offset = jnp.mod(home_index - dealt_starts, devices)
    ranks = jnp.arange(capacity, dtype=jnp.int32)
    slot_offset = first_offset[None, :] + ranks[:, None] * devices
    send_valid = slot_offset < dealt_lengths[None, :]
    send_rows = jnp.where(
        send_valid, (dealt_starts[None, :] + slot_offset - home_index) // devices, 0
    ).reshape(-1)
    my_start = lax.dynamic_index_in_dim(dealt_starts, home_index, 0, keepdims=False)
    my_length = lax.dynamic_index_in_dim(dealt_lengths, home_index, 0, keepdims=False)
    roll_shift = jnp.mod(my_start, devices)
    my_slots = jnp.sum(seg_onehot * inverse[None, :], axis=1)
    back_rows = positions // devices * devices + my_slots
    gain_values = norm_gain.astype(jnp.float32)
    normed = rms_rows(hidden.astype(jnp.float32), gain_values).astype(jnp.bfloat16)
    query_rows, key_rows, value_rows = project(
        normed, w_query, w_key, w_value, query_gain, key_gain, positions
    )
    qkv_rows = jnp.concatenate([query_rows, key_rows, value_rows], axis=1)
    picked = jnp.take(qkv_rows, send_rows, axis=0).reshape(capacity, devices, qkv_rows.shape[1])
    arrived = lax.all_to_all(
        jnp.where(send_valid[:, :, None], picked, jnp.zeros((), qkv_rows.dtype)),
        "req",
        split_axis=1,
        concat_axis=1,
        tiled=True,
    )
    slot_rows = jnp.roll(arrived, -roll_shift, axis=1).reshape(slot_len, arrived.shape[2])
    query_slot = slot_rows[:, :q_width]
    key_slot = slot_rows[:, q_width : q_width + k_width]
    value_slot = slot_rows[:, q_width + k_width :]
    mixture = attend(query_slot, key_slot, value_slot, my_length, head_dim)
    sendback = jnp.roll(mixture.reshape(capacity, devices, mixture.shape[1]), roll_shift, axis=1)
    returned = lax.all_to_all(sendback, "req", split_axis=1, concat_axis=1, tiled=True)
    attended = jnp.take(returned.reshape(capacity * devices, -1), back_rows, axis=0)
    kv_cache = jnp.stack([key_slot, value_slot])[:, None]
    summed = jnp.dot(
        lax.all_gather(attended, "tp", axis=1, tiled=True),
        w_out,
        preferred_element_type=jnp.float32,
    )
    branch = lax.optimization_barrier(summed.astype(jnp.bfloat16))
    residual = lax.dynamic_slice_in_dim(hidden, slice_index * out_width, out_width, 1)
    hidden_out = (residual.astype(jnp.float32) + branch.astype(jnp.float32)).astype(jnp.bfloat16)
    return (hidden_out, kv_cache)


def solution(mesh):
    in_specs = (
        P("req", None),
        P(),
        P(),
        P(),
        P(None, "tp"),
        P(None, "tp"),
        P(None, "tp"),
        P(),
        P(),
        P(None, "tp"),
    )
    out_specs = (P("req", "tp"), P(None, "req", None, "tp"))
    return jax.shard_map(
        on_device, mesh=mesh, in_specs=in_specs, out_specs=out_specs, check_vma=False
    )
```

```python
import jax
import jax.numpy as jnp
from jax import lax
from jax.experimental import pallas as pl
from jax.experimental.pallas import tpu as pltpu
from jax.sharding import PartitionSpec as P

EPS = 1e-06
THETA = 1000000.0


def rms_rows(values, scale_gain):
    inv_rms = lax.rsqrt(jnp.mean(values * values, axis=-1, keepdims=True) + EPS)
    return values * inv_rms * scale_gain


def rotate(values, positions):
    features = values.shape[-1]
    half_width = features // 2
    frequency = THETA ** (-(jnp.arange(half_width).astype(jnp.float32) * 2.0) / features)
    angles = positions.astype(jnp.float32)[:, None] * frequency[None, :]
    cosine = jnp.cos(angles)[:, None, :]
    sine_part = jnp.sin(angles)[:, None, :]
    first_half = values[..., :half_width]
    second_half = values[..., half_width:]
    return jnp.concatenate(
        [
            first_half * cosine - second_half * sine_part,
            second_half * cosine + first_half * sine_part,
        ],
        axis=-1,
    )


def project(normed, w_query, w_key, w_value, query_gain, key_gain, positions):
    head_dim = query_gain.shape[0]
    row_count = normed.shape[0]
    query_rows = jnp.dot(normed, w_query, preferred_element_type=jnp.float32).reshape(
        row_count, -1, head_dim
    )
    key_rows = jnp.dot(normed, w_key, preferred_element_type=jnp.float32).reshape(
        row_count, -1, head_dim
    )
    value_rows = jnp.dot(normed, w_value, preferred_element_type=jnp.float32).astype(jnp.bfloat16)
    query_rows = rotate(rms_rows(query_rows, query_gain.astype(jnp.float32)), positions).astype(
        jnp.bfloat16
    )
    key_rows = rotate(rms_rows(key_rows, key_gain.astype(jnp.float32)), positions).astype(
        jnp.bfloat16
    )
    return (query_rows.reshape(row_count, -1), key_rows.reshape(row_count, -1), value_rows)


def attention_kernel(qkv_ref, qpos_ref, kpos_ref, out_ref, *, q_width, k_width, head_dim, blocks):
    rows = qkv_ref.shape[0]
    block = rows // blocks
    kv_heads = k_width // head_dim
    group = q_width // head_dim // kv_heads
    scale = head_dim ** (-0.5)
    for i in range(blocks):
        key_rows = block * (i + 1)
        rows_here = pl.ds(i * block, block)
        allowed = kpos_ref[:, :key_rows] <= qpos_ref[rows_here, :]
        for h in range(kv_heads):
            k_col = q_width + h * head_dim
            v_col = q_width + k_width + h * head_dim
            keys = qkv_ref[:key_rows, k_col : k_col + head_dim]
            values = qkv_ref[:key_rows, v_col : v_col + head_dim]
            for g in range(group):
                q_col = (h * group + g) * head_dim
                queries = qkv_ref[rows_here, q_col : q_col + head_dim]
                scores = lax.dot_general(
                    queries,
                    keys,
                    (((1,), (1,)), ((), ())),
                    preferred_element_type=jnp.float32,
                ) * scale
                scores = jnp.where(allowed, scores, -jnp.inf)
                row_max = jnp.max(scores, axis=-1, keepdims=True)
                weights = jnp.exp(scores - row_max)
                weights = (weights / jnp.sum(weights, axis=-1, keepdims=True)).astype(jnp.bfloat16)
                mixed = jnp.dot(weights, values, preferred_element_type=jnp.float32)
                out_ref[rows_here, q_col : q_col + head_dim] = mixed.astype(out_ref.dtype)


def attend(qkv_slot, query_pos, key_pos, q_width, k_width, head_dim):
    rows = qkv_slot.shape[0]
    blocks = 4
    heads = q_width // head_dim
    causal_pairs = blocks * (blocks + 1) // 2
    pair_flops = 4 * (rows // blocks) ** 2 * head_dim
    vmem = pl.BlockSpec(memory_space=pltpu.VMEM)
    return pl.pallas_call(
        lambda *refs: attention_kernel(
            *refs, q_width=q_width, k_width=k_width, head_dim=head_dim, blocks=blocks
        ),
        out_shape=jax.ShapeDtypeStruct((rows, q_width), jnp.bfloat16),
        in_specs=[vmem, vmem, vmem],
        out_specs=vmem,
        cost_estimate=pl.CostEstimate(
            flops=heads * causal_pairs * pair_flops,
            transcendentals=heads * causal_pairs * (rows // blocks) ** 2,
            bytes_accessed=qkv_slot.size * 2 + rows * q_width * 2,
        ),
    )(qkv_slot, query_pos[:, None], key_pos[None, :])


def on_device(
    hidden, lengths, dealing, norm_gain, w_query, w_key, w_value, query_gain, key_gain, w_out
):
    devices = lax.axis_size("req")
    home_index = lax.axis_index("req")
    slice_index = lax.axis_index("tp")
    tok_rows, features = hidden.shape
    head_dim = query_gain.shape[0]
    out_width = w_out.shape[1]
    q_width = w_query.shape[1]
    k_width = w_key.shape[1]
    slot_len = 4 * tok_rows
    capacity = slot_len // devices
    prompt_total = lengths.shape[0]
    prompt_ids = jnp.arange(prompt_total, dtype=jnp.int32)
    prompt_ends = jnp.cumsum(lengths)
    starts = prompt_ends - lengths
    packed_ids = jnp.arange(tok_rows, dtype=jnp.int32) * devices + home_index
    segment = jnp.sum((packed_ids[:, None] >= prompt_ends[None, :]).astype(jnp.int32), axis=1)
    seg_onehot = (segment[:, None] == prompt_ids[None, :]).astype(jnp.int32)
    positions = packed_ids - jnp.sum(seg_onehot * starts[None, :], axis=1)
    inverse = jnp.zeros((prompt_total,), jnp.int32).at[dealing].set(prompt_ids)
    deal_hot = (dealing[:, None] == prompt_ids[None, :]).astype(jnp.int32)
    dealt_starts = jnp.sum(deal_hot * starts[None, :], axis=1)
    dealt_lengths = jnp.sum(deal_hot * lengths[None, :], axis=1)
    first_offset = jnp.mod(home_index - dealt_starts, devices)
    ranks = jnp.arange(capacity, dtype=jnp.int32)
    slot_offset = first_offset[None, :] + ranks[:, None] * devices
    send_valid = slot_offset < dealt_lengths[None, :]
    send_rows = jnp.where(
        send_valid, (dealt_starts[None, :] + slot_offset - home_index) // devices, 0
    ).reshape(-1)
    my_start = lax.dynamic_index_in_dim(dealt_starts, home_index, 0, keepdims=False)
    my_length = lax.dynamic_index_in_dim(dealt_lengths, home_index, 0, keepdims=False)
    roll_shift = jnp.mod(my_start, devices)
    my_slots = jnp.sum(seg_onehot * inverse[None, :], axis=1)
    back_rows = positions // devices * devices + my_slots
    gain_values = norm_gain.astype(jnp.float32)
    normed = rms_rows(hidden.astype(jnp.float32), gain_values).astype(jnp.bfloat16)
    query_rows, key_rows, value_rows = project(
        normed, w_query, w_key, w_value, query_gain, key_gain, positions
    )
    qkv_rows = jnp.concatenate([query_rows, key_rows, value_rows], axis=1)
    chosen = jnp.where(send_valid, send_rows.reshape(capacity, devices), -1).reshape(-1)
    one_hot = (chosen[:, None] == jnp.arange(tok_rows, dtype=jnp.int32)[None, :]).astype(
        qkv_rows.dtype
    )
    picked = jnp.dot(one_hot, qkv_rows, preferred_element_type=jnp.float32).astype(qkv_rows.dtype)
    arrived = lax.all_to_all(
        picked.reshape(capacity, devices, qkv_rows.shape[1]),
        "req",
        split_axis=1,
        concat_axis=1,
        tiled=True,
    )
    source_ids = jnp.arange(devices, dtype=jnp.int32)
    arrived_pos = (
        ranks[:, None] * devices + jnp.mod(source_ids[None, :] - my_start, devices)
    ).reshape(-1)
    key_pos = jnp.where(arrived_pos < my_length, arrived_pos, 1 << 30)
    mixture = attend(
        arrived.reshape(slot_len, arrived.shape[2]), arrived_pos, key_pos, q_width, k_width, head_dim
    )
    returned = lax.all_to_all(
        mixture.reshape(capacity, devices, mixture.shape[1]),
        "req",
        split_axis=1,
        concat_axis=1,
        tiled=True,
    )
    attended = jnp.take(returned.reshape(capacity * devices, -1), back_rows, axis=0)
    kv_rows = jnp.roll(arrived[:, :, q_width:], -roll_shift, axis=1).reshape(slot_len, -1)
    kv_cache = jnp.stack([kv_rows[:, :k_width], kv_rows[:, k_width:]])[:, None]
    tp_size = lax.axis_size("tp")
    w_rows = w_out.shape[0] // tp_size
    summed = jnp.dot(
        attended,
        lax.dynamic_slice_in_dim(w_out, slice_index * w_rows, w_rows, 0),
        preferred_element_type=jnp.float32,
    )
    for shift in range(1, tp_size):
        passed = lax.ppermute(
            attended, "tp", perm=[(i, (i + shift) % tp_size) for i in range(tp_size)]
        )
        source = jnp.mod(slice_index - shift, tp_size)
        summed = summed + jnp.dot(
            passed,
            lax.dynamic_slice_in_dim(w_out, source * w_rows, w_rows, 0),
            preferred_element_type=jnp.float32,
        )
    branch = lax.optimization_barrier(summed.astype(jnp.bfloat16))
    residual = lax.dynamic_slice_in_dim(hidden, slice_index * out_width, out_width, 1)
    hidden_out = (residual.astype(jnp.float32) + branch.astype(jnp.float32)).astype(jnp.bfloat16)
    return (hidden_out, kv_cache)


def solution(mesh):
    in_specs = (
        P("req", None),
        P(),
        P(),
        P(),
        P(None, "tp"),
        P(None, "tp"),
        P(None, "tp"),
        P(),
        P(),
        P(None, "tp"),
    )
    out_specs = (P("req", "tp"), P(None, "req", None, "tp"))
    return jax.shard_map(
        on_device, mesh=mesh, in_specs=in_specs, out_specs=out_specs, check_vma=False
    )
```

```python
import jax
import jax.numpy as jnp
from jax import lax
from jax.experimental import pallas as pl
from jax.experimental.pallas import tpu as pltpu
from jax.sharding import PartitionSpec as P

EPS = 1e-06
THETA = 1000000.0


def rms_rows(values, scale_gain):
    inv_rms = lax.rsqrt(jnp.mean(values * values, axis=-1, keepdims=True) + EPS)
    return values * inv_rms * scale_gain


def rotate(values, positions):
    features = values.shape[-1]
    half_width = features // 2
    frequency = THETA ** (-(jnp.arange(half_width).astype(jnp.float32) * 2.0) / features)
    angles = positions.astype(jnp.float32)[:, None] * frequency[None, :]
    cosine = jnp.cos(angles)[:, None, :]
    sine_part = jnp.sin(angles)[:, None, :]
    first_half = values[..., :half_width]
    second_half = values[..., half_width:]
    return jnp.concatenate(
        [
            first_half * cosine - second_half * sine_part,
            second_half * cosine + first_half * sine_part,
        ],
        axis=-1,
    )


def project(normed, w_query, w_key, w_value, query_gain, key_gain, positions):
    head_dim = query_gain.shape[0]
    row_count = normed.shape[0]
    query_rows = jnp.dot(normed, w_query, preferred_element_type=jnp.float32).reshape(
        row_count, -1, head_dim
    )
    key_rows = jnp.dot(normed, w_key, preferred_element_type=jnp.float32).reshape(
        row_count, -1, head_dim
    )
    value_rows = jnp.dot(normed, w_value, preferred_element_type=jnp.float32).astype(jnp.bfloat16)
    query_rows = rotate(rms_rows(query_rows, query_gain.astype(jnp.float32)), positions).astype(
        jnp.bfloat16
    )
    key_rows = rotate(rms_rows(key_rows, key_gain.astype(jnp.float32)), positions).astype(
        jnp.bfloat16
    )
    return (query_rows.reshape(row_count, -1), key_rows.reshape(row_count, -1), value_rows)


def attention_kernel(qkv_ref, qpos_ref, kpos_ref, out_ref, *, q_width, k_width, head_dim, blocks):
    rows = qkv_ref.shape[0]
    block = rows // blocks
    kv_heads = k_width // head_dim
    group = q_width // head_dim // kv_heads
    scale = head_dim ** (-0.5)
    for i in range(blocks):
        key_rows = block * (i + 1)
        rows_here = pl.ds(i * block, block)
        allowed = kpos_ref[:, :key_rows] <= qpos_ref[rows_here, :]
        for h in range(kv_heads):
            k_col = q_width + h * head_dim
            v_col = q_width + k_width + h * head_dim
            keys = qkv_ref[:key_rows, k_col : k_col + head_dim]
            values = qkv_ref[:key_rows, v_col : v_col + head_dim]
            for g in range(group):
                q_col = (h * group + g) * head_dim
                queries = qkv_ref[rows_here, q_col : q_col + head_dim]
                scores = lax.dot_general(
                    queries,
                    keys,
                    (((1,), (1,)), ((), ())),
                    preferred_element_type=jnp.float32,
                ) * scale
                scores = jnp.where(allowed, scores, -jnp.inf)
                row_max = jnp.max(scores, axis=-1, keepdims=True)
                weights = jnp.exp(scores - row_max)
                weights = (weights / jnp.sum(weights, axis=-1, keepdims=True)).astype(jnp.bfloat16)
                mixed = jnp.dot(weights, values, preferred_element_type=jnp.float32)
                out_ref[rows_here, q_col : q_col + head_dim] = mixed.astype(out_ref.dtype)


def attend(qkv_slot, query_pos, key_pos, q_width, k_width, head_dim):
    rows = qkv_slot.shape[0]
    blocks = 4
    heads = q_width // head_dim
    causal_pairs = blocks * (blocks + 1) // 2
    pair_flops = 4 * (rows // blocks) ** 2 * head_dim
    vmem = pl.BlockSpec(memory_space=pltpu.VMEM)
    return pl.pallas_call(
        lambda *refs: attention_kernel(
            *refs, q_width=q_width, k_width=k_width, head_dim=head_dim, blocks=blocks
        ),
        out_shape=jax.ShapeDtypeStruct((rows, q_width), jnp.bfloat16),
        in_specs=[vmem, vmem, vmem],
        out_specs=vmem,
        cost_estimate=pl.CostEstimate(
            flops=heads * causal_pairs * pair_flops,
            transcendentals=heads * causal_pairs * (rows // blocks) ** 2,
            bytes_accessed=qkv_slot.size * 2 + rows * q_width * 2,
        ),
    )(qkv_slot, query_pos[:, None], key_pos[None, :])


def on_device(
    hidden, lengths, dealing, norm_gain, w_query, w_key, w_value, query_gain, key_gain, w_out
):
    devices = lax.axis_size("req")
    home_index = lax.axis_index("req")
    slice_index = lax.axis_index("tp")
    tok_rows, features = hidden.shape
    head_dim = query_gain.shape[0]
    out_width = w_out.shape[1]
    q_width = w_query.shape[1]
    k_width = w_key.shape[1]
    slot_len = 4 * tok_rows
    capacity = slot_len // devices
    prompt_total = lengths.shape[0]
    prompt_ids = jnp.arange(prompt_total, dtype=jnp.int32)
    prompt_ends = jnp.cumsum(lengths)
    starts = prompt_ends - lengths
    packed_ids = jnp.arange(tok_rows, dtype=jnp.int32) * devices + home_index
    segment = jnp.sum((packed_ids[:, None] >= prompt_ends[None, :]).astype(jnp.int32), axis=1)
    seg_onehot = (segment[:, None] == prompt_ids[None, :]).astype(jnp.int32)
    positions = packed_ids - jnp.sum(seg_onehot * starts[None, :], axis=1)
    inverse = jnp.zeros((prompt_total,), jnp.int32).at[dealing].set(prompt_ids)
    deal_hot = (dealing[:, None] == prompt_ids[None, :]).astype(jnp.int32)
    dealt_starts = jnp.sum(deal_hot * starts[None, :], axis=1)
    dealt_lengths = jnp.sum(deal_hot * lengths[None, :], axis=1)
    first_offset = jnp.mod(home_index - dealt_starts, devices)
    ranks = jnp.arange(capacity, dtype=jnp.int32)
    slot_offset = first_offset[None, :] + ranks[:, None] * devices
    send_valid = slot_offset < dealt_lengths[None, :]
    send_rows = jnp.where(
        send_valid, (dealt_starts[None, :] + slot_offset - home_index) // devices, 0
    ).reshape(-1)
    my_start = lax.dynamic_index_in_dim(dealt_starts, home_index, 0, keepdims=False)
    my_length = lax.dynamic_index_in_dim(dealt_lengths, home_index, 0, keepdims=False)
    roll_shift = jnp.mod(my_start, devices)
    my_slots = jnp.sum(seg_onehot * inverse[None, :], axis=1)
    back_rows = positions // devices * devices + my_slots
    gain_values = norm_gain.astype(jnp.float32)
    normed = rms_rows(hidden.astype(jnp.float32), gain_values).astype(jnp.bfloat16)
    query_rows, key_rows, value_rows = project(
        normed, w_query, w_key, w_value, query_gain, key_gain, positions
    )
    qkv_rows = jnp.concatenate([query_rows, key_rows, value_rows], axis=1)
    chosen = jnp.where(send_valid, send_rows.reshape(capacity, devices), -1).reshape(-1)
    one_hot = (chosen[:, None] == jnp.arange(tok_rows, dtype=jnp.int32)[None, :]).astype(
        qkv_rows.dtype
    )
    picked = jnp.dot(one_hot, qkv_rows, preferred_element_type=jnp.float32).astype(qkv_rows.dtype)
    arrived = lax.all_to_all(
        picked.reshape(capacity, devices, qkv_rows.shape[1]),
        "req",
        split_axis=1,
        concat_axis=1,
        tiled=True,
    )
    source_ids = jnp.arange(devices, dtype=jnp.int32)
    arrived_pos = (
        ranks[:, None] * devices + jnp.mod(source_ids[None, :] - my_start, devices)
    ).reshape(-1)
    key_pos = jnp.where(arrived_pos < my_length, arrived_pos, 1 << 30)
    mixture = attend(
        arrived.reshape(slot_len, arrived.shape[2]), arrived_pos, key_pos, q_width, k_width, head_dim
    )
    returned = lax.all_to_all(
        mixture.reshape(capacity, devices, mixture.shape[1]),
        "req",
        split_axis=1,
        concat_axis=1,
        tiled=True,
    )
    attended = jnp.take(returned.reshape(capacity * devices, -1), back_rows, axis=0)
    kv_rows = jnp.roll(arrived[:, :, q_width:], -roll_shift, axis=1).reshape(slot_len, -1)
    kv_cache = jnp.stack([kv_rows[:, :k_width], kv_rows[:, k_width:]])[:, None]
    tp_size = lax.axis_size("tp")
    gathered = lax.all_to_all(
        jnp.broadcast_to(attended[None], (tp_size,) + attended.shape),
        "tp",
        split_axis=0,
        concat_axis=0,
        tiled=True,
    )
    summed = jnp.dot(
        gathered.transpose(1, 0, 2).reshape(attended.shape[0], -1),
        w_out,
        preferred_element_type=jnp.float32,
    )
    branch = lax.optimization_barrier(summed.astype(jnp.bfloat16))
    residual = lax.dynamic_slice_in_dim(hidden, slice_index * out_width, out_width, 1)
    hidden_out = (residual.astype(jnp.float32) + branch.astype(jnp.float32)).astype(jnp.bfloat16)
    return (hidden_out, kv_cache)


def solution(mesh):
    in_specs = (
        P("req", None),
        P(),
        P(),
        P(),
        P(None, "tp"),
        P(None, "tp"),
        P(None, "tp"),
        P(),
        P(),
        P(None, "tp"),
    )
    out_specs = (P("req", "tp"), P(None, "req", None, "tp"))
    return jax.shard_map(
        on_device, mesh=mesh, in_specs=in_specs, out_specs=out_specs, check_vma=False
    )
```

```python
import jax
import jax.numpy as jnp
from jax import lax
from jax.experimental import pallas as pl
from jax.experimental.pallas import tpu as pltpu
from jax.sharding import PartitionSpec as P

EPS = 1e-06
THETA = 1000000.0


def rms_rows(values, scale_gain):
    inv_rms = lax.rsqrt(jnp.mean(values * values, axis=-1, keepdims=True) + EPS)
    return values * inv_rms * scale_gain


def rotate(values, positions):
    features = values.shape[-1]
    half_width = features // 2
    frequency = THETA ** (-(jnp.arange(half_width).astype(jnp.float32) * 2.0) / features)
    angles = positions.astype(jnp.float32)[:, None] * frequency[None, :]
    cosine = jnp.cos(angles)[:, None, :]
    sine_part = jnp.sin(angles)[:, None, :]
    first_half = values[..., :half_width]
    second_half = values[..., half_width:]
    return jnp.concatenate(
        [
            first_half * cosine - second_half * sine_part,
            second_half * cosine + first_half * sine_part,
        ],
        axis=-1,
    )


def project(normed, w_query, w_key, w_value, query_gain, key_gain, positions):
    head_dim = query_gain.shape[0]
    row_count = normed.shape[0]
    query_rows = jnp.dot(normed, w_query, preferred_element_type=jnp.float32).reshape(
        row_count, -1, head_dim
    )
    key_rows = jnp.dot(normed, w_key, preferred_element_type=jnp.float32).reshape(
        row_count, -1, head_dim
    )
    value_rows = jnp.dot(normed, w_value, preferred_element_type=jnp.float32).astype(jnp.bfloat16)
    query_rows = rotate(rms_rows(query_rows, query_gain.astype(jnp.float32)), positions).astype(
        jnp.bfloat16
    )
    key_rows = rotate(rms_rows(key_rows, key_gain.astype(jnp.float32)), positions).astype(
        jnp.bfloat16
    )
    return (query_rows.reshape(row_count, -1), key_rows.reshape(row_count, -1), value_rows)


def prep_kernel(
    hidden_ref,
    norm_gain_ref,
    wq_ref,
    wk_ref,
    wv_ref,
    qgain_ref,
    kgain_ref,
    cos_ref,
    sin_ref,
    chosen_ref,
    out_ref,
    qkv_ref,
    *,
    head_dim,
    row_blocks,
):
    values = hidden_ref[...].astype(jnp.float32)
    inv_rms = lax.rsqrt(jnp.mean(values * values, axis=-1, keepdims=True) + EPS)
    normed = (values * inv_rms * norm_gain_ref[...]).astype(jnp.bfloat16)
    cosine = cos_ref[...]
    sine = sin_ref[...]
    column = 0
    for w_ref, gain_ref in ((wq_ref, qgain_ref), (wk_ref, kgain_ref)):
        rows = jnp.dot(normed, w_ref[...], preferred_element_type=jnp.float32)
        gain = gain_ref[...]
        for h in range(rows.shape[1] // head_dim):
            head = rows[:, h * head_dim : (h + 1) * head_dim]
            head_inv = lax.rsqrt(jnp.mean(head * head, axis=-1, keepdims=True) + EPS)
            head = head * head_inv * gain
            swapped = pltpu.roll(head, head_dim // 2, 1)
            qkv_ref[:, column : column + head_dim] = (head * cosine + swapped * sine).astype(
                jnp.bfloat16
            )
            column += head_dim
    v_width = wv_ref.shape[1]
    qkv_ref[:, column : column + v_width] = jnp.dot(
        normed, wv_ref[...], preferred_element_type=jnp.float32
    ).astype(jnp.bfloat16)
    tok_rows = qkv_ref.shape[0]
    out_rows = out_ref.shape[0]
    block = out_rows // row_blocks
    qkv = qkv_ref[...]
    token_ids = lax.broadcasted_iota(jnp.int32, (block, tok_rows), 1)
    for b in range(row_blocks):
        rows_here = pl.ds(b * block, block)
        one_hot = (chosen_ref[rows_here, :] == token_ids).astype(jnp.bfloat16)
        out_ref[rows_here, :] = jnp.dot(
            one_hot, qkv, preferred_element_type=jnp.float32
        ).astype(out_ref.dtype)


def prepare(hidden, norm_gain, w_query, w_key, w_value, query_gain, key_gain, positions, chosen):
    tok_rows, features = hidden.shape
    head_dim = query_gain.shape[0]
    half_width = head_dim // 2
    width = w_query.shape[1] + w_key.shape[1] + w_value.shape[1]
    frequency = THETA ** (-(jnp.arange(half_width).astype(jnp.float32) * 2.0) / head_dim)
    angles = positions.astype(jnp.float32)[:, None] * frequency[None, :]
    cosine = jnp.cos(angles)
    sine = jnp.sin(angles)
    cos_full = jnp.concatenate([cosine, cosine], axis=1)
    sin_signed = jnp.concatenate([-sine, sine], axis=1)
    out_rows = chosen.shape[0]
    vmem = pl.BlockSpec(memory_space=pltpu.VMEM)
    return pl.pallas_call(
        lambda *refs: prep_kernel(*refs, head_dim=head_dim, row_blocks=4),
        out_shape=jax.ShapeDtypeStruct((out_rows, width), jnp.bfloat16),
        in_specs=[vmem] * 10,
        out_specs=vmem,
        scratch_shapes=[pltpu.VMEM((tok_rows, width), jnp.bfloat16)],
        cost_estimate=pl.CostEstimate(
            flops=2 * tok_rows * features * width + 2 * out_rows * tok_rows * width,
            transcendentals=tok_rows * 8,
            bytes_accessed=hidden.size * 2 + features * width * 2 + out_rows * width * 2,
        ),
    )(
        hidden,
        norm_gain.astype(jnp.float32)[None, :],
        w_query,
        w_key,
        w_value,
        query_gain.astype(jnp.float32)[None, :],
        key_gain.astype(jnp.float32)[None, :],
        cos_full,
        sin_signed,
        chosen[:, None],
    )


def attention_kernel(qkv_ref, qpos_ref, kpos_ref, out_ref, *, q_width, k_width, head_dim, blocks):
    rows = qkv_ref.shape[0]
    block = rows // blocks
    kv_heads = k_width // head_dim
    group = q_width // head_dim // kv_heads
    scale = head_dim ** (-0.5)
    for i in range(blocks):
        key_rows = block * (i + 1)
        rows_here = pl.ds(i * block, block)
        allowed = kpos_ref[:, :key_rows] <= qpos_ref[rows_here, :]
        for h in range(kv_heads):
            k_col = q_width + h * head_dim
            v_col = q_width + k_width + h * head_dim
            keys = qkv_ref[:key_rows, k_col : k_col + head_dim]
            values = qkv_ref[:key_rows, v_col : v_col + head_dim]
            for g in range(group):
                q_col = (h * group + g) * head_dim
                queries = qkv_ref[rows_here, q_col : q_col + head_dim]
                scores = lax.dot_general(
                    queries,
                    keys,
                    (((1,), (1,)), ((), ())),
                    preferred_element_type=jnp.float32,
                ) * scale
                scores = jnp.where(allowed, scores, -jnp.inf)
                row_max = jnp.max(scores, axis=-1, keepdims=True)
                weights = jnp.exp(scores - row_max)
                weights = (weights / jnp.sum(weights, axis=-1, keepdims=True)).astype(jnp.bfloat16)
                mixed = jnp.dot(weights, values, preferred_element_type=jnp.float32)
                out_ref[rows_here, q_col : q_col + head_dim] = mixed.astype(out_ref.dtype)


def attend(qkv_slot, query_pos, key_pos, q_width, k_width, head_dim):
    rows = qkv_slot.shape[0]
    blocks = 4
    heads = q_width // head_dim
    causal_pairs = blocks * (blocks + 1) // 2
    pair_flops = 4 * (rows // blocks) ** 2 * head_dim
    vmem = pl.BlockSpec(memory_space=pltpu.VMEM)
    return pl.pallas_call(
        lambda *refs: attention_kernel(
            *refs, q_width=q_width, k_width=k_width, head_dim=head_dim, blocks=blocks
        ),
        out_shape=jax.ShapeDtypeStruct((rows, q_width), jnp.bfloat16),
        in_specs=[vmem, vmem, vmem],
        out_specs=vmem,
        cost_estimate=pl.CostEstimate(
            flops=heads * causal_pairs * pair_flops,
            transcendentals=heads * causal_pairs * (rows // blocks) ** 2,
            bytes_accessed=qkv_slot.size * 2 + rows * q_width * 2,
        ),
    )(qkv_slot, query_pos[:, None], key_pos[None, :])


def on_device(
    hidden, lengths, dealing, norm_gain, w_query, w_key, w_value, query_gain, key_gain, w_out
):
    devices = lax.axis_size("req")
    home_index = lax.axis_index("req")
    slice_index = lax.axis_index("tp")
    tok_rows, features = hidden.shape
    head_dim = query_gain.shape[0]
    out_width = w_out.shape[1]
    q_width = w_query.shape[1]
    k_width = w_key.shape[1]
    slot_len = 4 * tok_rows
    capacity = slot_len // devices
    prompt_total = lengths.shape[0]
    prompt_ids = jnp.arange(prompt_total, dtype=jnp.int32)
    prompt_ends = jnp.cumsum(lengths)
    starts = prompt_ends - lengths
    packed_ids = jnp.arange(tok_rows, dtype=jnp.int32) * devices + home_index
    segment = jnp.sum((packed_ids[:, None] >= prompt_ends[None, :]).astype(jnp.int32), axis=1)
    seg_onehot = (segment[:, None] == prompt_ids[None, :]).astype(jnp.int32)
    positions = packed_ids - jnp.sum(seg_onehot * starts[None, :], axis=1)
    inverse = jnp.zeros((prompt_total,), jnp.int32).at[dealing].set(prompt_ids)
    deal_hot = (dealing[:, None] == prompt_ids[None, :]).astype(jnp.int32)
    dealt_starts = jnp.sum(deal_hot * starts[None, :], axis=1)
    dealt_lengths = jnp.sum(deal_hot * lengths[None, :], axis=1)
    first_offset = jnp.mod(home_index - dealt_starts, devices)
    ranks = jnp.arange(capacity, dtype=jnp.int32)
    slot_offset = first_offset[None, :] + ranks[:, None] * devices
    send_valid = slot_offset < dealt_lengths[None, :]
    send_rows = jnp.where(
        send_valid, (dealt_starts[None, :] + slot_offset - home_index) // devices, 0
    ).reshape(-1)
    my_start = lax.dynamic_index_in_dim(dealt_starts, home_index, 0, keepdims=False)
    my_length = lax.dynamic_index_in_dim(dealt_lengths, home_index, 0, keepdims=False)
    roll_shift = jnp.mod(my_start, devices)
    my_slots = jnp.sum(seg_onehot * inverse[None, :], axis=1)
    back_rows = positions // devices * devices + my_slots
    chosen = jnp.where(send_valid, send_rows.reshape(capacity, devices), -1).T.reshape(-1)
    picked = prepare(
        hidden, norm_gain, w_query, w_key, w_value, query_gain, key_gain, positions, chosen
    )
    arrived = lax.all_to_all(
        picked.reshape(devices, capacity, picked.shape[1]),
        "req",
        split_axis=0,
        concat_axis=0,
        tiled=True,
    ).transpose(1, 0, 2)
    source_ids = jnp.arange(devices, dtype=jnp.int32)
    arrived_pos = (
        ranks[:, None] * devices + jnp.mod(source_ids[None, :] - my_start, devices)
    ).reshape(-1)
    key_pos = jnp.where(arrived_pos < my_length, arrived_pos, 1 << 30)
    mixture = attend(
        arrived.reshape(slot_len, arrived.shape[2]), arrived_pos, key_pos, q_width, k_width, head_dim
    )
    returned = lax.all_to_all(
        mixture.reshape(capacity, devices, mixture.shape[1]),
        "req",
        split_axis=1,
        concat_axis=1,
        tiled=True,
    )
    attended = jnp.take(returned.reshape(capacity * devices, -1), back_rows, axis=0)
    kv_rows = jnp.roll(arrived[:, :, q_width:], -roll_shift, axis=1).reshape(slot_len, -1)
    kv_cache = jnp.stack([kv_rows[:, :k_width], kv_rows[:, k_width:]])[:, None]
    tp_size = lax.axis_size("tp")
    w_rows = w_out.shape[0] // tp_size
    summed = jnp.dot(
        attended,
        lax.dynamic_slice_in_dim(w_out, slice_index * w_rows, w_rows, 0),
        preferred_element_type=jnp.float32,
    )
    for shift in range(1, tp_size):
        passed = lax.ppermute(
            attended, "tp", perm=[(i, (i + shift) % tp_size) for i in range(tp_size)]
        )
        source = jnp.mod(slice_index - shift, tp_size)
        summed = summed + jnp.dot(
            passed,
            lax.dynamic_slice_in_dim(w_out, source * w_rows, w_rows, 0),
            preferred_element_type=jnp.float32,
        )
    branch = lax.optimization_barrier(summed.astype(jnp.bfloat16))
    residual = lax.dynamic_slice_in_dim(hidden, slice_index * out_width, out_width, 1)
    hidden_out = (residual.astype(jnp.float32) + branch.astype(jnp.float32)).astype(jnp.bfloat16)
    return (hidden_out, kv_cache)


def solution(mesh):
    in_specs = (
        P("req", None),
        P(),
        P(),
        P(),
        P(None, "tp"),
        P(None, "tp"),
        P(None, "tp"),
        P(),
        P(),
        P(None, "tp"),
    )
    out_specs = (P("req", "tp"), P(None, "req", None, "tp"))
    return jax.shard_map(
        on_device, mesh=mesh, in_specs=in_specs, out_specs=out_specs, check_vma=False
    )
```

```python
import jax
import jax.numpy as jnp
from jax import lax
from jax.experimental import pallas as pl
from jax.experimental.pallas import tpu as pltpu
from jax.sharding import PartitionSpec as P

EPS = 1e-06
THETA = 1000000.0


def rms_rows(values, scale_gain):
    inv_rms = lax.rsqrt(jnp.mean(values * values, axis=-1, keepdims=True) + EPS)
    return values * inv_rms * scale_gain


def rotate(values, positions):
    features = values.shape[-1]
    half_width = features // 2
    frequency = THETA ** (-(jnp.arange(half_width).astype(jnp.float32) * 2.0) / features)
    angles = positions.astype(jnp.float32)[:, None] * frequency[None, :]
    cosine = jnp.cos(angles)[:, None, :]
    sine_part = jnp.sin(angles)[:, None, :]
    first_half = values[..., :half_width]
    second_half = values[..., half_width:]
    return jnp.concatenate(
        [
            first_half * cosine - second_half * sine_part,
            second_half * cosine + first_half * sine_part,
        ],
        axis=-1,
    )


def project(normed, w_query, w_key, w_value, query_gain, key_gain, positions):
    head_dim = query_gain.shape[0]
    row_count = normed.shape[0]
    query_rows = jnp.dot(normed, w_query, preferred_element_type=jnp.float32).reshape(
        row_count, -1, head_dim
    )
    key_rows = jnp.dot(normed, w_key, preferred_element_type=jnp.float32).reshape(
        row_count, -1, head_dim
    )
    value_rows = jnp.dot(normed, w_value, preferred_element_type=jnp.float32).astype(jnp.bfloat16)
    query_rows = rotate(rms_rows(query_rows, query_gain.astype(jnp.float32)), positions).astype(
        jnp.bfloat16
    )
    key_rows = rotate(rms_rows(key_rows, key_gain.astype(jnp.float32)), positions).astype(
        jnp.bfloat16
    )
    return (query_rows.reshape(row_count, -1), key_rows.reshape(row_count, -1), value_rows)


def prep_kernel(
    hidden_ref,
    norm_gain_ref,
    wq_ref,
    wk_ref,
    wv_ref,
    qgain_ref,
    kgain_ref,
    cos_ref,
    sin_ref,
    chosen_ref,
    out_ref,
    qkv_ref,
    *,
    head_dim,
    row_blocks,
):
    values = hidden_ref[...].astype(jnp.float32)
    inv_rms = lax.rsqrt(jnp.mean(values * values, axis=-1, keepdims=True) + EPS)
    normed = (values * inv_rms * norm_gain_ref[...]).astype(jnp.bfloat16)
    cosine = cos_ref[...]
    sine = sin_ref[...]
    column = 0
    for w_ref, gain_ref in ((wq_ref, qgain_ref), (wk_ref, kgain_ref)):
        rows = jnp.dot(normed, w_ref[...], preferred_element_type=jnp.float32)
        gain = gain_ref[...]
        for h in range(rows.shape[1] // head_dim):
            head = rows[:, h * head_dim : (h + 1) * head_dim]
            head_inv = lax.rsqrt(jnp.mean(head * head, axis=-1, keepdims=True) + EPS)
            head = head * head_inv * gain
            swapped = pltpu.roll(head, head_dim // 2, 1)
            qkv_ref[:, column : column + head_dim] = (head * cosine + swapped * sine).astype(
                jnp.bfloat16
            )
            column += head_dim
    v_width = wv_ref.shape[1]
    qkv_ref[:, column : column + v_width] = jnp.dot(
        normed, wv_ref[...], preferred_element_type=jnp.float32
    ).astype(jnp.bfloat16)
    tok_rows = qkv_ref.shape[0]
    out_rows = out_ref.shape[0]
    block = out_rows // row_blocks
    qkv = qkv_ref[...]
    token_ids = lax.broadcasted_iota(jnp.int32, (block, tok_rows), 1)
    for b in range(row_blocks):
        rows_here = pl.ds(b * block, block)
        one_hot = (chosen_ref[rows_here, :] == token_ids).astype(jnp.bfloat16)
        out_ref[rows_here, :] = jnp.dot(
            one_hot, qkv, preferred_element_type=jnp.float32
        ).astype(out_ref.dtype)


def prepare(hidden, norm_gain, w_query, w_key, w_value, query_gain, key_gain, positions, chosen):
    tok_rows, features = hidden.shape
    head_dim = query_gain.shape[0]
    half_width = head_dim // 2
    width = w_query.shape[1] + w_key.shape[1] + w_value.shape[1]
    frequency = THETA ** (-(jnp.arange(half_width).astype(jnp.float32) * 2.0) / head_dim)
    angles = positions.astype(jnp.float32)[:, None] * frequency[None, :]
    cosine = jnp.cos(angles)
    sine = jnp.sin(angles)
    cos_full = jnp.concatenate([cosine, cosine], axis=1)
    sin_signed = jnp.concatenate([-sine, sine], axis=1)
    out_rows = chosen.shape[0]
    vmem = pl.BlockSpec(memory_space=pltpu.VMEM)
    return pl.pallas_call(
        lambda *refs: prep_kernel(*refs, head_dim=head_dim, row_blocks=4),
        out_shape=jax.ShapeDtypeStruct((out_rows, width), jnp.bfloat16),
        in_specs=[vmem] * 10,
        out_specs=vmem,
        scratch_shapes=[pltpu.VMEM((tok_rows, width), jnp.bfloat16)],
        cost_estimate=pl.CostEstimate(
            flops=2 * tok_rows * features * width + 2 * out_rows * tok_rows * width,
            transcendentals=tok_rows * 8,
            bytes_accessed=hidden.size * 2 + features * width * 2 + out_rows * width * 2,
        ),
    )(
        hidden,
        norm_gain.astype(jnp.float32)[None, :],
        w_query,
        w_key,
        w_value,
        query_gain.astype(jnp.float32)[None, :],
        key_gain.astype(jnp.float32)[None, :],
        cos_full,
        sin_signed,
        chosen[:, None],
    )


def attention_kernel(
    qkv_ref, qpos_ref, kpos_ref, out_ref, *, q_width, k_width, head_dim, blocks, kv_head
):
    rows = qkv_ref.shape[0]
    block = rows // blocks
    kv_heads = k_width // head_dim
    group = q_width // head_dim // kv_heads
    scale = head_dim ** (-0.5)
    k_col = q_width + kv_head * head_dim
    v_col = q_width + k_width + kv_head * head_dim
    for i in range(blocks):
        key_rows = block * (i + 1)
        rows_here = pl.ds(i * block, block)
        allowed = kpos_ref[:, :key_rows] <= qpos_ref[rows_here, :]
        keys = qkv_ref[:key_rows, k_col : k_col + head_dim]
        values = qkv_ref[:key_rows, v_col : v_col + head_dim]
        for g in range(group):
            q_col = (kv_head * group + g) * head_dim
            queries = qkv_ref[rows_here, q_col : q_col + head_dim]
            scores = lax.dot_general(
                queries,
                keys,
                (((1,), (1,)), ((), ())),
                preferred_element_type=jnp.float32,
            ) * scale
            scores = jnp.where(allowed, scores, -jnp.inf)
            row_max = jnp.max(scores, axis=-1, keepdims=True)
            weights = jnp.exp(scores - row_max)
            weights = (weights / jnp.sum(weights, axis=-1, keepdims=True)).astype(jnp.bfloat16)
            mixed = jnp.dot(weights, values, preferred_element_type=jnp.float32)
            out_ref[rows_here, g * head_dim : (g + 1) * head_dim] = mixed.astype(out_ref.dtype)


def attend(qkv_slot, query_pos, key_pos, q_width, k_width, head_dim, kv_head):
    rows = qkv_slot.shape[0]
    blocks = 4
    heads = q_width // k_width
    causal_pairs = blocks * (blocks + 1) // 2
    pair_flops = 4 * (rows // blocks) ** 2 * head_dim
    vmem = pl.BlockSpec(memory_space=pltpu.VMEM)
    return pl.pallas_call(
        lambda *refs: attention_kernel(
            *refs,
            q_width=q_width,
            k_width=k_width,
            head_dim=head_dim,
            blocks=blocks,
            kv_head=kv_head,
        ),
        out_shape=jax.ShapeDtypeStruct((rows, heads * head_dim), jnp.bfloat16),
        in_specs=[vmem, vmem, vmem],
        out_specs=vmem,
        cost_estimate=pl.CostEstimate(
            flops=heads * causal_pairs * pair_flops,
            transcendentals=heads * causal_pairs * (rows // blocks) ** 2,
            bytes_accessed=qkv_slot.size * 2 + rows * heads * head_dim * 2,
        ),
    )(qkv_slot, query_pos[:, None], key_pos[None, :])


def on_device(
    hidden, lengths, dealing, norm_gain, w_query, w_key, w_value, query_gain, key_gain, w_out
):
    devices = lax.axis_size("req")
    home_index = lax.axis_index("req")
    slice_index = lax.axis_index("tp")
    tok_rows, features = hidden.shape
    head_dim = query_gain.shape[0]
    out_width = w_out.shape[1]
    q_width = w_query.shape[1]
    k_width = w_key.shape[1]
    slot_len = 4 * tok_rows
    capacity = slot_len // devices
    prompt_total = lengths.shape[0]
    prompt_ids = jnp.arange(prompt_total, dtype=jnp.int32)
    prompt_ends = jnp.cumsum(lengths)
    starts = prompt_ends - lengths
    packed_ids = jnp.arange(tok_rows, dtype=jnp.int32) * devices + home_index
    segment = jnp.sum((packed_ids[:, None] >= prompt_ends[None, :]).astype(jnp.int32), axis=1)
    seg_onehot = (segment[:, None] == prompt_ids[None, :]).astype(jnp.int32)
    positions = packed_ids - jnp.sum(seg_onehot * starts[None, :], axis=1)
    inverse = jnp.zeros((prompt_total,), jnp.int32).at[dealing].set(prompt_ids)
    deal_hot = (dealing[:, None] == prompt_ids[None, :]).astype(jnp.int32)
    dealt_starts = jnp.sum(deal_hot * starts[None, :], axis=1)
    dealt_lengths = jnp.sum(deal_hot * lengths[None, :], axis=1)
    first_offset = jnp.mod(home_index - dealt_starts, devices)
    ranks = jnp.arange(capacity, dtype=jnp.int32)
    slot_offset = first_offset[None, :] + ranks[:, None] * devices
    send_valid = slot_offset < dealt_lengths[None, :]
    send_rows = jnp.where(
        send_valid, (dealt_starts[None, :] + slot_offset - home_index) // devices, 0
    ).reshape(-1)
    my_start = lax.dynamic_index_in_dim(dealt_starts, home_index, 0, keepdims=False)
    my_length = lax.dynamic_index_in_dim(dealt_lengths, home_index, 0, keepdims=False)
    roll_shift = jnp.mod(my_start, devices)
    my_slots = jnp.sum(seg_onehot * inverse[None, :], axis=1)
    back_rows = positions // devices * devices + my_slots
    chosen = jnp.where(send_valid, send_rows.reshape(capacity, devices), -1).T.reshape(-1)
    picked = prepare(
        hidden, norm_gain, w_query, w_key, w_value, query_gain, key_gain, positions, chosen
    )
    arrived = lax.all_to_all(
        picked.reshape(devices, capacity, picked.shape[1]),
        "req",
        split_axis=0,
        concat_axis=0,
        tiled=True,
    ).transpose(1, 0, 2)
    source_ids = jnp.arange(devices, dtype=jnp.int32)
    arrived_pos = (
        ranks[:, None] * devices + jnp.mod(source_ids[None, :] - my_start, devices)
    ).reshape(-1)
    key_pos = jnp.where(arrived_pos < my_length, arrived_pos, 1 << 30)
    qkv_slot = arrived.reshape(slot_len, arrived.shape[2])
    kv_heads = k_width // head_dim
    tp_size = lax.axis_size("tp")
    w_rows = w_out.shape[0] // tp_size
    part_width = q_width // kv_heads
    mixtures = [
        attend(qkv_slot, arrived_pos, key_pos, q_width, k_width, head_dim, h)
        for h in range(kv_heads)
    ]
    summed = None
    attended = None
    for h in range(kv_heads):
        mixture = mixtures[h]
        if attended is not None:
            attended, mixture = lax.optimization_barrier((attended, mixture))
        returned = lax.all_to_all(
            mixture.reshape(capacity, devices, part_width),
            "req",
            split_axis=1,
            concat_axis=1,
            tiled=True,
        )
        attended = jnp.take(returned.reshape(capacity * devices, -1), back_rows, axis=0)
        for shift in range(tp_size):
            if shift == 0:
                passed = attended
            else:
                passed = lax.ppermute(
                    attended, "tp", perm=[(i, (i + shift) % tp_size) for i in range(tp_size)]
                )
            source = jnp.mod(slice_index - shift, tp_size)
            product = jnp.dot(
                passed,
                lax.dynamic_slice_in_dim(
                    w_out, source * w_rows + h * part_width, part_width, 0
                ),
                preferred_element_type=jnp.float32,
            )
            summed = product if summed is None else summed + product
    kv_rows = jnp.roll(arrived[:, :, q_width:], -roll_shift, axis=1).reshape(slot_len, -1)
    kv_cache = jnp.stack([kv_rows[:, :k_width], kv_rows[:, k_width:]])[:, None]
    branch = lax.optimization_barrier(summed.astype(jnp.bfloat16))
    residual = lax.dynamic_slice_in_dim(hidden, slice_index * out_width, out_width, 1)
    hidden_out = (residual.astype(jnp.float32) + branch.astype(jnp.float32)).astype(jnp.bfloat16)
    return (hidden_out, kv_cache)


def solution(mesh):
    in_specs = (
        P("req", None),
        P(),
        P(),
        P(),
        P(None, "tp"),
        P(None, "tp"),
        P(None, "tp"),
        P(),
        P(),
        P(None, "tp"),
    )
    out_specs = (P("req", "tp"), P(None, "req", None, "tp"))
    return jax.shard_map(
        on_device, mesh=mesh, in_specs=in_specs, out_specs=out_specs, check_vma=False
    )
```

```python
import jax
import jax.numpy as jnp
from jax import lax
from jax.experimental import pallas as pl
from jax.experimental.pallas import tpu as pltpu
from jax.sharding import PartitionSpec as P

EPS = 1e-06
THETA = 1000000.0


def rms_rows(values, scale_gain):
    inv_rms = lax.rsqrt(jnp.mean(values * values, axis=-1, keepdims=True) + EPS)
    return values * inv_rms * scale_gain


def rotate(values, positions):
    features = values.shape[-1]
    half_width = features // 2
    frequency = THETA ** (-(jnp.arange(half_width).astype(jnp.float32) * 2.0) / features)
    angles = positions.astype(jnp.float32)[:, None] * frequency[None, :]
    cosine = jnp.cos(angles)[:, None, :]
    sine_part = jnp.sin(angles)[:, None, :]
    first_half = values[..., :half_width]
    second_half = values[..., half_width:]
    return jnp.concatenate(
        [
            first_half * cosine - second_half * sine_part,
            second_half * cosine + first_half * sine_part,
        ],
        axis=-1,
    )


def project(normed, w_query, w_key, w_value, query_gain, key_gain, positions):
    head_dim = query_gain.shape[0]
    row_count = normed.shape[0]
    query_rows = jnp.dot(normed, w_query, preferred_element_type=jnp.float32).reshape(
        row_count, -1, head_dim
    )
    key_rows = jnp.dot(normed, w_key, preferred_element_type=jnp.float32).reshape(
        row_count, -1, head_dim
    )
    value_rows = jnp.dot(normed, w_value, preferred_element_type=jnp.float32).astype(jnp.bfloat16)
    query_rows = rotate(rms_rows(query_rows, query_gain.astype(jnp.float32)), positions).astype(
        jnp.bfloat16
    )
    key_rows = rotate(rms_rows(key_rows, key_gain.astype(jnp.float32)), positions).astype(
        jnp.bfloat16
    )
    return (query_rows.reshape(row_count, -1), key_rows.reshape(row_count, -1), value_rows)


def prep_kernel(
    lengths_ref,
    dealing_ref,
    home_ref,
    hidden_ref,
    norm_gain_ref,
    wq_ref,
    wk_ref,
    wv_ref,
    qgain_ref,
    kgain_ref,
    cos_ref,
    sin_ref,
    out_ref,
    qkv_ref,
    pick_ref,
    starts_ref,
    *,
    head_dim,
    capacity,
):
    devices = dealing_ref.shape[0]
    prompt_total = lengths_ref.shape[0]
    tok_rows = qkv_ref.shape[0]

    def running(p, total):
        starts_ref[p] = total
        return total + lengths_ref[p]

    lax.fori_loop(0, prompt_total, running, jnp.int32(0))
    home = home_ref[0]
    rank_ids = lax.broadcasted_iota(jnp.int32, (capacity, tok_rows), 0)
    row_gap = lax.broadcasted_iota(jnp.int32, (capacity, tok_rows), 1) - rank_ids

    def pick_rows(d, carry):
        prompt = dealing_ref[d]
        start = starts_ref[prompt]
        length = lengths_ref[prompt]
        first = lax.rem(lax.rem(home - start, devices) + devices, devices)
        first_row = lax.div(start + first - home, devices)
        count = jnp.minimum(lax.div(length - first + devices - 1, devices), capacity)
        hits = (row_gap == first_row) & (rank_ids < count)
        pick_ref[pl.ds(pl.multiple_of(d * capacity, capacity), capacity), :] = hits.astype(
            pick_ref.dtype
        )
        return carry

    lax.fori_loop(0, devices, pick_rows, 0)
    values = hidden_ref[...].astype(jnp.float32)
    inv_rms = lax.rsqrt(jnp.mean(values * values, axis=-1, keepdims=True) + EPS)
    normed = (values * inv_rms * norm_gain_ref[...].astype(jnp.float32)).astype(jnp.bfloat16)
    cosine = cos_ref[...]
    sine = sin_ref[...]
    column = 0
    for w_ref, gain_ref in ((wq_ref, qgain_ref), (wk_ref, kgain_ref)):
        rows = jnp.dot(normed, w_ref[...], preferred_element_type=jnp.float32)
        gain = gain_ref[...].astype(jnp.float32)
        for h in range(rows.shape[1] // head_dim):
            head = rows[:, h * head_dim : (h + 1) * head_dim]
            head_inv = lax.rsqrt(jnp.mean(head * head, axis=-1, keepdims=True) + EPS)
            head = head * head_inv * gain
            swapped = pltpu.roll(head, head_dim // 2, 1)
            qkv_ref[:, column : column + head_dim] = (head * cosine + swapped * sine).astype(
                jnp.bfloat16
            )
            column += head_dim
    v_width = wv_ref.shape[1]
    qkv_ref[:, column : column + v_width] = jnp.dot(
        normed, wv_ref[...], preferred_element_type=jnp.float32
    ).astype(jnp.bfloat16)
    qkv = qkv_ref[...]
    out_rows = out_ref.shape[0]
    block = out_rows // 4
    for b in range(4):
        rows_here = pl.ds(b * block, block)
        out_ref[rows_here, :] = jnp.dot(
            pick_ref[rows_here, :], qkv, preferred_element_type=jnp.float32
        ).astype(out_ref.dtype)


def prepare(
    hidden, lengths, dealing, home, norm_gain, w_query, w_key, w_value, query_gain, key_gain,
    positions, capacity,
):
    tok_rows, features = hidden.shape
    head_dim = query_gain.shape[0]
    half_width = head_dim // 2
    width = w_query.shape[1] + w_key.shape[1] + w_value.shape[1]
    devices = dealing.shape[0]
    out_rows = devices * capacity
    frequency = THETA ** (-(jnp.arange(half_width).astype(jnp.float32) * 2.0) / head_dim)
    frequency = jnp.concatenate([frequency, frequency])
    angles = positions.astype(jnp.float32)[:, None] * frequency[None, :]
    sign = jnp.where(jnp.arange(head_dim) < half_width, -1.0, 1.0).astype(jnp.float32)
    cos_full = jnp.cos(angles)
    sin_signed = jnp.sin(angles) * sign[None, :]
    vmem = pl.BlockSpec(memory_space=pltpu.VMEM)
    smem = pl.BlockSpec(memory_space=pltpu.SMEM)
    return pl.pallas_call(
        lambda *refs: prep_kernel(*refs, head_dim=head_dim, capacity=capacity),
        out_shape=jax.ShapeDtypeStruct((out_rows, width), jnp.bfloat16),
        in_specs=[smem] * 3 + [vmem] * 9,
        out_specs=vmem,
        scratch_shapes=[
            pltpu.VMEM((tok_rows, width), jnp.bfloat16),
            pltpu.VMEM((out_rows, tok_rows), jnp.bfloat16),
            pltpu.SMEM((lengths.shape[0],), jnp.int32),
        ],
        cost_estimate=pl.CostEstimate(
            flops=2 * tok_rows * features * width + 2 * out_rows * tok_rows * width,
            transcendentals=tok_rows * 8,
            bytes_accessed=hidden.size * 2 + features * width * 2 + out_rows * width * 2,
        ),
    )(
        lengths,
        dealing,
        home,
        hidden,
        norm_gain[None, :],
        w_query,
        w_key,
        w_value,
        query_gain[None, :],
        key_gain[None, :],
        cos_full,
        sin_signed,
    )


def attention_kernel(qkv_ref, qpos_ref, kpos_ref, out_ref, *, q_width, k_width, head_dim, blocks):
    rows = qkv_ref.shape[0]
    block = rows // blocks
    kv_heads = k_width // head_dim
    group = q_width // head_dim // kv_heads
    scale = head_dim ** (-0.5)
    for i in range(blocks):
        key_rows = block * (i + 1)
        rows_here = pl.ds(i * block, block)
        allowed = kpos_ref[:, :key_rows] <= qpos_ref[rows_here, :]
        for h in range(kv_heads):
            k_col = q_width + h * head_dim
            v_col = q_width + k_width + h * head_dim
            keys = qkv_ref[:key_rows, k_col : k_col + head_dim]
            values = qkv_ref[:key_rows, v_col : v_col + head_dim]
            for g in range(group):
                q_col = (h * group + g) * head_dim
                queries = qkv_ref[rows_here, q_col : q_col + head_dim]
                scores = lax.dot_general(
                    queries,
                    keys,
                    (((1,), (1,)), ((), ())),
                    preferred_element_type=jnp.float32,
                ) * scale
                scores = jnp.where(allowed, scores, -jnp.inf)
                row_max = jnp.max(scores, axis=-1, keepdims=True)
                weights = jnp.exp(scores - row_max)
                weights = (weights / jnp.sum(weights, axis=-1, keepdims=True)).astype(jnp.bfloat16)
                mixed = jnp.dot(weights, values, preferred_element_type=jnp.float32)
                out_ref[rows_here, q_col : q_col + head_dim] = mixed.astype(out_ref.dtype)


def attend(qkv_slot, query_pos, key_pos, q_width, k_width, head_dim):
    rows = qkv_slot.shape[0]
    blocks = 4
    heads = q_width // head_dim
    causal_pairs = blocks * (blocks + 1) // 2
    pair_flops = 4 * (rows // blocks) ** 2 * head_dim
    vmem = pl.BlockSpec(memory_space=pltpu.VMEM)
    return pl.pallas_call(
        lambda *refs: attention_kernel(
            *refs, q_width=q_width, k_width=k_width, head_dim=head_dim, blocks=blocks
        ),
        out_shape=jax.ShapeDtypeStruct((rows, q_width), jnp.bfloat16),
        in_specs=[vmem, vmem, vmem],
        out_specs=vmem,
        cost_estimate=pl.CostEstimate(
            flops=heads * causal_pairs * pair_flops,
            transcendentals=heads * causal_pairs * (rows // blocks) ** 2,
            bytes_accessed=qkv_slot.size * 2 + rows * q_width * 2,
        ),
    )(qkv_slot, query_pos[:, None], key_pos[None, :])


def on_device(
    hidden, lengths, dealing, norm_gain, w_query, w_key, w_value, query_gain, key_gain, w_out
):
    devices = lax.axis_size("req")
    home_index = lax.axis_index("req")
    slice_index = lax.axis_index("tp")
    tok_rows, features = hidden.shape
    head_dim = query_gain.shape[0]
    out_width = w_out.shape[1]
    q_width = w_query.shape[1]
    k_width = w_key.shape[1]
    slot_len = 4 * tok_rows
    capacity = slot_len // devices
    prompt_total = lengths.shape[0]
    prompt_ids = jnp.arange(prompt_total, dtype=jnp.int32)
    prompt_ends = jnp.cumsum(lengths)
    starts = prompt_ends - lengths
    packed_ids = jnp.arange(tok_rows, dtype=jnp.int32) * devices + home_index
    segment = jnp.sum((packed_ids[:, None] >= prompt_ends[None, :]).astype(jnp.int32), axis=1)
    seg_onehot = (segment[:, None] == prompt_ids[None, :]).astype(jnp.int32)
    positions = packed_ids - jnp.sum(seg_onehot * starts[None, :], axis=1)
    inverse = jnp.zeros((prompt_total,), jnp.int32).at[dealing].set(prompt_ids)
    deal_hot = (dealing[:, None] == prompt_ids[None, :]).astype(jnp.int32)
    dealt_starts = jnp.sum(deal_hot * starts[None, :], axis=1)
    dealt_lengths = jnp.sum(deal_hot * lengths[None, :], axis=1)
    ranks = jnp.arange(capacity, dtype=jnp.int32)
    my_start = lax.dynamic_index_in_dim(dealt_starts, home_index, 0, keepdims=False)
    my_length = lax.dynamic_index_in_dim(dealt_lengths, home_index, 0, keepdims=False)
    roll_shift = jnp.mod(my_start, devices)
    my_slots = jnp.sum(seg_onehot * inverse[None, :], axis=1)
    back_rows = positions // devices * devices + my_slots
    picked = prepare(
        hidden,
        lengths,
        dealing,
        jnp.reshape(home_index, (1,)).astype(jnp.int32),
        norm_gain,
        w_query,
        w_key,
        w_value,
        query_gain,
        key_gain,
        positions,
        capacity,
    )
    arrived = lax.all_to_all(
        picked.reshape(devices, capacity, picked.shape[1]),
        "req",
        split_axis=0,
        concat_axis=0,
        tiled=True,
    ).transpose(1, 0, 2)
    source_ids = jnp.arange(devices, dtype=jnp.int32)
    arrived_pos = (
        ranks[:, None] * devices + jnp.mod(source_ids[None, :] - my_start, devices)
    ).reshape(-1)
    key_pos = jnp.where(arrived_pos < my_length, arrived_pos, 1 << 30)
    mixture = attend(
        arrived.reshape(slot_len, arrived.shape[2]), arrived_pos, key_pos, q_width, k_width, head_dim
    )
    returned = lax.all_to_all(
        mixture.reshape(capacity, devices, mixture.shape[1]),
        "req",
        split_axis=1,
        concat_axis=1,
        tiled=True,
    )
    attended = jnp.take(returned.reshape(capacity * devices, -1), back_rows, axis=0)
    kv_rows = jnp.roll(arrived[:, :, q_width:], -roll_shift, axis=1).reshape(slot_len, -1)
    kv_cache = jnp.stack([kv_rows[:, :k_width], kv_rows[:, k_width:]])[:, None]
    tp_size = lax.axis_size("tp")
    w_rows = w_out.shape[0] // tp_size
    summed = jnp.dot(
        attended,
        lax.dynamic_slice_in_dim(w_out, slice_index * w_rows, w_rows, 0),
        preferred_element_type=jnp.float32,
    )
    for shift in range(1, tp_size):
        passed = lax.ppermute(
            attended, "tp", perm=[(i, (i + shift) % tp_size) for i in range(tp_size)]
        )
        source = jnp.mod(slice_index - shift, tp_size)
        summed = summed + jnp.dot(
            passed,
            lax.dynamic_slice_in_dim(w_out, source * w_rows, w_rows, 0),
            preferred_element_type=jnp.float32,
        )
    branch = lax.optimization_barrier(summed.astype(jnp.bfloat16))
    residual = lax.dynamic_slice_in_dim(hidden, slice_index * out_width, out_width, 1)
    hidden_out = (residual.astype(jnp.float32) + branch.astype(jnp.float32)).astype(jnp.bfloat16)
    return (hidden_out, kv_cache)


def solution(mesh):
    in_specs = (
        P("req", None),
        P(),
        P(),
        P(),
        P(None, "tp"),
        P(None, "tp"),
        P(None, "tp"),
        P(),
        P(),
        P(None, "tp"),
    )
    out_specs = (P("req", "tp"), P(None, "req", None, "tp"))
    return jax.shard_map(
        on_device, mesh=mesh, in_specs=in_specs, out_specs=out_specs, check_vma=False
    )
```

```python
import jax
import jax.numpy as jnp
from jax import lax
from jax.experimental import pallas as pl
from jax.experimental.pallas import tpu as pltpu
from jax.sharding import PartitionSpec as P

EPS = 1e-06
THETA = 1000000.0


def rms_rows(values, scale_gain):
    inv_rms = lax.rsqrt(jnp.mean(values * values, axis=-1, keepdims=True) + EPS)
    return values * inv_rms * scale_gain


def rotate(values, positions):
    features = values.shape[-1]
    half_width = features // 2
    frequency = THETA ** (-(jnp.arange(half_width).astype(jnp.float32) * 2.0) / features)
    angles = positions.astype(jnp.float32)[:, None] * frequency[None, :]
    cosine = jnp.cos(angles)[:, None, :]
    sine_part = jnp.sin(angles)[:, None, :]
    first_half = values[..., :half_width]
    second_half = values[..., half_width:]
    return jnp.concatenate(
        [
            first_half * cosine - second_half * sine_part,
            second_half * cosine + first_half * sine_part,
        ],
        axis=-1,
    )


def project(normed, w_query, w_key, w_value, query_gain, key_gain, positions):
    head_dim = query_gain.shape[0]
    row_count = normed.shape[0]
    query_rows = jnp.dot(normed, w_query, preferred_element_type=jnp.float32).reshape(
        row_count, -1, head_dim
    )
    key_rows = jnp.dot(normed, w_key, preferred_element_type=jnp.float32).reshape(
        row_count, -1, head_dim
    )
    value_rows = jnp.dot(normed, w_value, preferred_element_type=jnp.float32).astype(jnp.bfloat16)
    query_rows = rotate(rms_rows(query_rows, query_gain.astype(jnp.float32)), positions).astype(
        jnp.bfloat16
    )
    key_rows = rotate(rms_rows(key_rows, key_gain.astype(jnp.float32)), positions).astype(
        jnp.bfloat16
    )
    return (query_rows.reshape(row_count, -1), key_rows.reshape(row_count, -1), value_rows)


def prep_kernel(
    lengths_ref,
    dealing_ref,
    home_ref,
    hidden_ref,
    norm_gain_ref,
    wq_ref,
    wk_ref,
    wv_ref,
    qgain_ref,
    kgain_ref,
    cos_ref,
    sin_ref,
    *refs,
    head_dim,
    capacity,
):
    qkv_ref, pick_ref, starts_ref = refs[-3:]
    out_refs = refs[:-3]
    devices = dealing_ref.shape[0]
    prompt_total = lengths_ref.shape[0]
    tok_rows = qkv_ref.shape[0]

    def running(p, total):
        starts_ref[p] = total
        return total + lengths_ref[p]

    lax.fori_loop(0, prompt_total, running, jnp.int32(0))
    home = home_ref[0]
    rank_ids = lax.broadcasted_iota(jnp.int32, (capacity, tok_rows), 0)
    row_gap = lax.broadcasted_iota(jnp.int32, (capacity, tok_rows), 1) - rank_ids

    def pick_rows(d, carry):
        prompt = dealing_ref[d]
        start = starts_ref[prompt]
        length = lengths_ref[prompt]
        first = lax.rem(lax.rem(home - start, devices) + devices, devices)
        first_row = lax.div(start + first - home, devices)
        count = jnp.minimum(lax.div(length - first + devices - 1, devices), capacity)
        hits = (row_gap == first_row) & (rank_ids < count)
        pick_ref[pl.ds(pl.multiple_of(d * capacity, capacity), capacity), :] = hits.astype(
            pick_ref.dtype
        )
        return carry

    lax.fori_loop(0, devices, pick_rows, 0)
    values = hidden_ref[...].astype(jnp.float32)
    inv_rms = lax.rsqrt(jnp.mean(values * values, axis=-1, keepdims=True) + EPS)
    normed = (values * inv_rms * norm_gain_ref[...].astype(jnp.float32)).astype(jnp.bfloat16)
    cosine = cos_ref[...]
    sine = sin_ref[...]
    column = 0
    for w_ref, gain_ref in ((wq_ref, qgain_ref), (wk_ref, kgain_ref)):
        rows = jnp.dot(normed, w_ref[...], preferred_element_type=jnp.float32)
        gain = gain_ref[...].astype(jnp.float32)
        for h in range(rows.shape[1] // head_dim):
            head = rows[:, h * head_dim : (h + 1) * head_dim]
            head_inv = lax.rsqrt(jnp.mean(head * head, axis=-1, keepdims=True) + EPS)
            head = head * head_inv * gain
            swapped = pltpu.roll(head, head_dim // 2, 1)
            qkv_ref[:, column : column + head_dim] = (head * cosine + swapped * sine).astype(
                jnp.bfloat16
            )
            column += head_dim
    v_width = wv_ref.shape[1]
    qkv_ref[:, column : column + v_width] = jnp.dot(
        normed, wv_ref[...], preferred_element_type=jnp.float32
    ).astype(jnp.bfloat16)
    q_width = wq_ref.shape[1]
    k_width = wk_ref.shape[1]
    kv_heads = k_width // head_dim
    q_part = q_width // kv_heads
    out_rows = out_refs[0].shape[0]
    block = out_rows // 4
    for h, out_ref in enumerate(out_refs):
        part = jnp.concatenate(
            [
                qkv_ref[:, h * q_part : (h + 1) * q_part],
                qkv_ref[:, q_width + h * head_dim : q_width + (h + 1) * head_dim],
                qkv_ref[
                    :, q_width + k_width + h * head_dim : q_width + k_width + (h + 1) * head_dim
                ],
            ],
            axis=1,
        )
        for b in range(4):
            rows_here = pl.ds(b * block, block)
            out_ref[rows_here, :] = jnp.dot(
                pick_ref[rows_here, :], part, preferred_element_type=jnp.float32
            ).astype(out_ref.dtype)


def prepare(
    hidden, lengths, dealing, home, norm_gain, w_query, w_key, w_value, query_gain, key_gain,
    positions, capacity,
):
    tok_rows, features = hidden.shape
    head_dim = query_gain.shape[0]
    half_width = head_dim // 2
    width = w_query.shape[1] + w_key.shape[1] + w_value.shape[1]
    devices = dealing.shape[0]
    out_rows = devices * capacity
    kv_heads = w_key.shape[1] // head_dim
    frequency = THETA ** (-(jnp.arange(half_width).astype(jnp.float32) * 2.0) / head_dim)
    frequency = jnp.concatenate([frequency, frequency])
    angles = positions.astype(jnp.float32)[:, None] * frequency[None, :]
    sign = jnp.where(jnp.arange(head_dim) < half_width, -1.0, 1.0).astype(jnp.float32)
    cos_full = jnp.cos(angles)
    sin_signed = jnp.sin(angles) * sign[None, :]
    vmem = pl.BlockSpec(memory_space=pltpu.VMEM)
    smem = pl.BlockSpec(memory_space=pltpu.SMEM)
    return pl.pallas_call(
        lambda *refs: prep_kernel(*refs, head_dim=head_dim, capacity=capacity),
        out_shape=[jax.ShapeDtypeStruct((out_rows, width // kv_heads), jnp.bfloat16)] * kv_heads,
        in_specs=[smem] * 3 + [vmem] * 9,
        out_specs=[vmem] * kv_heads,
        scratch_shapes=[
            pltpu.VMEM((tok_rows, width), jnp.bfloat16),
            pltpu.VMEM((out_rows, tok_rows), jnp.bfloat16),
            pltpu.SMEM((lengths.shape[0],), jnp.int32),
        ],
        cost_estimate=pl.CostEstimate(
            flops=2 * tok_rows * features * width + 2 * out_rows * tok_rows * width,
            transcendentals=tok_rows * 8,
            bytes_accessed=hidden.size * 2 + features * width * 2 + out_rows * width * 2,
        ),
    )(
        lengths,
        dealing,
        home,
        hidden,
        norm_gain[None, :],
        w_query,
        w_key,
        w_value,
        query_gain[None, :],
        key_gain[None, :],
        cos_full,
        sin_signed,
    )


def attention_kernel(qkv_ref, qpos_ref, kpos_ref, out_ref, *, q_width, k_width, head_dim, blocks):
    rows = qkv_ref.shape[0]
    block = rows // blocks
    kv_heads = k_width // head_dim
    group = q_width // head_dim // kv_heads
    scale = head_dim ** (-0.5)
    for i in range(blocks):
        key_rows = block * (i + 1)
        rows_here = pl.ds(i * block, block)
        allowed = kpos_ref[:, :key_rows] <= qpos_ref[rows_here, :]
        for h in range(kv_heads):
            k_col = q_width + h * head_dim
            v_col = q_width + k_width + h * head_dim
            keys = qkv_ref[:key_rows, k_col : k_col + head_dim]
            values = qkv_ref[:key_rows, v_col : v_col + head_dim]
            for g in range(group):
                q_col = (h * group + g) * head_dim
                queries = qkv_ref[rows_here, q_col : q_col + head_dim]
                scores = lax.dot_general(
                    queries,
                    keys,
                    (((1,), (1,)), ((), ())),
                    preferred_element_type=jnp.float32,
                ) * scale
                scores = jnp.where(allowed, scores, -jnp.inf)
                row_max = jnp.max(scores, axis=-1, keepdims=True)
                weights = jnp.exp(scores - row_max)
                weights = (weights / jnp.sum(weights, axis=-1, keepdims=True)).astype(jnp.bfloat16)
                mixed = jnp.dot(weights, values, preferred_element_type=jnp.float32)
                out_ref[rows_here, q_col : q_col + head_dim] = mixed.astype(out_ref.dtype)


def attend(qkv_slot, query_pos, key_pos, q_width, k_width, head_dim):
    rows = qkv_slot.shape[0]
    blocks = 4
    heads = q_width // head_dim
    causal_pairs = blocks * (blocks + 1) // 2
    pair_flops = 4 * (rows // blocks) ** 2 * head_dim
    vmem = pl.BlockSpec(memory_space=pltpu.VMEM)
    return pl.pallas_call(
        lambda *refs: attention_kernel(
            *refs, q_width=q_width, k_width=k_width, head_dim=head_dim, blocks=blocks
        ),
        out_shape=jax.ShapeDtypeStruct((rows, q_width), jnp.bfloat16),
        in_specs=[vmem, vmem, vmem],
        out_specs=vmem,
        cost_estimate=pl.CostEstimate(
            flops=heads * causal_pairs * pair_flops,
            transcendentals=heads * causal_pairs * (rows // blocks) ** 2,
            bytes_accessed=qkv_slot.size * 2 + rows * q_width * 2,
        ),
    )(qkv_slot, query_pos[:, None], key_pos[None, :])


def on_device(
    hidden, lengths, dealing, norm_gain, w_query, w_key, w_value, query_gain, key_gain, w_out
):
    devices = lax.axis_size("req")
    home_index = lax.axis_index("req")
    slice_index = lax.axis_index("tp")
    tok_rows, features = hidden.shape
    head_dim = query_gain.shape[0]
    out_width = w_out.shape[1]
    q_width = w_query.shape[1]
    k_width = w_key.shape[1]
    slot_len = 4 * tok_rows
    capacity = slot_len // devices
    prompt_total = lengths.shape[0]
    prompt_ids = jnp.arange(prompt_total, dtype=jnp.int32)
    prompt_ends = jnp.cumsum(lengths)
    starts = prompt_ends - lengths
    packed_ids = jnp.arange(tok_rows, dtype=jnp.int32) * devices + home_index
    segment = jnp.sum((packed_ids[:, None] >= prompt_ends[None, :]).astype(jnp.int32), axis=1)
    seg_onehot = (segment[:, None] == prompt_ids[None, :]).astype(jnp.int32)
    positions = packed_ids - jnp.sum(seg_onehot * starts[None, :], axis=1)
    inverse = jnp.zeros((prompt_total,), jnp.int32).at[dealing].set(prompt_ids)
    deal_hot = (dealing[:, None] == prompt_ids[None, :]).astype(jnp.int32)
    dealt_starts = jnp.sum(deal_hot * starts[None, :], axis=1)
    dealt_lengths = jnp.sum(deal_hot * lengths[None, :], axis=1)
    ranks = jnp.arange(capacity, dtype=jnp.int32)
    my_start = lax.dynamic_index_in_dim(dealt_starts, home_index, 0, keepdims=False)
    my_length = lax.dynamic_index_in_dim(dealt_lengths, home_index, 0, keepdims=False)
    roll_shift = jnp.mod(my_start, devices)
    my_slots = jnp.sum(seg_onehot * inverse[None, :], axis=1)
    back_rows = positions // devices * devices + my_slots
    parts = prepare(
        hidden,
        lengths,
        dealing,
        jnp.reshape(home_index, (1,)).astype(jnp.int32),
        norm_gain,
        w_query,
        w_key,
        w_value,
        query_gain,
        key_gain,
        positions,
        capacity,
    )
    source_ids = jnp.arange(devices, dtype=jnp.int32)
    arrived_pos = (
        ranks[:, None] * devices + jnp.mod(source_ids[None, :] - my_start, devices)
    ).reshape(-1)
    key_pos = jnp.where(arrived_pos < my_length, arrived_pos, 1 << 30)
    kv_heads = k_width // head_dim
    q_part = q_width // kv_heads
    tp_size = lax.axis_size("tp")
    w_rows = w_out.shape[0] // tp_size
    summed = None
    passes = []
    key_parts = []
    value_parts = []
    for h in range(kv_heads):
        arrived = lax.all_to_all(
            parts[h].reshape(devices, capacity, parts[h].shape[1]),
            "req",
            split_axis=0,
            concat_axis=0,
            tiled=True,
        ).transpose(1, 0, 2)
        mixture = attend(
            arrived.reshape(slot_len, arrived.shape[2]),
            arrived_pos,
            key_pos,
            q_part,
            head_dim,
            head_dim,
        )
        kv_rows = jnp.roll(arrived[:, :, q_part:], -roll_shift, axis=1).reshape(slot_len, -1)
        key_parts.append(kv_rows[:, :head_dim])
        value_parts.append(kv_rows[:, head_dim:])
        if h > 0:
            attended, mixture = lax.optimization_barrier((attended, mixture))
            passes.append(attended)
        returned = lax.all_to_all(
            mixture.reshape(capacity, devices, q_part),
            "req",
            split_axis=1,
            concat_axis=1,
            tiled=True,
        )
        attended = jnp.take(returned.reshape(capacity * devices, -1), back_rows, axis=0)
    passes.append(attended)
    for h, attended in enumerate(passes):
        for shift in range(tp_size):
            if shift == 0:
                passed = attended
            else:
                passed = lax.ppermute(
                    attended, "tp", perm=[(i, (i + shift) % tp_size) for i in range(tp_size)]
                )
            source = jnp.mod(slice_index - shift, tp_size)
            product = jnp.dot(
                passed,
                lax.dynamic_slice_in_dim(w_out, source * w_rows + h * q_part, q_part, 0),
                preferred_element_type=jnp.float32,
            )
            summed = product if summed is None else summed + product
    kv_cache = jnp.stack(
        [jnp.concatenate(key_parts, axis=1), jnp.concatenate(value_parts, axis=1)]
    )[:, None]
    branch = lax.optimization_barrier(summed.astype(jnp.bfloat16))
    residual = lax.dynamic_slice_in_dim(hidden, slice_index * out_width, out_width, 1)
    hidden_out = (residual.astype(jnp.float32) + branch.astype(jnp.float32)).astype(jnp.bfloat16)
    return (hidden_out, kv_cache)


def solution(mesh):
    in_specs = (
        P("req", None),
        P(),
        P(),
        P(),
        P(None, "tp"),
        P(None, "tp"),
        P(None, "tp"),
        P(),
        P(),
        P(None, "tp"),
    )
    out_specs = (P("req", "tp"), P(None, "req", None, "tp"))
    return jax.shard_map(
        on_device, mesh=mesh, in_specs=in_specs, out_specs=out_specs, check_vma=False
    )
```

```python
import jax
import jax.numpy as jnp
from jax import lax
from jax.experimental import pallas as pl
from jax.experimental.pallas import tpu as pltpu
from jax.sharding import PartitionSpec as P

EPS = 1e-06
THETA = 1000000.0


def rms_rows(values, scale_gain):
    inv_rms = lax.rsqrt(jnp.mean(values * values, axis=-1, keepdims=True) + EPS)
    return values * inv_rms * scale_gain


def rotate(values, positions):
    features = values.shape[-1]
    half_width = features // 2
    frequency = THETA ** (-(jnp.arange(half_width).astype(jnp.float32) * 2.0) / features)
    angles = positions.astype(jnp.float32)[:, None] * frequency[None, :]
    cosine = jnp.cos(angles)[:, None, :]
    sine_part = jnp.sin(angles)[:, None, :]
    first_half = values[..., :half_width]
    second_half = values[..., half_width:]
    return jnp.concatenate(
        [
            first_half * cosine - second_half * sine_part,
            second_half * cosine + first_half * sine_part,
        ],
        axis=-1,
    )


def project(normed, w_query, w_key, w_value, query_gain, key_gain, positions):
    head_dim = query_gain.shape[0]
    row_count = normed.shape[0]
    query_rows = jnp.dot(normed, w_query, preferred_element_type=jnp.float32).reshape(
        row_count, -1, head_dim
    )
    key_rows = jnp.dot(normed, w_key, preferred_element_type=jnp.float32).reshape(
        row_count, -1, head_dim
    )
    value_rows = jnp.dot(normed, w_value, preferred_element_type=jnp.float32).astype(jnp.bfloat16)
    query_rows = rotate(rms_rows(query_rows, query_gain.astype(jnp.float32)), positions).astype(
        jnp.bfloat16
    )
    key_rows = rotate(rms_rows(key_rows, key_gain.astype(jnp.float32)), positions).astype(
        jnp.bfloat16
    )
    return (query_rows.reshape(row_count, -1), key_rows.reshape(row_count, -1), value_rows)


def prep_kernel(
    lengths_ref,
    dealing_ref,
    home_ref,
    hidden_ref,
    norm_gain_ref,
    wq_ref,
    wk_ref,
    wv_ref,
    qgain_ref,
    kgain_ref,
    cos_ref,
    sin_ref,
    out_ref,
    qkv_ref,
    pick_ref,
    starts_ref,
    *,
    head_dim,
    capacity,
):
    devices = dealing_ref.shape[0]
    prompt_total = lengths_ref.shape[0]
    tok_rows = qkv_ref.shape[0]

    def running(p, total):
        starts_ref[p] = total
        return total + lengths_ref[p]

    lax.fori_loop(0, prompt_total, running, jnp.int32(0))
    home = home_ref[0]
    rank_ids = lax.broadcasted_iota(jnp.int32, (capacity, tok_rows), 0)
    row_gap = lax.broadcasted_iota(jnp.int32, (capacity, tok_rows), 1) - rank_ids

    def pick_rows(d, carry):
        prompt = dealing_ref[d]
        start = starts_ref[prompt]
        length = lengths_ref[prompt]
        first = lax.rem(lax.rem(home - start, devices) + devices, devices)
        first_row = lax.div(start + first - home, devices)
        count = jnp.minimum(lax.div(length - first + devices - 1, devices), capacity)
        hits = (row_gap == first_row) & (rank_ids < count)
        pick_ref[pl.ds(pl.multiple_of(d * capacity, capacity), capacity), :] = hits.astype(
            pick_ref.dtype
        )
        return carry

    lax.fori_loop(0, devices, pick_rows, 0)
    values = hidden_ref[...].astype(jnp.float32)
    inv_rms = lax.rsqrt(jnp.mean(values * values, axis=-1, keepdims=True) + EPS)
    normed = (values * inv_rms * norm_gain_ref[...].astype(jnp.float32)).astype(jnp.bfloat16)
    cosine = cos_ref[...]
    sine = sin_ref[...]
    column = 0
    for w_ref, gain_ref in ((wq_ref, qgain_ref), (wk_ref, kgain_ref)):
        rows = jnp.dot(normed, w_ref[...], preferred_element_type=jnp.float32)
        gain = gain_ref[...].astype(jnp.float32)
        for h in range(rows.shape[1] // head_dim):
            head = rows[:, h * head_dim : (h + 1) * head_dim]
            head_inv = lax.rsqrt(jnp.mean(head * head, axis=-1, keepdims=True) + EPS)
            head = head * head_inv * gain
            swapped = pltpu.roll(head, head_dim // 2, 1)
            qkv_ref[:, column : column + head_dim] = (head * cosine + swapped * sine).astype(
                jnp.bfloat16
            )
            column += head_dim
    v_width = wv_ref.shape[1]
    qkv_ref[:, column : column + v_width] = jnp.dot(
        normed, wv_ref[...], preferred_element_type=jnp.float32
    ).astype(jnp.bfloat16)
    qkv = qkv_ref[...]
    out_rows = out_ref.shape[0]
    block = out_rows // 4
    for b in range(4):
        rows_here = pl.ds(b * block, block)
        out_ref[rows_here, :] = jnp.dot(
            pick_ref[rows_here, :], qkv, preferred_element_type=jnp.float32
        ).astype(out_ref.dtype)


def prepare(
    hidden, lengths, dealing, home, norm_gain, w_query, w_key, w_value, query_gain, key_gain,
    positions, capacity,
):
    tok_rows, features = hidden.shape
    head_dim = query_gain.shape[0]
    half_width = head_dim // 2
    width = w_query.shape[1] + w_key.shape[1] + w_value.shape[1]
    devices = dealing.shape[0]
    out_rows = devices * capacity
    frequency = THETA ** (-(jnp.arange(half_width).astype(jnp.float32) * 2.0) / head_dim)
    frequency = jnp.concatenate([frequency, frequency])
    angles = positions.astype(jnp.float32)[:, None] * frequency[None, :]
    sign = jnp.where(jnp.arange(head_dim) < half_width, -1.0, 1.0).astype(jnp.float32)
    cos_full = jnp.cos(angles)
    sin_signed = jnp.sin(angles) * sign[None, :]
    vmem = pl.BlockSpec(memory_space=pltpu.VMEM)
    smem = pl.BlockSpec(memory_space=pltpu.SMEM)
    return pl.pallas_call(
        lambda *refs: prep_kernel(*refs, head_dim=head_dim, capacity=capacity),
        out_shape=jax.ShapeDtypeStruct((out_rows, width), jnp.bfloat16),
        in_specs=[smem] * 3 + [vmem] * 9,
        out_specs=vmem,
        scratch_shapes=[
            pltpu.VMEM((tok_rows, width), jnp.bfloat16),
            pltpu.VMEM((out_rows, tok_rows), jnp.bfloat16),
            pltpu.SMEM((lengths.shape[0],), jnp.int32),
        ],
        cost_estimate=pl.CostEstimate(
            flops=2 * tok_rows * features * width + 2 * out_rows * tok_rows * width,
            transcendentals=tok_rows * 8,
            bytes_accessed=hidden.size * 2 + features * width * 2 + out_rows * width * 2,
        ),
    )(
        lengths,
        dealing,
        home,
        hidden,
        norm_gain[None, :],
        w_query,
        w_key,
        w_value,
        query_gain[None, :],
        key_gain[None, :],
        cos_full,
        sin_signed,
    )


def attention_kernel(qkv_ref, qpos_ref, kpos_ref, out_ref, *, q_width, k_width, head_dim, blocks):
    rows = qkv_ref.shape[0]
    block = rows // blocks
    kv_heads = k_width // head_dim
    group = q_width // head_dim // kv_heads
    scale = head_dim ** (-0.5)
    for i in range(blocks):
        key_rows = block * (i + 1)
        rows_here = pl.ds(i * block, block)
        allowed = kpos_ref[:, :key_rows] <= qpos_ref[rows_here, :]
        for h in range(kv_heads):
            k_col = q_width + h * head_dim
            v_col = q_width + k_width + h * head_dim
            keys = qkv_ref[:key_rows, k_col : k_col + head_dim]
            values = qkv_ref[:key_rows, v_col : v_col + head_dim]
            for g in range(group):
                q_col = (h * group + g) * head_dim
                queries = qkv_ref[rows_here, q_col : q_col + head_dim]
                scores = lax.dot_general(
                    queries,
                    keys,
                    (((1,), (1,)), ((), ())),
                    preferred_element_type=jnp.float32,
                ) * scale
                scores = jnp.where(allowed, scores, -jnp.inf)
                row_max = jnp.max(scores, axis=-1, keepdims=True)
                weights = jnp.exp(scores - row_max)
                weights = (weights / jnp.sum(weights, axis=-1, keepdims=True)).astype(jnp.bfloat16)
                mixed = jnp.dot(weights, values, preferred_element_type=jnp.float32)
                out_ref[rows_here, q_col : q_col + head_dim] = mixed.astype(out_ref.dtype)


def attend(qkv_slot, query_pos, key_pos, q_width, k_width, head_dim):
    rows = qkv_slot.shape[0]
    blocks = 4
    heads = q_width // head_dim
    causal_pairs = blocks * (blocks + 1) // 2
    pair_flops = 4 * (rows // blocks) ** 2 * head_dim
    vmem = pl.BlockSpec(memory_space=pltpu.VMEM)
    return pl.pallas_call(
        lambda *refs: attention_kernel(
            *refs, q_width=q_width, k_width=k_width, head_dim=head_dim, blocks=blocks
        ),
        out_shape=jax.ShapeDtypeStruct((rows, q_width), jnp.bfloat16),
        in_specs=[vmem, vmem, vmem],
        out_specs=vmem,
        cost_estimate=pl.CostEstimate(
            flops=heads * causal_pairs * pair_flops,
            transcendentals=heads * causal_pairs * (rows // blocks) ** 2,
            bytes_accessed=qkv_slot.size * 2 + rows * q_width * 2,
        ),
    )(qkv_slot, query_pos[:, None], key_pos[None, :])


def on_device(
    hidden, lengths, dealing, norm_gain, w_query, w_key, w_value, query_gain, key_gain, w_out
):
    devices = lax.axis_size("req")
    home_index = lax.axis_index("req")
    slice_index = lax.axis_index("tp")
    tok_rows, features = hidden.shape
    head_dim = query_gain.shape[0]
    out_width = w_out.shape[1]
    q_width = w_query.shape[1]
    k_width = w_key.shape[1]
    slot_len = 4 * tok_rows
    capacity = slot_len // devices
    prompt_total = lengths.shape[0]
    prompt_ids = jnp.arange(prompt_total, dtype=jnp.int32)
    prompt_ends = jnp.cumsum(lengths)
    starts = prompt_ends - lengths
    packed_ids = jnp.arange(tok_rows, dtype=jnp.int32) * devices + home_index
    segment = jnp.sum((packed_ids[:, None] >= prompt_ends[None, :]).astype(jnp.int32), axis=1)
    seg_onehot = (segment[:, None] == prompt_ids[None, :]).astype(jnp.int32)
    positions = packed_ids - jnp.sum(seg_onehot * starts[None, :], axis=1)
    picked = prepare(
        hidden,
        lengths,
        dealing,
        jnp.reshape(home_index, (1,)).astype(jnp.int32),
        norm_gain,
        w_query,
        w_key,
        w_value,
        query_gain,
        key_gain,
        positions,
        capacity,
    )
    picked, lengths, dealing, starts, seg_onehot = lax.optimization_barrier(
        (picked, lengths, dealing, starts, seg_onehot)
    )
    inverse = jnp.zeros((prompt_total,), jnp.int32).at[dealing].set(prompt_ids)
    deal_hot = (dealing[:, None] == prompt_ids[None, :]).astype(jnp.int32)
    dealt_starts = jnp.sum(deal_hot * starts[None, :], axis=1)
    dealt_lengths = jnp.sum(deal_hot * lengths[None, :], axis=1)
    ranks = jnp.arange(capacity, dtype=jnp.int32)
    my_start = lax.dynamic_index_in_dim(dealt_starts, home_index, 0, keepdims=False)
    my_length = lax.dynamic_index_in_dim(dealt_lengths, home_index, 0, keepdims=False)
    roll_shift = jnp.mod(my_start, devices)
    my_slots = jnp.sum(seg_onehot * inverse[None, :], axis=1)
    back_rows = my_slots * capacity + positions // devices
    arrived = lax.all_to_all(
        picked.reshape(devices, capacity, picked.shape[1]),
        "req",
        split_axis=0,
        concat_axis=0,
        tiled=True,
    ).transpose(1, 0, 2)
    source_ids = jnp.arange(devices, dtype=jnp.int32)
    arrived_pos = (
        ranks[:, None] * devices + jnp.mod(source_ids[None, :] - my_start, devices)
    ).reshape(-1)
    key_pos = jnp.where(arrived_pos < my_length, arrived_pos, 1 << 30)
    mixture = attend(
        arrived.reshape(slot_len, arrived.shape[2]), arrived_pos, key_pos, q_width, k_width, head_dim
    )
    returned = lax.all_to_all(
        mixture.reshape(capacity, devices, mixture.shape[1]).transpose(1, 0, 2),
        "req",
        split_axis=0,
        concat_axis=0,
        tiled=True,
    )
    attended = jnp.take(returned.reshape(capacity * devices, -1), back_rows, axis=0)
    kv_rows = jnp.roll(arrived[:, :, q_width:], -roll_shift, axis=1).reshape(slot_len, -1)
    kv_cache = jnp.stack([kv_rows[:, :k_width], kv_rows[:, k_width:]])[:, None]
    tp_size = lax.axis_size("tp")
    w_rows = w_out.shape[0] // tp_size
    summed = jnp.dot(
        attended,
        lax.dynamic_slice_in_dim(w_out, slice_index * w_rows, w_rows, 0),
        preferred_element_type=jnp.float32,
    )
    for shift in range(1, tp_size):
        passed = lax.ppermute(
            attended, "tp", perm=[(i, (i + shift) % tp_size) for i in range(tp_size)]
        )
        source = jnp.mod(slice_index - shift, tp_size)
        summed = summed + jnp.dot(
            passed,
            lax.dynamic_slice_in_dim(w_out, source * w_rows, w_rows, 0),
            preferred_element_type=jnp.float32,
        )
    branch = lax.optimization_barrier(summed.astype(jnp.bfloat16))
    residual = lax.dynamic_slice_in_dim(hidden, slice_index * out_width, out_width, 1)
    hidden_out = (residual.astype(jnp.float32) + branch.astype(jnp.float32)).astype(jnp.bfloat16)
    return (hidden_out, kv_cache)


def solution(mesh):
    in_specs = (
        P("req", None),
        P(),
        P(),
        P(),
        P(None, "tp"),
        P(None, "tp"),
        P(None, "tp"),
        P(),
        P(),
        P(None, "tp"),
    )
    out_specs = (P("req", "tp"), P(None, "req", None, "tp"))
    return jax.shard_map(
        on_device, mesh=mesh, in_specs=in_specs, out_specs=out_specs, check_vma=False
    )
```

```python
import jax
import jax.numpy as jnp
from jax import lax
from jax.experimental import pallas as pl
from jax.experimental.pallas import tpu as pltpu
from jax.sharding import PartitionSpec as P

EPS = 1e-06
THETA = 1000000.0


def rms_rows(values, scale_gain):
    inv_rms = lax.rsqrt(jnp.mean(values * values, axis=-1, keepdims=True) + EPS)
    return values * inv_rms * scale_gain


def rotate(values, positions):
    features = values.shape[-1]
    half_width = features // 2
    frequency = THETA ** (-(jnp.arange(half_width).astype(jnp.float32) * 2.0) / features)
    angles = positions.astype(jnp.float32)[:, None] * frequency[None, :]
    cosine = jnp.cos(angles)[:, None, :]
    sine_part = jnp.sin(angles)[:, None, :]
    first_half = values[..., :half_width]
    second_half = values[..., half_width:]
    return jnp.concatenate(
        [
            first_half * cosine - second_half * sine_part,
            second_half * cosine + first_half * sine_part,
        ],
        axis=-1,
    )


def project(normed, w_query, w_key, w_value, query_gain, key_gain, positions):
    head_dim = query_gain.shape[0]
    row_count = normed.shape[0]
    query_rows = jnp.dot(normed, w_query, preferred_element_type=jnp.float32).reshape(
        row_count, -1, head_dim
    )
    key_rows = jnp.dot(normed, w_key, preferred_element_type=jnp.float32).reshape(
        row_count, -1, head_dim
    )
    value_rows = jnp.dot(normed, w_value, preferred_element_type=jnp.float32).astype(jnp.bfloat16)
    query_rows = rotate(rms_rows(query_rows, query_gain.astype(jnp.float32)), positions).astype(
        jnp.bfloat16
    )
    key_rows = rotate(rms_rows(key_rows, key_gain.astype(jnp.float32)), positions).astype(
        jnp.bfloat16
    )
    return (query_rows.reshape(row_count, -1), key_rows.reshape(row_count, -1), value_rows)


def prep_kernel(
    lengths_ref,
    dealing_ref,
    home_ref,
    hidden_ref,
    norm_gain_ref,
    wq_ref,
    wk_ref,
    wv_ref,
    qgain_ref,
    kgain_ref,
    cos_ref,
    sin_ref,
    out_ref,
    qkv_ref,
    pick_ref,
    starts_ref,
    *,
    head_dim,
    capacity,
):
    devices = dealing_ref.shape[0]
    prompt_total = lengths_ref.shape[0]
    tok_rows = qkv_ref.shape[0]

    def running(p, total):
        starts_ref[p] = total
        return total + lengths_ref[p]

    lax.fori_loop(0, prompt_total, running, jnp.int32(0))
    home = home_ref[0]
    rank_ids = lax.broadcasted_iota(jnp.int32, (capacity, tok_rows), 0)
    row_gap = lax.broadcasted_iota(jnp.int32, (capacity, tok_rows), 1) - rank_ids

    def pick_rows(d, carry):
        prompt = dealing_ref[d]
        start = starts_ref[prompt]
        length = lengths_ref[prompt]
        first = lax.rem(lax.rem(home - start, devices) + devices, devices)
        first_row = lax.div(start + first - home, devices)
        count = jnp.minimum(lax.div(length - first + devices - 1, devices), capacity)
        hits = (row_gap == first_row) & (rank_ids < count)
        pick_ref[pl.ds(pl.multiple_of(d * capacity, capacity), capacity), :] = hits.astype(
            pick_ref.dtype
        )
        return carry

    lax.fori_loop(0, devices, pick_rows, 0)
    values = hidden_ref[...].astype(jnp.float32)
    inv_rms = lax.rsqrt(jnp.mean(values * values, axis=-1, keepdims=True) + EPS)
    normed = (values * inv_rms * norm_gain_ref[...].astype(jnp.float32)[None, :]).astype(
        jnp.bfloat16
    )
    cosine = cos_ref[...]
    sine = sin_ref[...]
    column = 0
    for w_ref, gain_ref in ((wq_ref, qgain_ref), (wk_ref, kgain_ref)):
        rows = jnp.dot(normed, w_ref[...], preferred_element_type=jnp.float32)
        gain = gain_ref[...].astype(jnp.float32)
        for h in range(rows.shape[1] // head_dim):
            head = rows[:, h * head_dim : (h + 1) * head_dim]
            head_inv = lax.rsqrt(jnp.mean(head * head, axis=-1, keepdims=True) + EPS)
            head = head * head_inv * gain
            swapped = pltpu.roll(head, head_dim // 2, 1)
            qkv_ref[:, column : column + head_dim] = (head * cosine + swapped * sine).astype(
                jnp.bfloat16
            )
            column += head_dim
    v_width = wv_ref.shape[1]
    qkv_ref[:, column : column + v_width] = jnp.dot(
        normed, wv_ref[...], preferred_element_type=jnp.float32
    ).astype(jnp.bfloat16)
    qkv = qkv_ref[...]
    out_rows = out_ref.shape[0]
    block = out_rows // 4
    for b in range(4):
        rows_here = pl.ds(b * block, block)
        out_ref[rows_here, :] = jnp.dot(
            pick_ref[rows_here, :], qkv, preferred_element_type=jnp.float32
        ).astype(out_ref.dtype)


def prepare(
    hidden, lengths, dealing, home, norm_gain, w_query, w_key, w_value, query_gain, key_gain,
    positions, capacity,
):
    tok_rows, features = hidden.shape
    head_dim = query_gain.shape[0]
    half_width = head_dim // 2
    width = w_query.shape[1] + w_key.shape[1] + w_value.shape[1]
    devices = dealing.shape[0]
    out_rows = devices * capacity
    frequency = THETA ** (-(jnp.arange(half_width).astype(jnp.float32) * 2.0) / head_dim)
    frequency = jnp.concatenate([frequency, frequency])
    angles = positions.astype(jnp.float32)[:, None] * frequency[None, :]
    sign = jnp.where(jnp.arange(head_dim) < half_width, -1.0, 1.0).astype(jnp.float32)
    cos_full = jnp.cos(angles)
    sin_signed = jnp.sin(angles) * sign[None, :]
    vmem = pl.BlockSpec(memory_space=pltpu.VMEM)
    smem = pl.BlockSpec(memory_space=pltpu.SMEM)
    return pl.pallas_call(
        lambda *refs: prep_kernel(*refs, head_dim=head_dim, capacity=capacity),
        out_shape=jax.ShapeDtypeStruct((out_rows, width), jnp.bfloat16),
        in_specs=[smem] * 3 + [vmem] * 9,
        out_specs=vmem,
        scratch_shapes=[
            pltpu.VMEM((tok_rows, width), jnp.bfloat16),
            pltpu.VMEM((out_rows, tok_rows), jnp.bfloat16),
            pltpu.SMEM((lengths.shape[0],), jnp.int32),
        ],
        cost_estimate=pl.CostEstimate(
            flops=2 * tok_rows * features * width + 2 * out_rows * tok_rows * width,
            transcendentals=tok_rows * 8,
            bytes_accessed=hidden.size * 2 + features * width * 2 + out_rows * width * 2,
        ),
    )(
        lengths,
        dealing,
        home,
        hidden,
        norm_gain,
        w_query,
        w_key,
        w_value,
        query_gain[None, :],
        key_gain[None, :],
        cos_full,
        sin_signed,
    )


def attention_kernel(qkv_ref, qpos_ref, kpos_ref, out_ref, *, q_width, k_width, head_dim, blocks):
    rows = qkv_ref.shape[0]
    block = rows // blocks
    kv_heads = k_width // head_dim
    group = q_width // head_dim // kv_heads
    scale = head_dim ** (-0.5)
    for i in range(blocks):
        key_rows = block * (i + 1)
        rows_here = pl.ds(i * block, block)
        allowed = kpos_ref[:, :key_rows] <= qpos_ref[rows_here, :]
        for h in range(kv_heads):
            k_col = q_width + h * head_dim
            v_col = q_width + k_width + h * head_dim
            keys = qkv_ref[:key_rows, k_col : k_col + head_dim]
            values = qkv_ref[:key_rows, v_col : v_col + head_dim]
            for g in range(group):
                q_col = (h * group + g) * head_dim
                queries = qkv_ref[rows_here, q_col : q_col + head_dim]
                scores = lax.dot_general(
                    queries,
                    keys,
                    (((1,), (1,)), ((), ())),
                    preferred_element_type=jnp.float32,
                ) * scale
                scores = jnp.where(allowed, scores, -jnp.inf)
                row_max = jnp.max(scores, axis=-1, keepdims=True)
                weights = jnp.exp(scores - row_max)
                weights = (weights / jnp.sum(weights, axis=-1, keepdims=True)).astype(jnp.bfloat16)
                mixed = jnp.dot(weights, values, preferred_element_type=jnp.float32)
                out_ref[rows_here, q_col : q_col + head_dim] = mixed.astype(out_ref.dtype)


def attend(qkv_slot, query_pos, key_pos, q_width, k_width, head_dim):
    rows = qkv_slot.shape[0]
    blocks = 4
    heads = q_width // head_dim
    causal_pairs = blocks * (blocks + 1) // 2
    pair_flops = 4 * (rows // blocks) ** 2 * head_dim
    vmem = pl.BlockSpec(memory_space=pltpu.VMEM)
    return pl.pallas_call(
        lambda *refs: attention_kernel(
            *refs, q_width=q_width, k_width=k_width, head_dim=head_dim, blocks=blocks
        ),
        out_shape=jax.ShapeDtypeStruct((rows, q_width), jnp.bfloat16),
        in_specs=[vmem, vmem, vmem],
        out_specs=vmem,
        cost_estimate=pl.CostEstimate(
            flops=heads * causal_pairs * pair_flops,
            transcendentals=heads * causal_pairs * (rows // blocks) ** 2,
            bytes_accessed=qkv_slot.size * 2 + rows * q_width * 2,
        ),
    )(qkv_slot, query_pos[:, None], key_pos[None, :])


def on_device(
    hidden, lengths, dealing, norm_gain, w_query, w_key, w_value, query_gain, key_gain, w_out
):
    devices = lax.axis_size("req")
    home_index = lax.axis_index("req")
    slice_index = lax.axis_index("tp")
    tok_rows, features = hidden.shape
    head_dim = query_gain.shape[0]
    out_width = w_out.shape[1]
    q_width = w_query.shape[1]
    k_width = w_key.shape[1]
    slot_len = 4 * tok_rows
    capacity = slot_len // devices
    prompt_total = lengths.shape[0]
    prompt_ids = jnp.arange(prompt_total, dtype=jnp.int32)
    prompt_ends = jnp.cumsum(lengths)
    starts = prompt_ends - lengths
    packed_ids = jnp.arange(tok_rows, dtype=jnp.int32) * devices + home_index
    segment = jnp.sum((packed_ids[:, None] >= prompt_ends[None, :]).astype(jnp.int32), axis=1)
    seg_onehot = (segment[:, None] == prompt_ids[None, :]).astype(jnp.int32)
    positions = packed_ids - jnp.sum(seg_onehot * starts[None, :], axis=1)
    picked = prepare(
        hidden,
        lengths,
        dealing,
        jnp.reshape(home_index, (1,)).astype(jnp.int32),
        norm_gain,
        w_query,
        w_key,
        w_value,
        query_gain,
        key_gain,
        positions,
        capacity,
    )
    picked, lengths, dealing, starts, seg_onehot = lax.optimization_barrier(
        (picked, lengths, dealing, starts, seg_onehot)
    )
    inverse = jnp.zeros((prompt_total,), jnp.int32).at[dealing].set(prompt_ids)
    deal_hot = (dealing[:, None] == prompt_ids[None, :]).astype(jnp.int32)
    dealt_starts = jnp.sum(deal_hot * starts[None, :], axis=1)
    dealt_lengths = jnp.sum(deal_hot * lengths[None, :], axis=1)
    ranks = jnp.arange(capacity, dtype=jnp.int32)
    my_start = lax.dynamic_index_in_dim(dealt_starts, home_index, 0, keepdims=False)
    my_length = lax.dynamic_index_in_dim(dealt_lengths, home_index, 0, keepdims=False)
    roll_shift = jnp.mod(my_start, devices)
    my_slots = jnp.sum(seg_onehot * inverse[None, :], axis=1)
    back_rows = my_slots * capacity + positions // devices
    arrived = lax.all_to_all(
        picked.reshape(devices, capacity, picked.shape[1]),
        "req",
        split_axis=0,
        concat_axis=0,
        tiled=True,
    ).transpose(1, 0, 2)
    source_ids = jnp.arange(devices, dtype=jnp.int32)
    arrived_pos = (
        ranks[:, None] * devices + jnp.mod(source_ids[None, :] - my_start, devices)
    ).reshape(-1)
    key_pos = jnp.where(arrived_pos < my_length, arrived_pos, 1 << 30)
    mixture = attend(
        arrived.reshape(slot_len, arrived.shape[2]), arrived_pos, key_pos, q_width, k_width, head_dim
    )
    returned = lax.all_to_all(
        mixture.reshape(capacity, devices, mixture.shape[1]).transpose(1, 0, 2),
        "req",
        split_axis=0,
        concat_axis=0,
        tiled=True,
    )
    attended = jnp.take(returned.reshape(capacity * devices, -1), back_rows, axis=0)
    kv_rows = jnp.roll(arrived[:, :, q_width:], -roll_shift, axis=1).reshape(slot_len, -1)
    kv_cache = jnp.stack([kv_rows[:, :k_width], kv_rows[:, k_width:]])[:, None]
    tp_size = lax.axis_size("tp")
    w_rows = w_out.shape[0] // tp_size
    summed = jnp.dot(
        attended,
        lax.dynamic_slice_in_dim(w_out, slice_index * w_rows, w_rows, 0),
        preferred_element_type=jnp.float32,
    )
    for shift in range(1, tp_size):
        passed = lax.ppermute(
            attended, "tp", perm=[(i, (i + shift) % tp_size) for i in range(tp_size)]
        )
        source = jnp.mod(slice_index - shift, tp_size)
        summed = summed + jnp.dot(
            passed,
            lax.dynamic_slice_in_dim(w_out, source * w_rows, w_rows, 0),
            preferred_element_type=jnp.float32,
        )
    branch = lax.optimization_barrier(summed.astype(jnp.bfloat16))
    residual = lax.dynamic_slice_in_dim(hidden, slice_index * out_width, out_width, 1)
    hidden_out = (residual.astype(jnp.float32) + branch.astype(jnp.float32)).astype(jnp.bfloat16)
    return (hidden_out, kv_cache)


def solution(mesh):
    in_specs = (
        P("req", None),
        P(),
        P(),
        P(),
        P(None, "tp"),
        P(None, "tp"),
        P(None, "tp"),
        P(),
        P(),
        P(None, "tp"),
    )
    out_specs = (P("req", "tp"), P(None, "req", None, "tp"))
    return jax.shard_map(
        on_device, mesh=mesh, in_specs=in_specs, out_specs=out_specs, check_vma=False
    )
```

```python
import jax
import jax.numpy as jnp
from jax import lax
from jax.experimental import pallas as pl
from jax.experimental.pallas import tpu as pltpu
from jax.sharding import PartitionSpec as P

EPS = 1e-06
THETA = 1000000.0


def rms_rows(values, scale_gain):
    inv_rms = lax.rsqrt(jnp.mean(values * values, axis=-1, keepdims=True) + EPS)
    return values * inv_rms * scale_gain


def rotate(values, positions):
    features = values.shape[-1]
    half_width = features // 2
    frequency = THETA ** (-(jnp.arange(half_width).astype(jnp.float32) * 2.0) / features)
    angles = positions.astype(jnp.float32)[:, None] * frequency[None, :]
    cosine = jnp.cos(angles)[:, None, :]
    sine_part = jnp.sin(angles)[:, None, :]
    first_half = values[..., :half_width]
    second_half = values[..., half_width:]
    return jnp.concatenate(
        [
            first_half * cosine - second_half * sine_part,
            second_half * cosine + first_half * sine_part,
        ],
        axis=-1,
    )


def project(normed, w_query, w_key, w_value, query_gain, key_gain, positions):
    head_dim = query_gain.shape[0]
    row_count = normed.shape[0]
    query_rows = jnp.dot(normed, w_query, preferred_element_type=jnp.float32).reshape(
        row_count, -1, head_dim
    )
    key_rows = jnp.dot(normed, w_key, preferred_element_type=jnp.float32).reshape(
        row_count, -1, head_dim
    )
    value_rows = jnp.dot(normed, w_value, preferred_element_type=jnp.float32).astype(jnp.bfloat16)
    query_rows = rotate(rms_rows(query_rows, query_gain.astype(jnp.float32)), positions).astype(
        jnp.bfloat16
    )
    key_rows = rotate(rms_rows(key_rows, key_gain.astype(jnp.float32)), positions).astype(
        jnp.bfloat16
    )
    return (query_rows.reshape(row_count, -1), key_rows.reshape(row_count, -1), value_rows)


def prep_kernel(
    lengths_ref,
    dealing_ref,
    home_ref,
    hidden_ref,
    norm_gain_ref,
    wq_ref,
    wk_ref,
    wv_ref,
    qgain_ref,
    kgain_ref,
    cos_ref,
    sin_ref,
    out_ref,
    qkv_ref,
    pick_ref,
    starts_ref,
    *,
    head_dim,
    capacity,
):
    devices = dealing_ref.shape[0]
    prompt_total = lengths_ref.shape[0]
    tok_rows = qkv_ref.shape[0]

    def running(p, total):
        starts_ref[p] = total
        return total + lengths_ref[p]

    lax.fori_loop(0, prompt_total, running, jnp.int32(0))
    home = home_ref[0]
    rank_ids = lax.broadcasted_iota(jnp.int32, (capacity, tok_rows), 0)
    row_gap = lax.broadcasted_iota(jnp.int32, (capacity, tok_rows), 1) - rank_ids

    def pick_rows(d, carry):
        prompt = dealing_ref[d]
        start = starts_ref[prompt]
        length = lengths_ref[prompt]
        first = lax.rem(lax.rem(home - start, devices) + devices, devices)
        first_row = lax.div(start + first - home, devices)
        count = jnp.minimum(lax.div(length - first + devices - 1, devices), capacity)
        hits = (row_gap == first_row) & (rank_ids < count)
        pick_ref[pl.ds(pl.multiple_of(d * capacity, capacity), capacity), :] = hits.astype(
            pick_ref.dtype
        )
        return carry

    lax.fori_loop(0, devices, pick_rows, 0)
    values = hidden_ref[...].astype(jnp.float32)
    inv_rms = lax.rsqrt(jnp.mean(values * values, axis=-1, keepdims=True) + EPS)
    normed = (values * inv_rms * norm_gain_ref[...].astype(jnp.float32)[None, :]).astype(
        jnp.bfloat16
    )
    cosine = cos_ref[...]
    sine = sin_ref[...]
    column = 0
    for w_ref, gain_ref in ((wq_ref, qgain_ref), (wk_ref, kgain_ref)):
        rows = jnp.dot(normed, w_ref[...], preferred_element_type=jnp.float32)
        gain = gain_ref[...].astype(jnp.float32)
        for h in range(rows.shape[1] // head_dim):
            head = rows[:, h * head_dim : (h + 1) * head_dim]
            head_inv = lax.rsqrt(jnp.mean(head * head, axis=-1, keepdims=True) + EPS)
            head = head * head_inv * gain
            swapped = pltpu.roll(head, head_dim // 2, 1)
            qkv_ref[:, column : column + head_dim] = (head * cosine + swapped * sine).astype(
                jnp.bfloat16
            )
            column += head_dim
    v_width = wv_ref.shape[1]
    qkv_ref[:, column : column + v_width] = jnp.dot(
        normed, wv_ref[...], preferred_element_type=jnp.float32
    ).astype(jnp.bfloat16)
    qkv = qkv_ref[...]
    out_rows = out_ref.shape[0]
    block = out_rows // 4
    for b in range(4):
        rows_here = pl.ds(b * block, block)
        out_ref[rows_here, :] = jnp.dot(
            pick_ref[rows_here, :], qkv, preferred_element_type=jnp.float32
        ).astype(out_ref.dtype)


def prepare(
    hidden, lengths, dealing, home, norm_gain, w_query, w_key, w_value, query_gain, key_gain,
    positions, capacity,
):
    tok_rows, features = hidden.shape
    head_dim = query_gain.shape[0]
    half_width = head_dim // 2
    width = w_query.shape[1] + w_key.shape[1] + w_value.shape[1]
    devices = dealing.shape[0]
    out_rows = devices * capacity
    frequency = THETA ** (-(jnp.arange(half_width).astype(jnp.float32) * 2.0) / head_dim)
    frequency = jnp.concatenate([frequency, frequency])
    angles = positions.astype(jnp.float32)[:, None] * frequency[None, :]
    sign = jnp.where(jnp.arange(head_dim) < half_width, -1.0, 1.0).astype(jnp.float32)
    cos_full = jnp.cos(angles)
    sin_signed = jnp.sin(angles) * sign[None, :]
    vmem = pl.BlockSpec(memory_space=pltpu.VMEM)
    smem = pl.BlockSpec(memory_space=pltpu.SMEM)
    return pl.pallas_call(
        lambda *refs: prep_kernel(*refs, head_dim=head_dim, capacity=capacity),
        out_shape=jax.ShapeDtypeStruct((out_rows, width), jnp.bfloat16),
        in_specs=[smem] * 3 + [vmem] * 9,
        out_specs=vmem,
        scratch_shapes=[
            pltpu.VMEM((tok_rows, width), jnp.bfloat16),
            pltpu.VMEM((out_rows, tok_rows), jnp.bfloat16),
            pltpu.SMEM((lengths.shape[0],), jnp.int32),
        ],
        cost_estimate=pl.CostEstimate(
            flops=2 * tok_rows * features * width + 2 * out_rows * tok_rows * width,
            transcendentals=tok_rows * 8,
            bytes_accessed=hidden.size * 2 + features * width * 2 + out_rows * width * 2,
        ),
    )(
        lengths,
        dealing,
        home,
        hidden,
        norm_gain,
        w_query,
        w_key,
        w_value,
        query_gain[None, :],
        key_gain[None, :],
        cos_full,
        sin_signed,
    )


def attention_kernel(qkv_ref, qpos_ref, kpos_ref, out_ref, *, q_width, k_width, head_dim, blocks):
    rows = qkv_ref.shape[0]
    block = rows // blocks
    kv_heads = k_width // head_dim
    group = q_width // head_dim // kv_heads
    scale = head_dim ** (-0.5)
    for i in range(blocks):
        key_rows = block * (i + 1)
        rows_here = pl.ds(i * block, block)
        allowed = kpos_ref[:, :key_rows] <= qpos_ref[rows_here, :]
        for h in range(kv_heads):
            k_col = q_width + h * head_dim
            v_col = q_width + k_width + h * head_dim
            keys = qkv_ref[:key_rows, k_col : k_col + head_dim]
            values = qkv_ref[:key_rows, v_col : v_col + head_dim]
            for g in range(group):
                q_col = (h * group + g) * head_dim
                queries = qkv_ref[rows_here, q_col : q_col + head_dim]
                scores = lax.dot_general(
                    queries,
                    keys,
                    (((1,), (1,)), ((), ())),
                    preferred_element_type=jnp.float32,
                ) * scale
                scores = jnp.where(allowed, scores, -jnp.inf)
                row_max = jnp.max(scores, axis=-1, keepdims=True)
                weights = jnp.exp(scores - row_max)
                weights = (weights / jnp.sum(weights, axis=-1, keepdims=True)).astype(jnp.bfloat16)
                mixed = jnp.dot(weights, values, preferred_element_type=jnp.float32)
                out_ref[rows_here, q_col : q_col + head_dim] = mixed.astype(out_ref.dtype)


def attend(qkv_slot, query_pos, key_pos, q_width, k_width, head_dim):
    rows = qkv_slot.shape[0]
    blocks = 8
    heads = q_width // head_dim
    causal_pairs = blocks * (blocks + 1) // 2
    pair_flops = 4 * (rows // blocks) ** 2 * head_dim
    vmem = pl.BlockSpec(memory_space=pltpu.VMEM)
    return pl.pallas_call(
        lambda *refs: attention_kernel(
            *refs, q_width=q_width, k_width=k_width, head_dim=head_dim, blocks=blocks
        ),
        out_shape=jax.ShapeDtypeStruct((rows, q_width), jnp.bfloat16),
        in_specs=[vmem, vmem, vmem],
        out_specs=vmem,
        cost_estimate=pl.CostEstimate(
            flops=heads * causal_pairs * pair_flops,
            transcendentals=heads * causal_pairs * (rows // blocks) ** 2,
            bytes_accessed=qkv_slot.size * 2 + rows * q_width * 2,
        ),
    )(qkv_slot, query_pos[:, None], key_pos[None, :])


def on_device(
    hidden, lengths, dealing, norm_gain, w_query, w_key, w_value, query_gain, key_gain, w_out
):
    devices = lax.axis_size("req")
    home_index = lax.axis_index("req")
    slice_index = lax.axis_index("tp")
    tok_rows, features = hidden.shape
    head_dim = query_gain.shape[0]
    out_width = w_out.shape[1]
    q_width = w_query.shape[1]
    k_width = w_key.shape[1]
    slot_len = 4 * tok_rows
    capacity = slot_len // devices
    prompt_total = lengths.shape[0]
    prompt_ids = jnp.arange(prompt_total, dtype=jnp.int32)
    prompt_ends = jnp.cumsum(lengths)
    starts = prompt_ends - lengths
    packed_ids = jnp.arange(tok_rows, dtype=jnp.int32) * devices + home_index
    segment = jnp.sum((packed_ids[:, None] >= prompt_ends[None, :]).astype(jnp.int32), axis=1)
    seg_onehot = (segment[:, None] == prompt_ids[None, :]).astype(jnp.int32)
    positions = packed_ids - jnp.sum(seg_onehot * starts[None, :], axis=1)
    picked = prepare(
        hidden,
        lengths,
        dealing,
        jnp.reshape(home_index, (1,)).astype(jnp.int32),
        norm_gain,
        w_query,
        w_key,
        w_value,
        query_gain,
        key_gain,
        positions,
        capacity,
    )
    picked, lengths, dealing, starts, seg_onehot = lax.optimization_barrier(
        (picked, lengths, dealing, starts, seg_onehot)
    )
    inverse = jnp.zeros((prompt_total,), jnp.int32).at[dealing].set(prompt_ids)
    deal_hot = (dealing[:, None] == prompt_ids[None, :]).astype(jnp.int32)
    dealt_starts = jnp.sum(deal_hot * starts[None, :], axis=1)
    dealt_lengths = jnp.sum(deal_hot * lengths[None, :], axis=1)
    ranks = jnp.arange(capacity, dtype=jnp.int32)
    my_start = lax.dynamic_index_in_dim(dealt_starts, home_index, 0, keepdims=False)
    my_length = lax.dynamic_index_in_dim(dealt_lengths, home_index, 0, keepdims=False)
    roll_shift = jnp.mod(my_start, devices)
    my_slots = jnp.sum(seg_onehot * inverse[None, :], axis=1)
    back_rows = my_slots * capacity + positions // devices
    arrived = lax.all_to_all(
        picked.reshape(devices, capacity, picked.shape[1]),
        "req",
        split_axis=0,
        concat_axis=0,
        tiled=True,
    ).transpose(1, 0, 2)
    source_ids = jnp.arange(devices, dtype=jnp.int32)
    arrived_pos = (
        ranks[:, None] * devices + jnp.mod(source_ids[None, :] - my_start, devices)
    ).reshape(-1)
    key_pos = jnp.where(arrived_pos < my_length, arrived_pos, 1 << 30)
    mixture = attend(
        arrived.reshape(slot_len, arrived.shape[2]), arrived_pos, key_pos, q_width, k_width, head_dim
    )
    returned = lax.all_to_all(
        mixture.reshape(capacity, devices, mixture.shape[1]).transpose(1, 0, 2),
        "req",
        split_axis=0,
        concat_axis=0,
        tiled=True,
    )
    attended = jnp.take(returned.reshape(capacity * devices, -1), back_rows, axis=0)
    kv_rows = jnp.roll(arrived[:, :, q_width:], -roll_shift, axis=1).reshape(slot_len, -1)
    kv_cache = jnp.stack([kv_rows[:, :k_width], kv_rows[:, k_width:]])[:, None]
    tp_size = lax.axis_size("tp")
    w_rows = w_out.shape[0] // tp_size
    summed = jnp.dot(
        attended,
        lax.dynamic_slice_in_dim(w_out, slice_index * w_rows, w_rows, 0),
        preferred_element_type=jnp.float32,
    )
    for shift in range(1, tp_size):
        passed = lax.ppermute(
            attended, "tp", perm=[(i, (i + shift) % tp_size) for i in range(tp_size)]
        )
        source = jnp.mod(slice_index - shift, tp_size)
        summed = summed + jnp.dot(
            passed,
            lax.dynamic_slice_in_dim(w_out, source * w_rows, w_rows, 0),
            preferred_element_type=jnp.float32,
        )
    branch = lax.optimization_barrier(summed.astype(jnp.bfloat16))
    residual = lax.dynamic_slice_in_dim(hidden, slice_index * out_width, out_width, 1)
    hidden_out = (residual.astype(jnp.float32) + branch.astype(jnp.float32)).astype(jnp.bfloat16)
    return (hidden_out, kv_cache)


def solution(mesh):
    in_specs = (
        P("req", None),
        P(),
        P(),
        P(),
        P(None, "tp"),
        P(None, "tp"),
        P(None, "tp"),
        P(),
        P(),
        P(None, "tp"),
    )
    out_specs = (P("req", "tp"), P(None, "req", None, "tp"))
    return jax.shard_map(
        on_device, mesh=mesh, in_specs=in_specs, out_specs=out_specs, check_vma=False
    )
```

```python
import jax
import jax.numpy as jnp
from jax import lax
from jax.experimental import pallas as pl
from jax.experimental.pallas import tpu as pltpu
from jax.sharding import PartitionSpec as P

EPS = 1e-06
THETA = 1000000.0


def rms_rows(values, scale_gain):
    inv_rms = lax.rsqrt(jnp.mean(values * values, axis=-1, keepdims=True) + EPS)
    return values * inv_rms * scale_gain


def rotate(values, positions):
    features = values.shape[-1]
    half_width = features // 2
    frequency = THETA ** (-(jnp.arange(half_width).astype(jnp.float32) * 2.0) / features)
    angles = positions.astype(jnp.float32)[:, None] * frequency[None, :]
    cosine = jnp.cos(angles)[:, None, :]
    sine_part = jnp.sin(angles)[:, None, :]
    first_half = values[..., :half_width]
    second_half = values[..., half_width:]
    return jnp.concatenate(
        [
            first_half * cosine - second_half * sine_part,
            second_half * cosine + first_half * sine_part,
        ],
        axis=-1,
    )


def project(normed, w_query, w_key, w_value, query_gain, key_gain, positions):
    head_dim = query_gain.shape[0]
    row_count = normed.shape[0]
    query_rows = jnp.dot(normed, w_query, preferred_element_type=jnp.float32).reshape(
        row_count, -1, head_dim
    )
    key_rows = jnp.dot(normed, w_key, preferred_element_type=jnp.float32).reshape(
        row_count, -1, head_dim
    )
    value_rows = jnp.dot(normed, w_value, preferred_element_type=jnp.float32).astype(jnp.bfloat16)
    query_rows = rotate(rms_rows(query_rows, query_gain.astype(jnp.float32)), positions).astype(
        jnp.bfloat16
    )
    key_rows = rotate(rms_rows(key_rows, key_gain.astype(jnp.float32)), positions).astype(
        jnp.bfloat16
    )
    return (query_rows.reshape(row_count, -1), key_rows.reshape(row_count, -1), value_rows)


def prep_kernel(
    lengths_ref,
    dealing_ref,
    home_ref,
    hidden_ref,
    norm_gain_ref,
    wq_ref,
    wk_ref,
    wv_ref,
    qgain_ref,
    kgain_ref,
    cos_ref,
    sin_ref,
    out_ref,
    qkv_ref,
    pick_ref,
    starts_ref,
    *,
    head_dim,
    capacity,
):
    devices = dealing_ref.shape[0]
    prompt_total = lengths_ref.shape[0]
    tok_rows = qkv_ref.shape[0]

    def running(p, total):
        starts_ref[p] = total
        return total + lengths_ref[p]

    lax.fori_loop(0, prompt_total, running, jnp.int32(0))
    home = home_ref[0]
    rank_ids = lax.broadcasted_iota(jnp.int32, (capacity, tok_rows), 0)
    row_gap = lax.broadcasted_iota(jnp.int32, (capacity, tok_rows), 1) - rank_ids

    def pick_rows(d, carry):
        prompt = dealing_ref[d]
        start = starts_ref[prompt]
        length = lengths_ref[prompt]
        first = lax.rem(lax.rem(home - start, devices) + devices, devices)
        first_row = lax.div(start + first - home, devices)
        count = jnp.minimum(lax.div(length - first + devices - 1, devices), capacity)
        hits = (row_gap == first_row) & (rank_ids < count)
        pick_ref[pl.ds(pl.multiple_of(d * capacity, capacity), capacity), :] = hits.astype(
            pick_ref.dtype
        )
        return carry

    lax.fori_loop(0, devices, pick_rows, 0)
    values = hidden_ref[...].astype(jnp.float32)
    inv_rms = lax.rsqrt(jnp.mean(values * values, axis=-1, keepdims=True) + EPS)
    normed = (values * inv_rms * norm_gain_ref[...].astype(jnp.float32)[None, :]).astype(
        jnp.bfloat16
    )
    cosine = cos_ref[...]
    sine = sin_ref[...]
    column = 0
    for w_ref, gain_ref in ((wq_ref, qgain_ref), (wk_ref, kgain_ref)):
        rows = jnp.dot(normed, w_ref[...], preferred_element_type=jnp.float32)
        gain = gain_ref[...].astype(jnp.float32)
        for h in range(rows.shape[1] // head_dim):
            head = rows[:, h * head_dim : (h + 1) * head_dim]
            head_inv = lax.rsqrt(jnp.mean(head * head, axis=-1, keepdims=True) + EPS)
            head = head * head_inv * gain
            swapped = pltpu.roll(head, head_dim // 2, 1)
            qkv_ref[:, column : column + head_dim] = (head * cosine + swapped * sine).astype(
                jnp.bfloat16
            )
            column += head_dim
    v_width = wv_ref.shape[1]
    qkv_ref[:, column : column + v_width] = jnp.dot(
        normed, wv_ref[...], preferred_element_type=jnp.float32
    ).astype(jnp.bfloat16)
    qkv = qkv_ref[...]
    out_rows = out_ref.shape[0]
    block = out_rows // 4
    for b in range(4):
        rows_here = pl.ds(b * block, block)
        out_ref[rows_here, :] = jnp.dot(
            pick_ref[rows_here, :], qkv, preferred_element_type=jnp.float32
        ).astype(out_ref.dtype)


def prepare(
    hidden, lengths, dealing, home, norm_gain, w_query, w_key, w_value, query_gain, key_gain,
    positions, capacity,
):
    tok_rows, features = hidden.shape
    head_dim = query_gain.shape[0]
    half_width = head_dim // 2
    width = w_query.shape[1] + w_key.shape[1] + w_value.shape[1]
    devices = dealing.shape[0]
    out_rows = devices * capacity
    frequency = THETA ** (-(jnp.arange(half_width).astype(jnp.float32) * 2.0) / head_dim)
    frequency = jnp.concatenate([frequency, frequency])
    angles = positions.astype(jnp.float32)[:, None] * frequency[None, :]
    sign = jnp.where(jnp.arange(head_dim) < half_width, -1.0, 1.0).astype(jnp.float32)
    cos_full = jnp.cos(angles)
    sin_signed = jnp.sin(angles) * sign[None, :]
    vmem = pl.BlockSpec(memory_space=pltpu.VMEM)
    smem = pl.BlockSpec(memory_space=pltpu.SMEM)
    return pl.pallas_call(
        lambda *refs: prep_kernel(*refs, head_dim=head_dim, capacity=capacity),
        out_shape=jax.ShapeDtypeStruct((out_rows, width), jnp.bfloat16),
        in_specs=[smem] * 3 + [vmem] * 9,
        out_specs=vmem,
        scratch_shapes=[
            pltpu.VMEM((tok_rows, width), jnp.bfloat16),
            pltpu.VMEM((out_rows, tok_rows), jnp.bfloat16),
            pltpu.SMEM((lengths.shape[0],), jnp.int32),
        ],
        cost_estimate=pl.CostEstimate(
            flops=2 * tok_rows * features * width + 2 * out_rows * tok_rows * width,
            transcendentals=tok_rows * 8,
            bytes_accessed=hidden.size * 2 + features * width * 2 + out_rows * width * 2,
        ),
    )(
        lengths,
        dealing,
        home,
        hidden,
        norm_gain,
        w_query,
        w_key,
        w_value,
        query_gain[None, :],
        key_gain[None, :],
        cos_full,
        sin_signed,
    )


def attention_kernel(qkv_ref, qpos_ref, kpos_ref, out_ref, *, q_width, k_width, head_dim, blocks):
    rows = qkv_ref.shape[0]
    block = rows // blocks
    kv_heads = k_width // head_dim
    group = q_width // head_dim // kv_heads
    scale = head_dim ** (-0.5)
    for i in range(blocks):
        key_rows = block * (i + 1)
        rows_here = pl.ds(i * block, block)
        allowed = kpos_ref[:, :key_rows] <= qpos_ref[rows_here, :]
        for h in range(kv_heads):
            k_col = q_width + h * head_dim
            v_col = q_width + k_width + h * head_dim
            keys = qkv_ref[:key_rows, k_col : k_col + head_dim]
            values = qkv_ref[:key_rows, v_col : v_col + head_dim]
            for g in range(group):
                q_col = (h * group + g) * head_dim
                queries = qkv_ref[rows_here, q_col : q_col + head_dim]
                scores = lax.dot_general(
                    queries,
                    keys,
                    (((1,), (1,)), ((), ())),
                    preferred_element_type=jnp.float32,
                ) * scale
                scores = jnp.where(allowed, scores, -jnp.inf)
                row_max = jnp.max(scores, axis=-1, keepdims=True)
                weights = jnp.exp(scores - row_max)
                weights = (weights / jnp.sum(weights, axis=-1, keepdims=True)).astype(jnp.bfloat16)
                mixed = jnp.dot(weights, values, preferred_element_type=jnp.float32)
                out_ref[rows_here, q_col : q_col + head_dim] = mixed.astype(out_ref.dtype)


def attend(qkv_slot, query_pos, key_pos, q_width, k_width, head_dim):
    rows = qkv_slot.shape[0]
    blocks = 2
    heads = q_width // head_dim
    causal_pairs = blocks * (blocks + 1) // 2
    pair_flops = 4 * (rows // blocks) ** 2 * head_dim
    vmem = pl.BlockSpec(memory_space=pltpu.VMEM)
    return pl.pallas_call(
        lambda *refs: attention_kernel(
            *refs, q_width=q_width, k_width=k_width, head_dim=head_dim, blocks=blocks
        ),
        out_shape=jax.ShapeDtypeStruct((rows, q_width), jnp.bfloat16),
        in_specs=[vmem, vmem, vmem],
        out_specs=vmem,
        cost_estimate=pl.CostEstimate(
            flops=heads * causal_pairs * pair_flops,
            transcendentals=heads * causal_pairs * (rows // blocks) ** 2,
            bytes_accessed=qkv_slot.size * 2 + rows * q_width * 2,
        ),
    )(qkv_slot, query_pos[:, None], key_pos[None, :])


def on_device(
    hidden, lengths, dealing, norm_gain, w_query, w_key, w_value, query_gain, key_gain, w_out
):
    devices = lax.axis_size("req")
    home_index = lax.axis_index("req")
    slice_index = lax.axis_index("tp")
    tok_rows, features = hidden.shape
    head_dim = query_gain.shape[0]
    out_width = w_out.shape[1]
    q_width = w_query.shape[1]
    k_width = w_key.shape[1]
    slot_len = 4 * tok_rows
    capacity = slot_len // devices
    prompt_total = lengths.shape[0]
    prompt_ids = jnp.arange(prompt_total, dtype=jnp.int32)
    prompt_ends = jnp.cumsum(lengths)
    starts = prompt_ends - lengths
    packed_ids = jnp.arange(tok_rows, dtype=jnp.int32) * devices + home_index
    segment = jnp.sum((packed_ids[:, None] >= prompt_ends[None, :]).astype(jnp.int32), axis=1)
    seg_onehot = (segment[:, None] == prompt_ids[None, :]).astype(jnp.int32)
    positions = packed_ids - jnp.sum(seg_onehot * starts[None, :], axis=1)
    picked = prepare(
        hidden,
        lengths,
        dealing,
        jnp.reshape(home_index, (1,)).astype(jnp.int32),
        norm_gain,
        w_query,
        w_key,
        w_value,
        query_gain,
        key_gain,
        positions,
        capacity,
    )
    picked, lengths, dealing, starts, seg_onehot = lax.optimization_barrier(
        (picked, lengths, dealing, starts, seg_onehot)
    )
    inverse = jnp.zeros((prompt_total,), jnp.int32).at[dealing].set(prompt_ids)
    deal_hot = (dealing[:, None] == prompt_ids[None, :]).astype(jnp.int32)
    dealt_starts = jnp.sum(deal_hot * starts[None, :], axis=1)
    dealt_lengths = jnp.sum(deal_hot * lengths[None, :], axis=1)
    ranks = jnp.arange(capacity, dtype=jnp.int32)
    my_start = lax.dynamic_index_in_dim(dealt_starts, home_index, 0, keepdims=False)
    my_length = lax.dynamic_index_in_dim(dealt_lengths, home_index, 0, keepdims=False)
    roll_shift = jnp.mod(my_start, devices)
    my_slots = jnp.sum(seg_onehot * inverse[None, :], axis=1)
    back_rows = my_slots * capacity + positions // devices
    arrived = lax.all_to_all(
        picked.reshape(devices, capacity, picked.shape[1]),
        "req",
        split_axis=0,
        concat_axis=0,
        tiled=True,
    ).transpose(1, 0, 2)
    source_ids = jnp.arange(devices, dtype=jnp.int32)
    arrived_pos = (
        ranks[:, None] * devices + jnp.mod(source_ids[None, :] - my_start, devices)
    ).reshape(-1)
    key_pos = jnp.where(arrived_pos < my_length, arrived_pos, 1 << 30)
    mixture = attend(
        arrived.reshape(slot_len, arrived.shape[2]), arrived_pos, key_pos, q_width, k_width, head_dim
    )
    returned = lax.all_to_all(
        mixture.reshape(capacity, devices, mixture.shape[1]).transpose(1, 0, 2),
        "req",
        split_axis=0,
        concat_axis=0,
        tiled=True,
    )
    attended = jnp.take(returned.reshape(capacity * devices, -1), back_rows, axis=0)
    kv_rows = jnp.roll(arrived[:, :, q_width:], -roll_shift, axis=1).reshape(slot_len, -1)
    kv_cache = jnp.stack([kv_rows[:, :k_width], kv_rows[:, k_width:]])[:, None]
    tp_size = lax.axis_size("tp")
    w_rows = w_out.shape[0] // tp_size
    summed = jnp.dot(
        attended,
        lax.dynamic_slice_in_dim(w_out, slice_index * w_rows, w_rows, 0),
        preferred_element_type=jnp.float32,
    )
    for shift in range(1, tp_size):
        passed = lax.ppermute(
            attended, "tp", perm=[(i, (i + shift) % tp_size) for i in range(tp_size)]
        )
        source = jnp.mod(slice_index - shift, tp_size)
        summed = summed + jnp.dot(
            passed,
            lax.dynamic_slice_in_dim(w_out, source * w_rows, w_rows, 0),
            preferred_element_type=jnp.float32,
        )
    branch = lax.optimization_barrier(summed.astype(jnp.bfloat16))
    residual = lax.dynamic_slice_in_dim(hidden, slice_index * out_width, out_width, 1)
    hidden_out = (residual.astype(jnp.float32) + branch.astype(jnp.float32)).astype(jnp.bfloat16)
    return (hidden_out, kv_cache)


def solution(mesh):
    in_specs = (
        P("req", None),
        P(),
        P(),
        P(),
        P(None, "tp"),
        P(None, "tp"),
        P(None, "tp"),
        P(),
        P(),
        P(None, "tp"),
    )
    out_specs = (P("req", "tp"), P(None, "req", None, "tp"))
    return jax.shard_map(
        on_device, mesh=mesh, in_specs=in_specs, out_specs=out_specs, check_vma=False
    )
```

```python
import jax
import jax.numpy as jnp
from jax import lax
from jax.experimental import pallas as pl
from jax.experimental.pallas import tpu as pltpu
from jax.sharding import PartitionSpec as P

EPS = 1e-06
THETA = 1000000.0


def rms_rows(values, scale_gain):
    inv_rms = lax.rsqrt(jnp.mean(values * values, axis=-1, keepdims=True) + EPS)
    return values * inv_rms * scale_gain


def rotate(values, positions):
    features = values.shape[-1]
    half_width = features // 2
    frequency = THETA ** (-(jnp.arange(half_width).astype(jnp.float32) * 2.0) / features)
    angles = positions.astype(jnp.float32)[:, None] * frequency[None, :]
    cosine = jnp.cos(angles)[:, None, :]
    sine_part = jnp.sin(angles)[:, None, :]
    first_half = values[..., :half_width]
    second_half = values[..., half_width:]
    return jnp.concatenate(
        [
            first_half * cosine - second_half * sine_part,
            second_half * cosine + first_half * sine_part,
        ],
        axis=-1,
    )


def project(normed, w_query, w_key, w_value, query_gain, key_gain, positions):
    head_dim = query_gain.shape[0]
    row_count = normed.shape[0]
    query_rows = jnp.dot(normed, w_query, preferred_element_type=jnp.float32).reshape(
        row_count, -1, head_dim
    )
    key_rows = jnp.dot(normed, w_key, preferred_element_type=jnp.float32).reshape(
        row_count, -1, head_dim
    )
    value_rows = jnp.dot(normed, w_value, preferred_element_type=jnp.float32).astype(jnp.bfloat16)
    query_rows = rotate(rms_rows(query_rows, query_gain.astype(jnp.float32)), positions).astype(
        jnp.bfloat16
    )
    key_rows = rotate(rms_rows(key_rows, key_gain.astype(jnp.float32)), positions).astype(
        jnp.bfloat16
    )
    return (query_rows.reshape(row_count, -1), key_rows.reshape(row_count, -1), value_rows)


def prep_kernel(
    lengths_ref,
    dealing_ref,
    home_ref,
    hidden_ref,
    norm_gain_ref,
    wq_ref,
    wk_ref,
    wv_ref,
    qgain_ref,
    kgain_ref,
    cos_ref,
    sin_ref,
    out_ref,
    qkv_ref,
    pick_ref,
    starts_ref,
    *,
    head_dim,
    capacity,
):
    devices = dealing_ref.shape[0]
    prompt_total = lengths_ref.shape[0]
    tok_rows = qkv_ref.shape[0]

    def running(p, total):
        starts_ref[p] = total
        return total + lengths_ref[p]

    lax.fori_loop(0, prompt_total, running, jnp.int32(0))
    home = home_ref[0]
    rank_ids = lax.broadcasted_iota(jnp.int32, (capacity, tok_rows), 0)
    row_gap = lax.broadcasted_iota(jnp.int32, (capacity, tok_rows), 1) - rank_ids

    def pick_rows(d, carry):
        prompt = dealing_ref[d]
        start = starts_ref[prompt]
        length = lengths_ref[prompt]
        first = lax.rem(lax.rem(home - start, devices) + devices, devices)
        first_row = lax.div(start + first - home, devices)
        count = jnp.minimum(lax.div(length - first + devices - 1, devices), capacity)
        hits = (row_gap == first_row) & (rank_ids < count)
        pick_ref[pl.ds(pl.multiple_of(d * capacity, capacity), capacity), :] = hits.astype(
            pick_ref.dtype
        )
        return carry

    lax.fori_loop(0, devices, pick_rows, 0)
    values = hidden_ref[...].astype(jnp.float32)
    inv_rms = lax.rsqrt(jnp.mean(values * values, axis=-1, keepdims=True) + EPS)
    normed = (values * inv_rms * norm_gain_ref[...].astype(jnp.float32)[None, :]).astype(
        jnp.bfloat16
    )
    cosine = cos_ref[...]
    sine = sin_ref[...]
    column = 0
    for w_ref, gain_ref in ((wq_ref, qgain_ref), (wk_ref, kgain_ref)):
        rows = jnp.dot(normed, w_ref[...], preferred_element_type=jnp.float32)
        gain = gain_ref[...].astype(jnp.float32)
        for h in range(rows.shape[1] // head_dim):
            head = rows[:, h * head_dim : (h + 1) * head_dim]
            head_inv = lax.rsqrt(jnp.mean(head * head, axis=-1, keepdims=True) + EPS)
            head = head * head_inv * gain
            swapped = pltpu.roll(head, head_dim // 2, 1)
            qkv_ref[:, column : column + head_dim] = (head * cosine + swapped * sine).astype(
                jnp.bfloat16
            )
            column += head_dim
    v_width = wv_ref.shape[1]
    qkv_ref[:, column : column + v_width] = jnp.dot(
        normed, wv_ref[...], preferred_element_type=jnp.float32
    ).astype(jnp.bfloat16)
    qkv = qkv_ref[...]
    out_rows = out_ref.shape[0]
    block = out_rows // 4
    for b in range(4):
        rows_here = pl.ds(b * block, block)
        out_ref[rows_here, :] = jnp.dot(
            pick_ref[rows_here, :], qkv, preferred_element_type=jnp.float32
        ).astype(out_ref.dtype)


def prepare(
    hidden, lengths, dealing, home, norm_gain, w_query, w_key, w_value, query_gain, key_gain,
    positions, capacity,
):
    tok_rows, features = hidden.shape
    head_dim = query_gain.shape[0]
    half_width = head_dim // 2
    width = w_query.shape[1] + w_key.shape[1] + w_value.shape[1]
    devices = dealing.shape[0]
    out_rows = devices * capacity
    frequency = THETA ** (-(jnp.arange(half_width).astype(jnp.float32) * 2.0) / head_dim)
    frequency = jnp.concatenate([frequency, frequency])
    angles = positions.astype(jnp.float32)[:, None] * frequency[None, :]
    sign = jnp.where(jnp.arange(head_dim) < half_width, -1.0, 1.0).astype(jnp.float32)
    cos_full = jnp.cos(angles)
    sin_signed = jnp.sin(angles) * sign[None, :]
    vmem = pl.BlockSpec(memory_space=pltpu.VMEM)
    smem = pl.BlockSpec(memory_space=pltpu.SMEM)
    return pl.pallas_call(
        lambda *refs: prep_kernel(*refs, head_dim=head_dim, capacity=capacity),
        out_shape=jax.ShapeDtypeStruct((out_rows, width), jnp.bfloat16),
        in_specs=[smem] * 3 + [vmem] * 9,
        out_specs=vmem,
        scratch_shapes=[
            pltpu.VMEM((tok_rows, width), jnp.bfloat16),
            pltpu.VMEM((out_rows, tok_rows), jnp.bfloat16),
            pltpu.SMEM((lengths.shape[0],), jnp.int32),
        ],
        cost_estimate=pl.CostEstimate(
            flops=2 * tok_rows * features * width + 2 * out_rows * tok_rows * width,
            transcendentals=tok_rows * 8,
            bytes_accessed=hidden.size * 2 + features * width * 2 + out_rows * width * 2,
        ),
    )(
        lengths,
        dealing,
        home,
        hidden,
        norm_gain,
        w_query,
        w_key,
        w_value,
        query_gain[None, :],
        key_gain[None, :],
        cos_full,
        sin_signed,
    )


def attention_kernel(qkv_ref, qpos_ref, kpos_ref, out_ref, *, q_width, k_width, head_dim, blocks):
    rows = qkv_ref.shape[0]
    block = rows // blocks
    kv_heads = k_width // head_dim
    group = q_width // head_dim // kv_heads
    scale = head_dim ** (-0.5)
    for i in range(blocks):
        key_rows = block * (i + 1)
        rows_here = pl.ds(i * block, block)
        allowed = kpos_ref[:, :key_rows] <= qpos_ref[rows_here, :]
        for h in range(kv_heads):
            k_col = q_width + h * head_dim
            v_col = q_width + k_width + h * head_dim
            keys = qkv_ref[:key_rows, k_col : k_col + head_dim]
            values = qkv_ref[:key_rows, v_col : v_col + head_dim]
            for g in range(group):
                q_col = (h * group + g) * head_dim
                queries = qkv_ref[rows_here, q_col : q_col + head_dim]
                scores = lax.dot_general(
                    queries,
                    keys,
                    (((1,), (1,)), ((), ())),
                    preferred_element_type=jnp.float32,
                ) * scale
                scores = jnp.where(allowed, scores, -jnp.inf)
                row_max = jnp.max(scores, axis=-1, keepdims=True)
                weights = jnp.exp(scores - row_max)
                weights = (weights / jnp.sum(weights, axis=-1, keepdims=True)).astype(jnp.bfloat16)
                mixed = jnp.dot(weights, values, preferred_element_type=jnp.float32)
                out_ref[rows_here, q_col : q_col + head_dim] = mixed.astype(out_ref.dtype)


def attend(qkv_slot, query_pos, key_pos, q_width, k_width, head_dim):
    rows = qkv_slot.shape[0]
    blocks = 1
    heads = q_width // head_dim
    causal_pairs = blocks * (blocks + 1) // 2
    pair_flops = 4 * (rows // blocks) ** 2 * head_dim
    vmem = pl.BlockSpec(memory_space=pltpu.VMEM)
    return pl.pallas_call(
        lambda *refs: attention_kernel(
            *refs, q_width=q_width, k_width=k_width, head_dim=head_dim, blocks=blocks
        ),
        out_shape=jax.ShapeDtypeStruct((rows, q_width), jnp.bfloat16),
        in_specs=[vmem, vmem, vmem],
        out_specs=vmem,
        cost_estimate=pl.CostEstimate(
            flops=heads * causal_pairs * pair_flops,
            transcendentals=heads * causal_pairs * (rows // blocks) ** 2,
            bytes_accessed=qkv_slot.size * 2 + rows * q_width * 2,
        ),
    )(qkv_slot, query_pos[:, None], key_pos[None, :])


def on_device(
    hidden, lengths, dealing, norm_gain, w_query, w_key, w_value, query_gain, key_gain, w_out
):
    devices = lax.axis_size("req")
    home_index = lax.axis_index("req")
    slice_index = lax.axis_index("tp")
    tok_rows, features = hidden.shape
    head_dim = query_gain.shape[0]
    out_width = w_out.shape[1]
    q_width = w_query.shape[1]
    k_width = w_key.shape[1]
    slot_len = 4 * tok_rows
    capacity = slot_len // devices
    prompt_total = lengths.shape[0]
    prompt_ids = jnp.arange(prompt_total, dtype=jnp.int32)
    prompt_ends = jnp.cumsum(lengths)
    starts = prompt_ends - lengths
    packed_ids = jnp.arange(tok_rows, dtype=jnp.int32) * devices + home_index
    segment = jnp.sum((packed_ids[:, None] >= prompt_ends[None, :]).astype(jnp.int32), axis=1)
    seg_onehot = (segment[:, None] == prompt_ids[None, :]).astype(jnp.int32)
    positions = packed_ids - jnp.sum(seg_onehot * starts[None, :], axis=1)
    picked = prepare(
        hidden,
        lengths,
        dealing,
        jnp.reshape(home_index, (1,)).astype(jnp.int32),
        norm_gain,
        w_query,
        w_key,
        w_value,
        query_gain,
        key_gain,
        positions,
        capacity,
    )
    picked, lengths, dealing, starts, seg_onehot = lax.optimization_barrier(
        (picked, lengths, dealing, starts, seg_onehot)
    )
    inverse = jnp.zeros((prompt_total,), jnp.int32).at[dealing].set(prompt_ids)
    deal_hot = (dealing[:, None] == prompt_ids[None, :]).astype(jnp.int32)
    dealt_starts = jnp.sum(deal_hot * starts[None, :], axis=1)
    dealt_lengths = jnp.sum(deal_hot * lengths[None, :], axis=1)
    ranks = jnp.arange(capacity, dtype=jnp.int32)
    my_start = lax.dynamic_index_in_dim(dealt_starts, home_index, 0, keepdims=False)
    my_length = lax.dynamic_index_in_dim(dealt_lengths, home_index, 0, keepdims=False)
    roll_shift = jnp.mod(my_start, devices)
    my_slots = jnp.sum(seg_onehot * inverse[None, :], axis=1)
    back_rows = my_slots * capacity + positions // devices
    arrived = lax.all_to_all(
        picked.reshape(devices, capacity, picked.shape[1]),
        "req",
        split_axis=0,
        concat_axis=0,
        tiled=True,
    ).transpose(1, 0, 2)
    source_ids = jnp.arange(devices, dtype=jnp.int32)
    arrived_pos = (
        ranks[:, None] * devices + jnp.mod(source_ids[None, :] - my_start, devices)
    ).reshape(-1)
    key_pos = jnp.where(arrived_pos < my_length, arrived_pos, 1 << 30)
    mixture = attend(
        arrived.reshape(slot_len, arrived.shape[2]), arrived_pos, key_pos, q_width, k_width, head_dim
    )
    returned = lax.all_to_all(
        mixture.reshape(capacity, devices, mixture.shape[1]).transpose(1, 0, 2),
        "req",
        split_axis=0,
        concat_axis=0,
        tiled=True,
    )
    attended = jnp.take(returned.reshape(capacity * devices, -1), back_rows, axis=0)
    kv_rows = jnp.roll(arrived[:, :, q_width:], -roll_shift, axis=1).reshape(slot_len, -1)
    kv_cache = jnp.stack([kv_rows[:, :k_width], kv_rows[:, k_width:]])[:, None]
    tp_size = lax.axis_size("tp")
    w_rows = w_out.shape[0] // tp_size
    summed = jnp.dot(
        attended,
        lax.dynamic_slice_in_dim(w_out, slice_index * w_rows, w_rows, 0),
        preferred_element_type=jnp.float32,
    )
    for shift in range(1, tp_size):
        passed = lax.ppermute(
            attended, "tp", perm=[(i, (i + shift) % tp_size) for i in range(tp_size)]
        )
        source = jnp.mod(slice_index - shift, tp_size)
        summed = summed + jnp.dot(
            passed,
            lax.dynamic_slice_in_dim(w_out, source * w_rows, w_rows, 0),
            preferred_element_type=jnp.float32,
        )
    branch = lax.optimization_barrier(summed.astype(jnp.bfloat16))
    residual = lax.dynamic_slice_in_dim(hidden, slice_index * out_width, out_width, 1)
    hidden_out = (residual.astype(jnp.float32) + branch.astype(jnp.float32)).astype(jnp.bfloat16)
    return (hidden_out, kv_cache)


def solution(mesh):
    in_specs = (
        P("req", None),
        P(),
        P(),
        P(),
        P(None, "tp"),
        P(None, "tp"),
        P(None, "tp"),
        P(),
        P(),
        P(None, "tp"),
    )
    out_specs = (P("req", "tp"), P(None, "req", None, "tp"))
    return jax.shard_map(
        on_device, mesh=mesh, in_specs=in_specs, out_specs=out_specs, check_vma=False
    )
```

```python
import jax
import jax.numpy as jnp
from jax import lax
from jax.experimental import pallas as pl
from jax.experimental.pallas import tpu as pltpu
from jax.sharding import PartitionSpec as P

EPS = 1e-06
THETA = 1000000.0


def rms_rows(values, scale_gain):
    inv_rms = lax.rsqrt(jnp.mean(values * values, axis=-1, keepdims=True) + EPS)
    return values * inv_rms * scale_gain


def rotate(values, positions):
    features = values.shape[-1]
    half_width = features // 2
    frequency = THETA ** (-(jnp.arange(half_width).astype(jnp.float32) * 2.0) / features)
    angles = positions.astype(jnp.float32)[:, None] * frequency[None, :]
    cosine = jnp.cos(angles)[:, None, :]
    sine_part = jnp.sin(angles)[:, None, :]
    first_half = values[..., :half_width]
    second_half = values[..., half_width:]
    return jnp.concatenate(
        [
            first_half * cosine - second_half * sine_part,
            second_half * cosine + first_half * sine_part,
        ],
        axis=-1,
    )


def project(normed, w_query, w_key, w_value, query_gain, key_gain, positions):
    head_dim = query_gain.shape[0]
    row_count = normed.shape[0]
    query_rows = jnp.dot(normed, w_query, preferred_element_type=jnp.float32).reshape(
        row_count, -1, head_dim
    )
    key_rows = jnp.dot(normed, w_key, preferred_element_type=jnp.float32).reshape(
        row_count, -1, head_dim
    )
    value_rows = jnp.dot(normed, w_value, preferred_element_type=jnp.float32).astype(jnp.bfloat16)
    query_rows = rotate(rms_rows(query_rows, query_gain.astype(jnp.float32)), positions).astype(
        jnp.bfloat16
    )
    key_rows = rotate(rms_rows(key_rows, key_gain.astype(jnp.float32)), positions).astype(
        jnp.bfloat16
    )
    return (query_rows.reshape(row_count, -1), key_rows.reshape(row_count, -1), value_rows)


def prep_kernel(
    lengths_ref,
    dealing_ref,
    home_ref,
    hidden_ref,
    norm_gain_ref,
    wq_ref,
    wk_ref,
    wv_ref,
    qgain_ref,
    kgain_ref,
    cos_ref,
    sin_ref,
    out_ref,
    qkv_ref,
    pick_ref,
    starts_ref,
    *,
    head_dim,
    capacity,
):
    devices = dealing_ref.shape[0]
    prompt_total = lengths_ref.shape[0]
    tok_rows = qkv_ref.shape[0]

    def running(p, total):
        starts_ref[p] = total
        return total + lengths_ref[p]

    lax.fori_loop(0, prompt_total, running, jnp.int32(0))
    home = home_ref[0]
    rank_ids = lax.broadcasted_iota(jnp.int32, (capacity, tok_rows), 0)
    row_gap = lax.broadcasted_iota(jnp.int32, (capacity, tok_rows), 1) - rank_ids

    def pick_rows(d, carry):
        prompt = dealing_ref[d]
        start = starts_ref[prompt]
        length = lengths_ref[prompt]
        first = lax.rem(lax.rem(home - start, devices) + devices, devices)
        first_row = lax.div(start + first - home, devices)
        count = jnp.minimum(lax.div(length - first + devices - 1, devices), capacity)
        hits = (row_gap == first_row) & (rank_ids < count)
        pick_ref[pl.ds(pl.multiple_of(d * capacity, capacity), capacity), :] = hits.astype(
            pick_ref.dtype
        )
        return carry

    lax.fori_loop(0, devices, pick_rows, 0)
    values = hidden_ref[...].astype(jnp.float32)
    inv_rms = lax.rsqrt(jnp.mean(values * values, axis=-1, keepdims=True) + EPS)
    normed = (values * inv_rms * norm_gain_ref[...].astype(jnp.float32)[None, :]).astype(
        jnp.bfloat16
    )
    cosine = cos_ref[...]
    sine = sin_ref[...]
    column = 0
    for w_ref, gain_ref in ((wq_ref, qgain_ref), (wk_ref, kgain_ref)):
        rows = jnp.dot(normed, w_ref[...], preferred_element_type=jnp.float32)
        gain = gain_ref[...].astype(jnp.float32)
        for h in range(rows.shape[1] // head_dim):
            head = rows[:, h * head_dim : (h + 1) * head_dim]
            head_inv = lax.rsqrt(jnp.mean(head * head, axis=-1, keepdims=True) + EPS)
            head = head * head_inv * gain
            swapped = pltpu.roll(head, head_dim // 2, 1)
            qkv_ref[:, column : column + head_dim] = (head * cosine + swapped * sine).astype(
                jnp.bfloat16
            )
            column += head_dim
    v_width = wv_ref.shape[1]
    qkv_ref[:, column : column + v_width] = jnp.dot(
        normed, wv_ref[...], preferred_element_type=jnp.float32
    ).astype(jnp.bfloat16)
    qkv = qkv_ref[...]
    out_rows = out_ref.shape[0]
    block = out_rows // 4
    for b in range(4):
        rows_here = pl.ds(b * block, block)
        out_ref[rows_here, :] = jnp.dot(
            pick_ref[rows_here, :], qkv, preferred_element_type=jnp.float32
        ).astype(out_ref.dtype)


def prepare(
    hidden, lengths, dealing, home, norm_gain, w_query, w_key, w_value, query_gain, key_gain,
    positions, capacity,
):
    tok_rows, features = hidden.shape
    head_dim = query_gain.shape[0]
    half_width = head_dim // 2
    width = w_query.shape[1] + w_key.shape[1] + w_value.shape[1]
    devices = dealing.shape[0]
    out_rows = devices * capacity
    frequency = THETA ** (-(jnp.arange(half_width).astype(jnp.float32) * 2.0) / head_dim)
    frequency = jnp.concatenate([frequency, frequency])
    angles = positions.astype(jnp.float32)[:, None] * frequency[None, :]
    sign = jnp.where(jnp.arange(head_dim) < half_width, -1.0, 1.0).astype(jnp.float32)
    cos_full = jnp.cos(angles)
    sin_signed = jnp.sin(angles) * sign[None, :]
    vmem = pl.BlockSpec(memory_space=pltpu.VMEM)
    smem = pl.BlockSpec(memory_space=pltpu.SMEM)
    return pl.pallas_call(
        lambda *refs: prep_kernel(*refs, head_dim=head_dim, capacity=capacity),
        out_shape=jax.ShapeDtypeStruct((out_rows, width), jnp.bfloat16),
        in_specs=[smem] * 3 + [vmem] * 9,
        out_specs=vmem,
        scratch_shapes=[
            pltpu.VMEM((tok_rows, width), jnp.bfloat16),
            pltpu.VMEM((out_rows, tok_rows), jnp.bfloat16),
            pltpu.SMEM((lengths.shape[0],), jnp.int32),
        ],
        cost_estimate=pl.CostEstimate(
            flops=2 * tok_rows * features * width + 2 * out_rows * tok_rows * width,
            transcendentals=tok_rows * 8,
            bytes_accessed=hidden.size * 2 + features * width * 2 + out_rows * width * 2,
        ),
    )(
        lengths,
        dealing,
        home,
        hidden,
        norm_gain,
        w_query,
        w_key,
        w_value,
        query_gain[None, :],
        key_gain[None, :],
        cos_full,
        sin_signed,
    )


def attention_kernel(qkv_ref, qpos_ref, kpos_ref, out_ref, *, q_width, k_width, head_dim, blocks):
    rows = qkv_ref.shape[0]
    block = rows // blocks
    kv_heads = k_width // head_dim
    group = q_width // head_dim // kv_heads
    scale = head_dim ** (-0.5)
    for i in range(blocks):
        key_rows = block * (i + 1)
        rows_here = pl.ds(i * block, block)
        allowed = kpos_ref[:, :key_rows] <= qpos_ref[rows_here, :]
        for h in range(kv_heads):
            k_col = q_width + h * head_dim
            v_col = q_width + k_width + h * head_dim
            keys = qkv_ref[:key_rows, k_col : k_col + head_dim]
            values = qkv_ref[:key_rows, v_col : v_col + head_dim]
            q_cols = [(h * group + g) * head_dim for g in range(group)]
            queries = jnp.concatenate(
                [qkv_ref[rows_here, c : c + head_dim] for c in q_cols], axis=0
            )
            scores = lax.dot_general(
                queries,
                keys,
                (((1,), (1,)), ((), ())),
                preferred_element_type=jnp.float32,
            ) * scale
            scores = jnp.where(jnp.concatenate([allowed] * group, axis=0), scores, -jnp.inf)
            row_max = jnp.max(scores, axis=-1, keepdims=True)
            weights = jnp.exp(scores - row_max)
            weights = (weights / jnp.sum(weights, axis=-1, keepdims=True)).astype(jnp.bfloat16)
            mixed = jnp.dot(weights, values, preferred_element_type=jnp.float32)
            for g, c in enumerate(q_cols):
                out_ref[rows_here, c : c + head_dim] = mixed[g * block : (g + 1) * block].astype(
                    out_ref.dtype
                )


def attend(qkv_slot, query_pos, key_pos, q_width, k_width, head_dim):
    rows = qkv_slot.shape[0]
    blocks = 2
    heads = q_width // head_dim
    causal_pairs = blocks * (blocks + 1) // 2
    pair_flops = 4 * (rows // blocks) ** 2 * head_dim
    vmem = pl.BlockSpec(memory_space=pltpu.VMEM)
    return pl.pallas_call(
        lambda *refs: attention_kernel(
            *refs, q_width=q_width, k_width=k_width, head_dim=head_dim, blocks=blocks
        ),
        out_shape=jax.ShapeDtypeStruct((rows, q_width), jnp.bfloat16),
        in_specs=[vmem, vmem, vmem],
        out_specs=vmem,
        cost_estimate=pl.CostEstimate(
            flops=heads * causal_pairs * pair_flops,
            transcendentals=heads * causal_pairs * (rows // blocks) ** 2,
            bytes_accessed=qkv_slot.size * 2 + rows * q_width * 2,
        ),
    )(qkv_slot, query_pos[:, None], key_pos[None, :])


def on_device(
    hidden, lengths, dealing, norm_gain, w_query, w_key, w_value, query_gain, key_gain, w_out
):
    devices = lax.axis_size("req")
    home_index = lax.axis_index("req")
    slice_index = lax.axis_index("tp")
    tok_rows, features = hidden.shape
    head_dim = query_gain.shape[0]
    out_width = w_out.shape[1]
    q_width = w_query.shape[1]
    k_width = w_key.shape[1]
    slot_len = 4 * tok_rows
    capacity = slot_len // devices
    prompt_total = lengths.shape[0]
    prompt_ids = jnp.arange(prompt_total, dtype=jnp.int32)
    prompt_ends = jnp.cumsum(lengths)
    starts = prompt_ends - lengths
    packed_ids = jnp.arange(tok_rows, dtype=jnp.int32) * devices + home_index
    segment = jnp.sum((packed_ids[:, None] >= prompt_ends[None, :]).astype(jnp.int32), axis=1)
    seg_onehot = (segment[:, None] == prompt_ids[None, :]).astype(jnp.int32)
    positions = packed_ids - jnp.sum(seg_onehot * starts[None, :], axis=1)
    picked = prepare(
        hidden,
        lengths,
        dealing,
        jnp.reshape(home_index, (1,)).astype(jnp.int32),
        norm_gain,
        w_query,
        w_key,
        w_value,
        query_gain,
        key_gain,
        positions,
        capacity,
    )
    picked, lengths, dealing, starts, seg_onehot = lax.optimization_barrier(
        (picked, lengths, dealing, starts, seg_onehot)
    )
    inverse = jnp.zeros((prompt_total,), jnp.int32).at[dealing].set(prompt_ids)
    deal_hot = (dealing[:, None] == prompt_ids[None, :]).astype(jnp.int32)
    dealt_starts = jnp.sum(deal_hot * starts[None, :], axis=1)
    dealt_lengths = jnp.sum(deal_hot * lengths[None, :], axis=1)
    ranks = jnp.arange(capacity, dtype=jnp.int32)
    my_start = lax.dynamic_index_in_dim(dealt_starts, home_index, 0, keepdims=False)
    my_length = lax.dynamic_index_in_dim(dealt_lengths, home_index, 0, keepdims=False)
    roll_shift = jnp.mod(my_start, devices)
    my_slots = jnp.sum(seg_onehot * inverse[None, :], axis=1)
    back_rows = my_slots * capacity + positions // devices
    arrived = lax.all_to_all(
        picked.reshape(devices, capacity, picked.shape[1]),
        "req",
        split_axis=0,
        concat_axis=0,
        tiled=True,
    ).transpose(1, 0, 2)
    source_ids = jnp.arange(devices, dtype=jnp.int32)
    arrived_pos = (
        ranks[:, None] * devices + jnp.mod(source_ids[None, :] - my_start, devices)
    ).reshape(-1)
    key_pos = jnp.where(arrived_pos < my_length, arrived_pos, 1 << 30)
    mixture = attend(
        arrived.reshape(slot_len, arrived.shape[2]), arrived_pos, key_pos, q_width, k_width, head_dim
    )
    returned = lax.all_to_all(
        mixture.reshape(capacity, devices, mixture.shape[1]).transpose(1, 0, 2),
        "req",
        split_axis=0,
        concat_axis=0,
        tiled=True,
    )
    attended = jnp.take(returned.reshape(capacity * devices, -1), back_rows, axis=0)
    kv_rows = jnp.roll(arrived[:, :, q_width:], -roll_shift, axis=1).reshape(slot_len, -1)
    kv_cache = jnp.stack([kv_rows[:, :k_width], kv_rows[:, k_width:]])[:, None]
    tp_size = lax.axis_size("tp")
    w_rows = w_out.shape[0] // tp_size
    summed = jnp.dot(
        attended,
        lax.dynamic_slice_in_dim(w_out, slice_index * w_rows, w_rows, 0),
        preferred_element_type=jnp.float32,
    )
    for shift in range(1, tp_size):
        passed = lax.ppermute(
            attended, "tp", perm=[(i, (i + shift) % tp_size) for i in range(tp_size)]
        )
        source = jnp.mod(slice_index - shift, tp_size)
        summed = summed + jnp.dot(
            passed,
            lax.dynamic_slice_in_dim(w_out, source * w_rows, w_rows, 0),
            preferred_element_type=jnp.float32,
        )
    branch = lax.optimization_barrier(summed.astype(jnp.bfloat16))
    residual = lax.dynamic_slice_in_dim(hidden, slice_index * out_width, out_width, 1)
    hidden_out = (residual.astype(jnp.float32) + branch.astype(jnp.float32)).astype(jnp.bfloat16)
    return (hidden_out, kv_cache)


def solution(mesh):
    in_specs = (
        P("req", None),
        P(),
        P(),
        P(),
        P(None, "tp"),
        P(None, "tp"),
        P(None, "tp"),
        P(),
        P(),
        P(None, "tp"),
    )
    out_specs = (P("req", "tp"), P(None, "req", None, "tp"))
    return jax.shard_map(
        on_device, mesh=mesh, in_specs=in_specs, out_specs=out_specs, check_vma=False
    )
```

```python
import jax
import jax.numpy as jnp
from jax import lax
from jax.experimental import pallas as pl
from jax.experimental.pallas import tpu as pltpu
from jax.sharding import PartitionSpec as P

EPS = 1e-06
THETA = 1000000.0


def rms_rows(values, scale_gain):
    inv_rms = lax.rsqrt(jnp.mean(values * values, axis=-1, keepdims=True) + EPS)
    return values * inv_rms * scale_gain


def rotate(values, positions):
    features = values.shape[-1]
    half_width = features // 2
    frequency = THETA ** (-(jnp.arange(half_width).astype(jnp.float32) * 2.0) / features)
    angles = positions.astype(jnp.float32)[:, None] * frequency[None, :]
    cosine = jnp.cos(angles)[:, None, :]
    sine_part = jnp.sin(angles)[:, None, :]
    first_half = values[..., :half_width]
    second_half = values[..., half_width:]
    return jnp.concatenate(
        [
            first_half * cosine - second_half * sine_part,
            second_half * cosine + first_half * sine_part,
        ],
        axis=-1,
    )


def project(normed, w_query, w_key, w_value, query_gain, key_gain, positions):
    head_dim = query_gain.shape[0]
    row_count = normed.shape[0]
    query_rows = jnp.dot(normed, w_query, preferred_element_type=jnp.float32).reshape(
        row_count, -1, head_dim
    )
    key_rows = jnp.dot(normed, w_key, preferred_element_type=jnp.float32).reshape(
        row_count, -1, head_dim
    )
    value_rows = jnp.dot(normed, w_value, preferred_element_type=jnp.float32).astype(jnp.bfloat16)
    query_rows = rotate(rms_rows(query_rows, query_gain.astype(jnp.float32)), positions).astype(
        jnp.bfloat16
    )
    key_rows = rotate(rms_rows(key_rows, key_gain.astype(jnp.float32)), positions).astype(
        jnp.bfloat16
    )
    return (query_rows.reshape(row_count, -1), key_rows.reshape(row_count, -1), value_rows)


def prep_kernel(
    lengths_ref,
    dealing_ref,
    home_ref,
    hidden_ref,
    norm_gain_ref,
    wq_ref,
    wk_ref,
    wv_ref,
    qgain_ref,
    kgain_ref,
    cos_ref,
    sin_ref,
    out_ref,
    qkv_ref,
    pick_ref,
    starts_ref,
    *,
    head_dim,
    capacity,
):
    devices = dealing_ref.shape[0]
    prompt_total = lengths_ref.shape[0]
    tok_rows = qkv_ref.shape[0]

    def running(p, total):
        starts_ref[p] = total
        return total + lengths_ref[p]

    lax.fori_loop(0, prompt_total, running, jnp.int32(0))
    home = home_ref[0]
    rank_ids = lax.broadcasted_iota(jnp.int32, (capacity, tok_rows), 0)
    row_gap = lax.broadcasted_iota(jnp.int32, (capacity, tok_rows), 1) - rank_ids

    def pick_rows(d, carry):
        prompt = dealing_ref[d]
        start = starts_ref[prompt]
        length = lengths_ref[prompt]
        first = lax.rem(lax.rem(home - start, devices) + devices, devices)
        first_row = lax.div(start + first - home, devices)
        count = jnp.minimum(lax.div(length - first + devices - 1, devices), capacity)
        hits = (row_gap == first_row) & (rank_ids < count)
        pick_ref[pl.ds(pl.multiple_of(d * capacity, capacity), capacity), :] = hits.astype(
            pick_ref.dtype
        )
        return carry

    lax.fori_loop(0, devices, pick_rows, 0)
    values = hidden_ref[...].astype(jnp.float32)
    inv_rms = lax.rsqrt(jnp.mean(values * values, axis=-1, keepdims=True) + EPS)
    normed = (values * inv_rms * norm_gain_ref[...].astype(jnp.float32)[None, :]).astype(
        jnp.bfloat16
    )
    cosine = cos_ref[...]
    sine = sin_ref[...]
    column = 0
    for w_ref, gain_ref in ((wq_ref, qgain_ref), (wk_ref, kgain_ref)):
        rows = jnp.dot(normed, w_ref[...], preferred_element_type=jnp.float32)
        gain = gain_ref[...].astype(jnp.float32)
        for h in range(rows.shape[1] // head_dim):
            head = rows[:, h * head_dim : (h + 1) * head_dim]
            head_inv = lax.rsqrt(jnp.mean(head * head, axis=-1, keepdims=True) + EPS)
            head = head * head_inv * gain
            swapped = pltpu.roll(head, head_dim // 2, 1)
            qkv_ref[:, column : column + head_dim] = (head * cosine + swapped * sine).astype(
                jnp.bfloat16
            )
            column += head_dim
    v_width = wv_ref.shape[1]
    qkv_ref[:, column : column + v_width] = jnp.dot(
        normed, wv_ref[...], preferred_element_type=jnp.float32
    ).astype(jnp.bfloat16)
    qkv = qkv_ref[...]
    out_rows = out_ref.shape[0]
    block = out_rows // 2
    for b in range(2):
        rows_here = pl.ds(b * block, block)
        out_ref[rows_here, :] = jnp.dot(
            pick_ref[rows_here, :], qkv, preferred_element_type=jnp.float32
        ).astype(out_ref.dtype)


def prepare(
    hidden, lengths, dealing, home, norm_gain, w_query, w_key, w_value, query_gain, key_gain,
    positions, capacity,
):
    tok_rows, features = hidden.shape
    head_dim = query_gain.shape[0]
    half_width = head_dim // 2
    width = w_query.shape[1] + w_key.shape[1] + w_value.shape[1]
    devices = dealing.shape[0]
    out_rows = devices * capacity
    frequency = THETA ** (-(jnp.arange(half_width).astype(jnp.float32) * 2.0) / head_dim)
    frequency = jnp.concatenate([frequency, frequency])
    angles = positions.astype(jnp.float32)[:, None] * frequency[None, :]
    sign = jnp.where(jnp.arange(head_dim) < half_width, -1.0, 1.0).astype(jnp.float32)
    cos_full = jnp.cos(angles)
    sin_signed = jnp.sin(angles) * sign[None, :]
    vmem = pl.BlockSpec(memory_space=pltpu.VMEM)
    smem = pl.BlockSpec(memory_space=pltpu.SMEM)
    return pl.pallas_call(
        lambda *refs: prep_kernel(*refs, head_dim=head_dim, capacity=capacity),
        out_shape=jax.ShapeDtypeStruct((out_rows, width), jnp.bfloat16),
        in_specs=[smem] * 3 + [vmem] * 9,
        out_specs=vmem,
        scratch_shapes=[
            pltpu.VMEM((tok_rows, width), jnp.bfloat16),
            pltpu.VMEM((out_rows, tok_rows), jnp.bfloat16),
            pltpu.SMEM((lengths.shape[0],), jnp.int32),
        ],
        cost_estimate=pl.CostEstimate(
            flops=2 * tok_rows * features * width + 2 * out_rows * tok_rows * width,
            transcendentals=tok_rows * 8,
            bytes_accessed=hidden.size * 2 + features * width * 2 + out_rows * width * 2,
        ),
    )(
        lengths,
        dealing,
        home,
        hidden,
        norm_gain,
        w_query,
        w_key,
        w_value,
        query_gain[None, :],
        key_gain[None, :],
        cos_full,
        sin_signed,
    )


def attention_kernel(qkv_ref, qpos_ref, kpos_ref, out_ref, *, q_width, k_width, head_dim, blocks):
    rows = qkv_ref.shape[0]
    block = rows // blocks
    kv_heads = k_width // head_dim
    group = q_width // head_dim // kv_heads
    scale = head_dim ** (-0.5)
    for i in range(blocks):
        key_rows = block * (i + 1)
        rows_here = pl.ds(i * block, block)
        allowed = kpos_ref[:, :key_rows] <= qpos_ref[rows_here, :]
        for h in range(kv_heads):
            k_col = q_width + h * head_dim
            v_col = q_width + k_width + h * head_dim
            keys = qkv_ref[:key_rows, k_col : k_col + head_dim]
            values = qkv_ref[:key_rows, v_col : v_col + head_dim]
            for g in range(group):
                q_col = (h * group + g) * head_dim
                queries = qkv_ref[rows_here, q_col : q_col + head_dim]
                scores = lax.dot_general(
                    queries,
                    keys,
                    (((1,), (1,)), ((), ())),
                    preferred_element_type=jnp.float32,
                ) * scale
                scores = jnp.where(allowed, scores, -jnp.inf)
                row_max = jnp.max(scores, axis=-1, keepdims=True)
                weights = jnp.exp(scores - row_max)
                weights = (weights / jnp.sum(weights, axis=-1, keepdims=True)).astype(jnp.bfloat16)
                mixed = jnp.dot(weights, values, preferred_element_type=jnp.float32)
                out_ref[rows_here, q_col : q_col + head_dim] = mixed.astype(out_ref.dtype)


def attend(qkv_slot, query_pos, key_pos, q_width, k_width, head_dim):
    rows = qkv_slot.shape[0]
    blocks = 2
    heads = q_width // head_dim
    causal_pairs = blocks * (blocks + 1) // 2
    pair_flops = 4 * (rows // blocks) ** 2 * head_dim
    vmem = pl.BlockSpec(memory_space=pltpu.VMEM)
    return pl.pallas_call(
        lambda *refs: attention_kernel(
            *refs, q_width=q_width, k_width=k_width, head_dim=head_dim, blocks=blocks
        ),
        out_shape=jax.ShapeDtypeStruct((rows, q_width), jnp.bfloat16),
        in_specs=[vmem, vmem, vmem],
        out_specs=vmem,
        cost_estimate=pl.CostEstimate(
            flops=heads * causal_pairs * pair_flops,
            transcendentals=heads * causal_pairs * (rows // blocks) ** 2,
            bytes_accessed=qkv_slot.size * 2 + rows * q_width * 2,
        ),
    )(qkv_slot, query_pos[:, None], key_pos[None, :])


def on_device(
    hidden, lengths, dealing, norm_gain, w_query, w_key, w_value, query_gain, key_gain, w_out
):
    devices = lax.axis_size("req")
    home_index = lax.axis_index("req")
    slice_index = lax.axis_index("tp")
    tok_rows, features = hidden.shape
    head_dim = query_gain.shape[0]
    out_width = w_out.shape[1]
    q_width = w_query.shape[1]
    k_width = w_key.shape[1]
    slot_len = 4 * tok_rows
    capacity = slot_len // devices
    prompt_total = lengths.shape[0]
    prompt_ids = jnp.arange(prompt_total, dtype=jnp.int32)
    prompt_ends = jnp.cumsum(lengths)
    starts = prompt_ends - lengths
    packed_ids = jnp.arange(tok_rows, dtype=jnp.int32) * devices + home_index
    segment = jnp.sum((packed_ids[:, None] >= prompt_ends[None, :]).astype(jnp.int32), axis=1)
    seg_onehot = (segment[:, None] == prompt_ids[None, :]).astype(jnp.int32)
    positions = packed_ids - jnp.sum(seg_onehot * starts[None, :], axis=1)
    picked = prepare(
        hidden,
        lengths,
        dealing,
        jnp.reshape(home_index, (1,)).astype(jnp.int32),
        norm_gain,
        w_query,
        w_key,
        w_value,
        query_gain,
        key_gain,
        positions,
        capacity,
    )
    picked, lengths, dealing, starts, seg_onehot = lax.optimization_barrier(
        (picked, lengths, dealing, starts, seg_onehot)
    )
    inverse = jnp.zeros((prompt_total,), jnp.int32).at[dealing].set(prompt_ids)
    deal_hot = (dealing[:, None] == prompt_ids[None, :]).astype(jnp.int32)
    dealt_starts = jnp.sum(deal_hot * starts[None, :], axis=1)
    dealt_lengths = jnp.sum(deal_hot * lengths[None, :], axis=1)
    ranks = jnp.arange(capacity, dtype=jnp.int32)
    my_start = lax.dynamic_index_in_dim(dealt_starts, home_index, 0, keepdims=False)
    my_length = lax.dynamic_index_in_dim(dealt_lengths, home_index, 0, keepdims=False)
    roll_shift = jnp.mod(my_start, devices)
    my_slots = jnp.sum(seg_onehot * inverse[None, :], axis=1)
    back_rows = my_slots * capacity + positions // devices
    arrived = lax.all_to_all(
        picked.reshape(devices, capacity, picked.shape[1]),
        "req",
        split_axis=0,
        concat_axis=0,
        tiled=True,
    ).transpose(1, 0, 2)
    source_ids = jnp.arange(devices, dtype=jnp.int32)
    arrived_pos = (
        ranks[:, None] * devices + jnp.mod(source_ids[None, :] - my_start, devices)
    ).reshape(-1)
    key_pos = jnp.where(arrived_pos < my_length, arrived_pos, 1 << 30)
    mixture = attend(
        arrived.reshape(slot_len, arrived.shape[2]), arrived_pos, key_pos, q_width, k_width, head_dim
    )
    returned = lax.all_to_all(
        mixture.reshape(capacity, devices, mixture.shape[1]).transpose(1, 0, 2),
        "req",
        split_axis=0,
        concat_axis=0,
        tiled=True,
    )
    attended = jnp.take(returned.reshape(capacity * devices, -1), back_rows, axis=0)
    kv_rows = jnp.roll(arrived[:, :, q_width:], -roll_shift, axis=1).reshape(slot_len, -1)
    kv_cache = jnp.stack([kv_rows[:, :k_width], kv_rows[:, k_width:]])[:, None]
    tp_size = lax.axis_size("tp")
    w_rows = w_out.shape[0] // tp_size
    summed = jnp.dot(
        attended,
        lax.dynamic_slice_in_dim(w_out, slice_index * w_rows, w_rows, 0),
        preferred_element_type=jnp.float32,
    )
    for shift in range(1, tp_size):
        passed = lax.ppermute(
            attended, "tp", perm=[(i, (i + shift) % tp_size) for i in range(tp_size)]
        )
        source = jnp.mod(slice_index - shift, tp_size)
        summed = summed + jnp.dot(
            passed,
            lax.dynamic_slice_in_dim(w_out, source * w_rows, w_rows, 0),
            preferred_element_type=jnp.float32,
        )
    branch = lax.optimization_barrier(summed.astype(jnp.bfloat16))
    residual = lax.dynamic_slice_in_dim(hidden, slice_index * out_width, out_width, 1)
    hidden_out = (residual.astype(jnp.float32) + branch.astype(jnp.float32)).astype(jnp.bfloat16)
    return (hidden_out, kv_cache)


def solution(mesh):
    in_specs = (
        P("req", None),
        P(),
        P(),
        P(),
        P(None, "tp"),
        P(None, "tp"),
        P(None, "tp"),
        P(),
        P(),
        P(None, "tp"),
    )
    out_specs = (P("req", "tp"), P(None, "req", None, "tp"))
    return jax.shard_map(
        on_device, mesh=mesh, in_specs=in_specs, out_specs=out_specs, check_vma=False
    )
```

```python
import jax
import jax.numpy as jnp
from jax import lax
from jax.experimental import pallas as pl
from jax.experimental.pallas import tpu as pltpu
from jax.sharding import PartitionSpec as P

EPS = 1e-06
THETA = 1000000.0


def rms_rows(values, scale_gain):
    inv_rms = lax.rsqrt(jnp.mean(values * values, axis=-1, keepdims=True) + EPS)
    return values * inv_rms * scale_gain


def rotate(values, positions):
    features = values.shape[-1]
    half_width = features // 2
    frequency = THETA ** (-(jnp.arange(half_width).astype(jnp.float32) * 2.0) / features)
    angles = positions.astype(jnp.float32)[:, None] * frequency[None, :]
    cosine = jnp.cos(angles)[:, None, :]
    sine_part = jnp.sin(angles)[:, None, :]
    first_half = values[..., :half_width]
    second_half = values[..., half_width:]
    return jnp.concatenate(
        [
            first_half * cosine - second_half * sine_part,
            second_half * cosine + first_half * sine_part,
        ],
        axis=-1,
    )


def project(normed, w_query, w_key, w_value, query_gain, key_gain, positions):
    head_dim = query_gain.shape[0]
    row_count = normed.shape[0]
    query_rows = jnp.dot(normed, w_query, preferred_element_type=jnp.float32).reshape(
        row_count, -1, head_dim
    )
    key_rows = jnp.dot(normed, w_key, preferred_element_type=jnp.float32).reshape(
        row_count, -1, head_dim
    )
    value_rows = jnp.dot(normed, w_value, preferred_element_type=jnp.float32).astype(jnp.bfloat16)
    query_rows = rotate(rms_rows(query_rows, query_gain.astype(jnp.float32)), positions).astype(
        jnp.bfloat16
    )
    key_rows = rotate(rms_rows(key_rows, key_gain.astype(jnp.float32)), positions).astype(
        jnp.bfloat16
    )
    return (query_rows.reshape(row_count, -1), key_rows.reshape(row_count, -1), value_rows)


def prep_kernel(
    lengths_ref,
    dealing_ref,
    home_ref,
    hidden_ref,
    norm_gain_ref,
    wq_ref,
    wk_ref,
    wv_ref,
    qgain_ref,
    kgain_ref,
    cos_ref,
    sin_ref,
    out_ref,
    qkv_ref,
    pick_ref,
    starts_ref,
    *,
    head_dim,
    capacity,
):
    devices = dealing_ref.shape[0]
    prompt_total = lengths_ref.shape[0]
    tok_rows = qkv_ref.shape[0]

    def running(p, total):
        starts_ref[p] = total
        return total + lengths_ref[p]

    lax.fori_loop(0, prompt_total, running, jnp.int32(0))
    home = home_ref[0]
    rank_ids = lax.broadcasted_iota(jnp.int32, (capacity, tok_rows), 0)
    row_gap = lax.broadcasted_iota(jnp.int32, (capacity, tok_rows), 1) - rank_ids

    def pick_rows(d, carry):
        prompt = dealing_ref[d]
        start = starts_ref[prompt]
        length = lengths_ref[prompt]
        first = lax.rem(lax.rem(home - start, devices) + devices, devices)
        first_row = lax.div(start + first - home, devices)
        count = jnp.minimum(lax.div(length - first + devices - 1, devices), capacity)
        hits = (row_gap == first_row) & (rank_ids < count)
        pick_ref[pl.ds(pl.multiple_of(d * capacity, capacity), capacity), :] = hits.astype(
            pick_ref.dtype
        )
        return carry

    lax.fori_loop(0, devices, pick_rows, 0)
    values = hidden_ref[...].astype(jnp.float32)
    inv_rms = lax.rsqrt(jnp.mean(values * values, axis=-1, keepdims=True) + EPS)
    normed = (values * inv_rms * norm_gain_ref[...].astype(jnp.float32)[None, :]).astype(
        jnp.bfloat16
    )
    cosine = cos_ref[...]
    sine = sin_ref[...]
    column = 0
    for w_ref, gain_ref in ((wq_ref, qgain_ref), (wk_ref, kgain_ref)):
        rows = jnp.dot(normed, w_ref[...], preferred_element_type=jnp.float32)
        gain = gain_ref[...].astype(jnp.float32)
        for h in range(rows.shape[1] // head_dim):
            head = rows[:, h * head_dim : (h + 1) * head_dim]
            head_inv = lax.rsqrt(jnp.mean(head * head, axis=-1, keepdims=True) + EPS)
            head = head * head_inv * gain
            swapped = pltpu.roll(head, head_dim // 2, 1)
            qkv_ref[:, column : column + head_dim] = (head * cosine + swapped * sine).astype(
                jnp.bfloat16
            )
            column += head_dim
    v_width = wv_ref.shape[1]
    qkv_ref[:, column : column + v_width] = jnp.dot(
        normed, wv_ref[...], preferred_element_type=jnp.float32
    ).astype(jnp.bfloat16)
    qkv = qkv_ref[...]
    out_rows = out_ref.shape[0]
    block = out_rows // 4
    for b in range(4):
        rows_here = pl.ds(b * block, block)
        out_ref[rows_here, :] = jnp.dot(
            pick_ref[rows_here, :], qkv, preferred_element_type=jnp.float32
        ).astype(out_ref.dtype)


def prepare(
    hidden, lengths, dealing, home, norm_gain, w_query, w_key, w_value, query_gain, key_gain,
    positions, capacity,
):
    tok_rows, features = hidden.shape
    head_dim = query_gain.shape[0]
    half_width = head_dim // 2
    width = w_query.shape[1] + w_key.shape[1] + w_value.shape[1]
    devices = dealing.shape[0]
    out_rows = devices * capacity
    frequency = THETA ** (-(jnp.arange(half_width).astype(jnp.float32) * 2.0) / head_dim)
    frequency = jnp.concatenate([frequency, frequency])
    angles = positions.astype(jnp.float32)[:, None] * frequency[None, :]
    sign = jnp.where(jnp.arange(head_dim) < half_width, -1.0, 1.0).astype(jnp.float32)
    cos_full = jnp.cos(angles)
    sin_signed = jnp.sin(angles) * sign[None, :]
    vmem = pl.BlockSpec(memory_space=pltpu.VMEM)
    smem = pl.BlockSpec(memory_space=pltpu.SMEM)
    return pl.pallas_call(
        lambda *refs: prep_kernel(*refs, head_dim=head_dim, capacity=capacity),
        out_shape=jax.ShapeDtypeStruct((out_rows, width), jnp.bfloat16),
        in_specs=[smem] * 3 + [vmem] * 9,
        out_specs=vmem,
        scratch_shapes=[
            pltpu.VMEM((tok_rows, width), jnp.bfloat16),
            pltpu.VMEM((out_rows, tok_rows), jnp.bfloat16),
            pltpu.SMEM((lengths.shape[0],), jnp.int32),
        ],
        cost_estimate=pl.CostEstimate(
            flops=2 * tok_rows * features * width + 2 * out_rows * tok_rows * width,
            transcendentals=tok_rows * 8,
            bytes_accessed=hidden.size * 2 + features * width * 2 + out_rows * width * 2,
        ),
    )(
        lengths,
        dealing,
        home,
        hidden,
        norm_gain,
        w_query,
        w_key,
        w_value,
        query_gain[None, :],
        key_gain[None, :],
        cos_full,
        sin_signed,
    )


def attention_kernel(qkv_ref, qpos_ref, kpos_ref, out_ref, *, q_width, k_width, head_dim, blocks):
    rows = qkv_ref.shape[0]
    block = rows // blocks
    kv_heads = k_width // head_dim
    group = q_width // head_dim // kv_heads
    scale = head_dim ** (-0.5)
    for i in range(blocks):
        key_rows = block * (i + 1)
        rows_here = pl.ds(i * block, block)
        allowed = kpos_ref[:, :key_rows] <= qpos_ref[rows_here, :]
        for h in range(kv_heads):
            k_col = q_width + h * head_dim
            v_col = q_width + k_width + h * head_dim
            keys = qkv_ref[:key_rows, k_col : k_col + head_dim]
            values = qkv_ref[:key_rows, v_col : v_col + head_dim]
            for g in range(group):
                q_col = (h * group + g) * head_dim
                queries = qkv_ref[rows_here, q_col : q_col + head_dim]
                scores = lax.dot_general(
                    queries,
                    keys,
                    (((1,), (1,)), ((), ())),
                    preferred_element_type=jnp.float32,
                ) * scale
                scores = jnp.where(allowed, scores, -jnp.inf)
                row_max = jnp.max(scores, axis=-1, keepdims=True)
                weights = jnp.exp(scores - row_max)
                weights = (weights / jnp.sum(weights, axis=-1, keepdims=True)).astype(jnp.bfloat16)
                mixed = jnp.dot(weights, values, preferred_element_type=jnp.float32)
                out_ref[rows_here, q_col : q_col + head_dim] = mixed.astype(out_ref.dtype)


def attend(qkv_slot, query_pos, key_pos, q_width, k_width, head_dim):
    rows = qkv_slot.shape[0]
    blocks = 1
    heads = q_width // head_dim
    causal_pairs = blocks * (blocks + 1) // 2
    pair_flops = 4 * (rows // blocks) ** 2 * head_dim
    vmem = pl.BlockSpec(memory_space=pltpu.VMEM)
    return pl.pallas_call(
        lambda *refs: attention_kernel(
            *refs, q_width=q_width, k_width=k_width, head_dim=head_dim, blocks=blocks
        ),
        out_shape=jax.ShapeDtypeStruct((rows, q_width), jnp.bfloat16),
        in_specs=[vmem, vmem, vmem],
        out_specs=vmem,
        cost_estimate=pl.CostEstimate(
            flops=heads * causal_pairs * pair_flops,
            transcendentals=heads * causal_pairs * (rows // blocks) ** 2,
            bytes_accessed=qkv_slot.size * 2 + rows * q_width * 2,
        ),
    )(qkv_slot, query_pos[:, None], key_pos[None, :])


def on_device(
    hidden, lengths, dealing, norm_gain, w_query, w_key, w_value, query_gain, key_gain, w_out
):
    devices = lax.axis_size("req")
    home_index = lax.axis_index("req")
    slice_index = lax.axis_index("tp")
    tok_rows, features = hidden.shape
    head_dim = query_gain.shape[0]
    out_width = w_out.shape[1]
    q_width = w_query.shape[1]
    k_width = w_key.shape[1]
    slot_len = 4 * tok_rows
    capacity = slot_len // devices
    prompt_total = lengths.shape[0]
    prompt_ids = jnp.arange(prompt_total, dtype=jnp.int32)
    prompt_ends = jnp.cumsum(lengths)
    starts = prompt_ends - lengths
    packed_ids = jnp.arange(tok_rows, dtype=jnp.int32) * devices + home_index
    segment = jnp.sum((packed_ids[:, None] >= prompt_ends[None, :]).astype(jnp.int32), axis=1)
    seg_onehot = (segment[:, None] == prompt_ids[None, :]).astype(jnp.int32)
    positions = packed_ids - jnp.sum(seg_onehot * starts[None, :], axis=1)
    picked = prepare(
        hidden,
        lengths,
        dealing,
        jnp.reshape(home_index, (1,)).astype(jnp.int32),
        norm_gain,
        w_query,
        w_key,
        w_value,
        query_gain,
        key_gain,
        positions,
        capacity,
    )
    picked, lengths, dealing, starts, seg_onehot = lax.optimization_barrier(
        (picked, lengths, dealing, starts, seg_onehot)
    )
    inverse = jnp.zeros((prompt_total,), jnp.int32).at[dealing].set(prompt_ids)
    deal_hot = (dealing[:, None] == prompt_ids[None, :]).astype(jnp.int32)
    dealt_starts = jnp.sum(deal_hot * starts[None, :], axis=1)
    dealt_lengths = jnp.sum(deal_hot * lengths[None, :], axis=1)
    ranks = jnp.arange(capacity, dtype=jnp.int32)
    my_start = lax.dynamic_index_in_dim(dealt_starts, home_index, 0, keepdims=False)
    my_length = lax.dynamic_index_in_dim(dealt_lengths, home_index, 0, keepdims=False)
    roll_shift = jnp.mod(my_start, devices)
    my_slots = jnp.sum(seg_onehot * inverse[None, :], axis=1)
    back_rows = my_slots * capacity + positions // devices
    arrived = lax.all_to_all(
        picked.reshape(devices, capacity, picked.shape[1]),
        "req",
        split_axis=0,
        concat_axis=0,
        tiled=True,
    )
    source_ids = jnp.arange(devices, dtype=jnp.int32)
    arrived_pos = (
        ranks[None, :] * devices + jnp.mod(source_ids[:, None] - my_start, devices)
    ).reshape(-1)
    key_pos = jnp.where(arrived_pos < my_length, arrived_pos, 1 << 30)
    mixture = attend(
        arrived.reshape(slot_len, arrived.shape[2]), arrived_pos, key_pos, q_width, k_width, head_dim
    )
    returned = lax.all_to_all(
        mixture.reshape(devices, capacity, mixture.shape[1]),
        "req",
        split_axis=0,
        concat_axis=0,
        tiled=True,
    )
    attended = jnp.take(returned.reshape(capacity * devices, -1), back_rows, axis=0)
    kv_rows = (
        jnp.roll(arrived[:, :, q_width:], -roll_shift, axis=0)
        .transpose(1, 0, 2)
        .reshape(slot_len, -1)
    )
    kv_cache = jnp.stack([kv_rows[:, :k_width], kv_rows[:, k_width:]])[:, None]
    tp_size = lax.axis_size("tp")
    w_rows = w_out.shape[0] // tp_size
    summed = jnp.dot(
        attended,
        lax.dynamic_slice_in_dim(w_out, slice_index * w_rows, w_rows, 0),
        preferred_element_type=jnp.float32,
    )
    for shift in range(1, tp_size):
        passed = lax.ppermute(
            attended, "tp", perm=[(i, (i + shift) % tp_size) for i in range(tp_size)]
        )
        source = jnp.mod(slice_index - shift, tp_size)
        summed = summed + jnp.dot(
            passed,
            lax.dynamic_slice_in_dim(w_out, source * w_rows, w_rows, 0),
            preferred_element_type=jnp.float32,
        )
    branch = lax.optimization_barrier(summed.astype(jnp.bfloat16))
    residual = lax.dynamic_slice_in_dim(hidden, slice_index * out_width, out_width, 1)
    hidden_out = (residual.astype(jnp.float32) + branch.astype(jnp.float32)).astype(jnp.bfloat16)
    return (hidden_out, kv_cache)


def solution(mesh):
    in_specs = (
        P("req", None),
        P(),
        P(),
        P(),
        P(None, "tp"),
        P(None, "tp"),
        P(None, "tp"),
        P(),
        P(),
        P(None, "tp"),
    )
    out_specs = (P("req", "tp"), P(None, "req", None, "tp"))
    return jax.shard_map(
        on_device, mesh=mesh, in_specs=in_specs, out_specs=out_specs, check_vma=False
    )
```

```python
import jax
import jax.numpy as jnp
from jax import lax
from jax.experimental import pallas as pl
from jax.experimental.pallas import tpu as pltpu
from jax.sharding import PartitionSpec as P

EPS = 1e-06
THETA = 1000000.0


def rms_rows(values, scale_gain):
    inv_rms = lax.rsqrt(jnp.mean(values * values, axis=-1, keepdims=True) + EPS)
    return values * inv_rms * scale_gain


def rotate(values, positions):
    features = values.shape[-1]
    half_width = features // 2
    frequency = THETA ** (-(jnp.arange(half_width).astype(jnp.float32) * 2.0) / features)
    angles = positions.astype(jnp.float32)[:, None] * frequency[None, :]
    cosine = jnp.cos(angles)[:, None, :]
    sine_part = jnp.sin(angles)[:, None, :]
    first_half = values[..., :half_width]
    second_half = values[..., half_width:]
    return jnp.concatenate(
        [
            first_half * cosine - second_half * sine_part,
            second_half * cosine + first_half * sine_part,
        ],
        axis=-1,
    )


def project(normed, w_query, w_key, w_value, query_gain, key_gain, positions):
    head_dim = query_gain.shape[0]
    row_count = normed.shape[0]
    query_rows = jnp.dot(normed, w_query, preferred_element_type=jnp.float32).reshape(
        row_count, -1, head_dim
    )
    key_rows = jnp.dot(normed, w_key, preferred_element_type=jnp.float32).reshape(
        row_count, -1, head_dim
    )
    value_rows = jnp.dot(normed, w_value, preferred_element_type=jnp.float32).astype(jnp.bfloat16)
    query_rows = rotate(rms_rows(query_rows, query_gain.astype(jnp.float32)), positions).astype(
        jnp.bfloat16
    )
    key_rows = rotate(rms_rows(key_rows, key_gain.astype(jnp.float32)), positions).astype(
        jnp.bfloat16
    )
    return (query_rows.reshape(row_count, -1), key_rows.reshape(row_count, -1), value_rows)


def prep_kernel(
    lengths_ref,
    dealing_ref,
    home_ref,
    hidden_ref,
    norm_gain_ref,
    wq_ref,
    wk_ref,
    wv_ref,
    qgain_ref,
    kgain_ref,
    cos_ref,
    sin_ref,
    out_ref,
    qkv_ref,
    pick_ref,
    starts_ref,
    *,
    head_dim,
    capacity,
):
    devices = dealing_ref.shape[0]
    prompt_total = lengths_ref.shape[0]
    tok_rows = qkv_ref.shape[0]

    def running(p, total):
        starts_ref[p] = total
        return total + lengths_ref[p]

    lax.fori_loop(0, prompt_total, running, jnp.int32(0))
    home = home_ref[0]
    rank_ids = lax.broadcasted_iota(jnp.int32, (capacity, tok_rows), 0)
    row_gap = lax.broadcasted_iota(jnp.int32, (capacity, tok_rows), 1) - rank_ids

    def pick_rows(d, carry):
        prompt = dealing_ref[d]
        start = starts_ref[prompt]
        length = lengths_ref[prompt]
        first = lax.rem(lax.rem(home - start, devices) + devices, devices)
        first_row = lax.div(start + first - home, devices)
        count = jnp.minimum(lax.div(length - first + devices - 1, devices), capacity)
        hits = (row_gap == first_row) & (rank_ids < count)
        pick_ref[pl.ds(pl.multiple_of(d * capacity, capacity), capacity), :] = hits.astype(
            pick_ref.dtype
        )
        return carry

    lax.fori_loop(0, devices, pick_rows, 0)
    values = hidden_ref[...].astype(jnp.float32)
    inv_rms = lax.rsqrt(jnp.mean(values * values, axis=-1, keepdims=True) + EPS)
    normed = (values * inv_rms * norm_gain_ref[...].astype(jnp.float32)[None, :]).astype(
        jnp.bfloat16
    )
    cosine = cos_ref[...]
    sine = sin_ref[...]
    column = 0
    for w_ref, gain_ref in ((wq_ref, qgain_ref), (wk_ref, kgain_ref)):
        rows = jnp.dot(normed, w_ref[...], preferred_element_type=jnp.float32)
        gain = gain_ref[...].astype(jnp.float32)
        for h in range(rows.shape[1] // head_dim):
            head = rows[:, h * head_dim : (h + 1) * head_dim]
            head_inv = lax.rsqrt(jnp.mean(head * head, axis=-1, keepdims=True) + EPS)
            head = head * head_inv * gain
            swapped = pltpu.roll(head, head_dim // 2, 1)
            qkv_ref[:, column : column + head_dim] = (head * cosine + swapped * sine).astype(
                jnp.bfloat16
            )
            column += head_dim
    v_width = wv_ref.shape[1]
    qkv_ref[:, column : column + v_width] = jnp.dot(
        normed, wv_ref[...], preferred_element_type=jnp.float32
    ).astype(jnp.bfloat16)
    qkv = qkv_ref[...]
    out_rows = out_ref.shape[0]
    block = out_rows // 4
    for b in range(4):
        rows_here = pl.ds(b * block, block)
        out_ref[rows_here, :] = jnp.dot(
            pick_ref[rows_here, :], qkv, preferred_element_type=jnp.float32
        ).astype(out_ref.dtype)


def prepare(
    hidden, lengths, dealing, home, norm_gain, w_query, w_key, w_value, query_gain, key_gain,
    positions, capacity,
):
    tok_rows, features = hidden.shape
    head_dim = query_gain.shape[0]
    half_width = head_dim // 2
    width = w_query.shape[1] + w_key.shape[1] + w_value.shape[1]
    devices = dealing.shape[0]
    out_rows = devices * capacity
    frequency = THETA ** (-(jnp.arange(half_width).astype(jnp.float32) * 2.0) / head_dim)
    frequency = jnp.concatenate([frequency, frequency])
    angles = positions.astype(jnp.float32)[:, None] * frequency[None, :]
    sign = jnp.where(jnp.arange(head_dim) < half_width, -1.0, 1.0).astype(jnp.float32)
    cos_full = jnp.cos(angles)
    sin_signed = jnp.sin(angles) * sign[None, :]
    vmem = pl.BlockSpec(memory_space=pltpu.VMEM)
    smem = pl.BlockSpec(memory_space=pltpu.SMEM)
    return pl.pallas_call(
        lambda *refs: prep_kernel(*refs, head_dim=head_dim, capacity=capacity),
        out_shape=jax.ShapeDtypeStruct((out_rows, width), jnp.bfloat16),
        in_specs=[smem] * 3 + [vmem] * 9,
        out_specs=vmem,
        scratch_shapes=[
            pltpu.VMEM((tok_rows, width), jnp.bfloat16),
            pltpu.VMEM((out_rows, tok_rows), jnp.bfloat16),
            pltpu.SMEM((lengths.shape[0],), jnp.int32),
        ],
        cost_estimate=pl.CostEstimate(
            flops=2 * tok_rows * features * width + 2 * out_rows * tok_rows * width,
            transcendentals=tok_rows * 8,
            bytes_accessed=hidden.size * 2 + features * width * 2 + out_rows * width * 2,
        ),
    )(
        lengths,
        dealing,
        home,
        hidden,
        norm_gain,
        w_query,
        w_key,
        w_value,
        query_gain[None, :],
        key_gain[None, :],
        cos_full,
        sin_signed,
    )


def attention_kernel(qkv_ref, qpos_ref, kpos_ref, out_ref, *, q_width, k_width, head_dim, blocks):
    rows = qkv_ref.shape[0]
    block = rows // blocks
    kv_heads = k_width // head_dim
    group = q_width // head_dim // kv_heads
    scale = head_dim ** (-0.5)
    for i in range(blocks):
        key_rows = rows
        rows_here = pl.ds(i * block, block)
        allowed = kpos_ref[:, :key_rows] <= qpos_ref[rows_here, :]
        for h in range(kv_heads):
            k_col = q_width + h * head_dim
            v_col = q_width + k_width + h * head_dim
            keys = qkv_ref[:key_rows, k_col : k_col + head_dim]
            values = qkv_ref[:key_rows, v_col : v_col + head_dim]
            for g in range(group):
                q_col = (h * group + g) * head_dim
                queries = qkv_ref[rows_here, q_col : q_col + head_dim]
                scores = lax.dot_general(
                    queries,
                    keys,
                    (((1,), (1,)), ((), ())),
                    preferred_element_type=jnp.float32,
                ) * scale
                scores = jnp.where(allowed, scores, -jnp.inf)
                row_max = jnp.max(scores, axis=-1, keepdims=True)
                weights = jnp.exp(scores - row_max)
                weights = (weights / jnp.sum(weights, axis=-1, keepdims=True)).astype(jnp.bfloat16)
                mixed = jnp.dot(weights, values, preferred_element_type=jnp.float32)
                out_ref[rows_here, q_col : q_col + head_dim] = mixed.astype(out_ref.dtype)


def attend(qkv_slot, query_pos, key_pos, q_width, k_width, head_dim):
    rows = qkv_slot.shape[0]
    blocks = 2
    heads = q_width // head_dim
    causal_pairs = blocks * blocks
    pair_flops = 4 * (rows // blocks) ** 2 * head_dim
    vmem = pl.BlockSpec(memory_space=pltpu.VMEM)
    return pl.pallas_call(
        lambda *refs: attention_kernel(
            *refs, q_width=q_width, k_width=k_width, head_dim=head_dim, blocks=blocks
        ),
        out_shape=jax.ShapeDtypeStruct((rows, q_width), jnp.bfloat16),
        in_specs=[vmem, vmem, vmem],
        out_specs=vmem,
        cost_estimate=pl.CostEstimate(
            flops=heads * causal_pairs * pair_flops,
            transcendentals=heads * causal_pairs * (rows // blocks) ** 2,
            bytes_accessed=qkv_slot.size * 2 + rows * q_width * 2,
        ),
    )(qkv_slot, query_pos[:, None], key_pos[None, :])


def on_device(
    hidden, lengths, dealing, norm_gain, w_query, w_key, w_value, query_gain, key_gain, w_out
):
    devices = lax.axis_size("req")
    home_index = lax.axis_index("req")
    slice_index = lax.axis_index("tp")
    tok_rows, features = hidden.shape
    head_dim = query_gain.shape[0]
    out_width = w_out.shape[1]
    q_width = w_query.shape[1]
    k_width = w_key.shape[1]
    slot_len = 4 * tok_rows
    capacity = slot_len // devices
    prompt_total = lengths.shape[0]
    prompt_ids = jnp.arange(prompt_total, dtype=jnp.int32)
    prompt_ends = jnp.cumsum(lengths)
    starts = prompt_ends - lengths
    packed_ids = jnp.arange(tok_rows, dtype=jnp.int32) * devices + home_index
    segment = jnp.sum((packed_ids[:, None] >= prompt_ends[None, :]).astype(jnp.int32), axis=1)
    seg_onehot = (segment[:, None] == prompt_ids[None, :]).astype(jnp.int32)
    positions = packed_ids - jnp.sum(seg_onehot * starts[None, :], axis=1)
    picked = prepare(
        hidden,
        lengths,
        dealing,
        jnp.reshape(home_index, (1,)).astype(jnp.int32),
        norm_gain,
        w_query,
        w_key,
        w_value,
        query_gain,
        key_gain,
        positions,
        capacity,
    )
    picked, lengths, dealing, starts, seg_onehot = lax.optimization_barrier(
        (picked, lengths, dealing, starts, seg_onehot)
    )
    inverse = jnp.zeros((prompt_total,), jnp.int32).at[dealing].set(prompt_ids)
    deal_hot = (dealing[:, None] == prompt_ids[None, :]).astype(jnp.int32)
    dealt_starts = jnp.sum(deal_hot * starts[None, :], axis=1)
    dealt_lengths = jnp.sum(deal_hot * lengths[None, :], axis=1)
    ranks = jnp.arange(capacity, dtype=jnp.int32)
    my_start = lax.dynamic_index_in_dim(dealt_starts, home_index, 0, keepdims=False)
    my_length = lax.dynamic_index_in_dim(dealt_lengths, home_index, 0, keepdims=False)
    roll_shift = jnp.mod(my_start, devices)
    my_slots = jnp.sum(seg_onehot * inverse[None, :], axis=1)
    back_rows = my_slots * capacity + positions // devices
    arrived = lax.all_to_all(
        picked.reshape(devices, capacity, picked.shape[1]),
        "req",
        split_axis=0,
        concat_axis=0,
        tiled=True,
    )
    source_ids = jnp.arange(devices, dtype=jnp.int32)
    arrived_pos = (
        ranks[None, :] * devices + jnp.mod(source_ids[:, None] - my_start, devices)
    ).reshape(-1)
    key_pos = jnp.where(arrived_pos < my_length, arrived_pos, 1 << 30)
    mixture = attend(
        arrived.reshape(slot_len, arrived.shape[2]), arrived_pos, key_pos, q_width, k_width, head_dim
    )
    returned = lax.all_to_all(
        mixture.reshape(devices, capacity, mixture.shape[1]),
        "req",
        split_axis=0,
        concat_axis=0,
        tiled=True,
    )
    attended = jnp.take(returned.reshape(capacity * devices, -1), back_rows, axis=0)
    kv_rows = (
        jnp.roll(arrived[:, :, q_width:], -roll_shift, axis=0)
        .transpose(1, 0, 2)
        .reshape(slot_len, -1)
    )
    kv_cache = jnp.stack([kv_rows[:, :k_width], kv_rows[:, k_width:]])[:, None]
    tp_size = lax.axis_size("tp")
    w_rows = w_out.shape[0] // tp_size
    summed = jnp.dot(
        attended,
        lax.dynamic_slice_in_dim(w_out, slice_index * w_rows, w_rows, 0),
        preferred_element_type=jnp.float32,
    )
    for shift in range(1, tp_size):
        passed = lax.ppermute(
            attended, "tp", perm=[(i, (i + shift) % tp_size) for i in range(tp_size)]
        )
        source = jnp.mod(slice_index - shift, tp_size)
        summed = summed + jnp.dot(
            passed,
            lax.dynamic_slice_in_dim(w_out, source * w_rows, w_rows, 0),
            preferred_element_type=jnp.float32,
        )
    branch = lax.optimization_barrier(summed.astype(jnp.bfloat16))
    residual = lax.dynamic_slice_in_dim(hidden, slice_index * out_width, out_width, 1)
    hidden_out = (residual.astype(jnp.float32) + branch.astype(jnp.float32)).astype(jnp.bfloat16)
    return (hidden_out, kv_cache)


def solution(mesh):
    in_specs = (
        P("req", None),
        P(),
        P(),
        P(),
        P(None, "tp"),
        P(None, "tp"),
        P(None, "tp"),
        P(),
        P(),
        P(None, "tp"),
    )
    out_specs = (P("req", "tp"), P(None, "req", None, "tp"))
    return jax.shard_map(
        on_device, mesh=mesh, in_specs=in_specs, out_specs=out_specs, check_vma=False
    )
```

```python
import jax
import jax.numpy as jnp
from jax import lax
from jax.experimental import pallas as pl
from jax.experimental.pallas import tpu as pltpu
from jax.sharding import PartitionSpec as P

EPS = 1e-06
THETA = 1000000.0


def rms_rows(values, scale_gain):
    inv_rms = lax.rsqrt(jnp.mean(values * values, axis=-1, keepdims=True) + EPS)
    return values * inv_rms * scale_gain


def rotate(values, positions):
    features = values.shape[-1]
    half_width = features // 2
    frequency = THETA ** (-(jnp.arange(half_width).astype(jnp.float32) * 2.0) / features)
    angles = positions.astype(jnp.float32)[:, None] * frequency[None, :]
    cosine = jnp.cos(angles)[:, None, :]
    sine_part = jnp.sin(angles)[:, None, :]
    first_half = values[..., :half_width]
    second_half = values[..., half_width:]
    return jnp.concatenate(
        [
            first_half * cosine - second_half * sine_part,
            second_half * cosine + first_half * sine_part,
        ],
        axis=-1,
    )


def project(normed, w_query, w_key, w_value, query_gain, key_gain, positions):
    head_dim = query_gain.shape[0]
    row_count = normed.shape[0]
    query_rows = jnp.dot(normed, w_query, preferred_element_type=jnp.float32).reshape(
        row_count, -1, head_dim
    )
    key_rows = jnp.dot(normed, w_key, preferred_element_type=jnp.float32).reshape(
        row_count, -1, head_dim
    )
    value_rows = jnp.dot(normed, w_value, preferred_element_type=jnp.float32).astype(jnp.bfloat16)
    query_rows = rotate(rms_rows(query_rows, query_gain.astype(jnp.float32)), positions).astype(
        jnp.bfloat16
    )
    key_rows = rotate(rms_rows(key_rows, key_gain.astype(jnp.float32)), positions).astype(
        jnp.bfloat16
    )
    return (query_rows.reshape(row_count, -1), key_rows.reshape(row_count, -1), value_rows)


def prep_kernel(
    lengths_ref,
    dealing_ref,
    home_ref,
    hidden_ref,
    norm_gain_ref,
    wq_ref,
    wk_ref,
    wv_ref,
    qgain_ref,
    kgain_ref,
    cos_ref,
    sin_ref,
    out_ref,
    qkv_ref,
    pick_ref,
    starts_ref,
    *,
    head_dim,
    capacity,
):
    devices = dealing_ref.shape[0]
    prompt_total = lengths_ref.shape[0]
    tok_rows = qkv_ref.shape[0]

    def running(p, total):
        starts_ref[p] = total
        return total + lengths_ref[p]

    lax.fori_loop(0, prompt_total, running, jnp.int32(0))
    home = home_ref[0]
    rank_ids = lax.broadcasted_iota(jnp.int32, (capacity, tok_rows), 0)
    row_gap = lax.broadcasted_iota(jnp.int32, (capacity, tok_rows), 1) - rank_ids

    def pick_rows(d, carry):
        prompt = dealing_ref[d]
        start = starts_ref[prompt]
        length = lengths_ref[prompt]
        first = lax.rem(lax.rem(home - start, devices) + devices, devices)
        first_row = lax.div(start + first - home, devices)
        count = jnp.minimum(lax.div(length - first + devices - 1, devices), capacity)
        hits = (row_gap == first_row) & (rank_ids < count)
        pick_ref[pl.ds(pl.multiple_of(d * capacity, capacity), capacity), :] = hits.astype(
            pick_ref.dtype
        )
        return carry

    lax.fori_loop(0, devices, pick_rows, 0)
    values = hidden_ref[...].astype(jnp.float32)
    inv_rms = lax.rsqrt(jnp.mean(values * values, axis=-1, keepdims=True) + EPS)
    normed = (values * inv_rms * norm_gain_ref[...].astype(jnp.float32)[None, :]).astype(
        jnp.bfloat16
    )
    cosine = cos_ref[...]
    sine = sin_ref[...]
    column = 0
    for w_ref, gain_ref in ((wq_ref, qgain_ref), (wk_ref, kgain_ref)):
        rows = jnp.dot(normed, w_ref[...], preferred_element_type=jnp.float32)
        gain = gain_ref[...].astype(jnp.float32)
        for h in range(rows.shape[1] // head_dim):
            head = rows[:, h * head_dim : (h + 1) * head_dim]
            head_inv = lax.rsqrt(jnp.mean(head * head, axis=-1, keepdims=True) + EPS)
            head = head * head_inv * gain
            swapped = pltpu.roll(head, head_dim // 2, 1)
            qkv_ref[:, column : column + head_dim] = (head * cosine + swapped * sine).astype(
                jnp.bfloat16
            )
            column += head_dim
    v_width = wv_ref.shape[1]
    qkv_ref[:, column : column + v_width] = jnp.dot(
        normed, wv_ref[...], preferred_element_type=jnp.float32
    ).astype(jnp.bfloat16)
    qkv = qkv_ref[...]
    out_rows = out_ref.shape[0]
    block = out_rows // 4
    for b in range(4):
        rows_here = pl.ds(b * block, block)
        out_ref[rows_here, :] = jnp.dot(
            pick_ref[rows_here, :], qkv, preferred_element_type=jnp.float32
        ).astype(out_ref.dtype)


def prepare(
    hidden, lengths, dealing, home, norm_gain, w_query, w_key, w_value, query_gain, key_gain,
    positions, capacity,
):
    tok_rows, features = hidden.shape
    head_dim = query_gain.shape[0]
    half_width = head_dim // 2
    width = w_query.shape[1] + w_key.shape[1] + w_value.shape[1]
    devices = dealing.shape[0]
    out_rows = devices * capacity
    frequency = THETA ** (-(jnp.arange(half_width).astype(jnp.float32) * 2.0) / head_dim)
    frequency = jnp.concatenate([frequency, frequency])
    angles = positions.astype(jnp.float32)[:, None] * frequency[None, :]
    sign = jnp.where(jnp.arange(head_dim) < half_width, -1.0, 1.0).astype(jnp.float32)
    cos_full = jnp.cos(angles)
    sin_signed = jnp.sin(angles) * sign[None, :]
    vmem = pl.BlockSpec(memory_space=pltpu.VMEM)
    smem = pl.BlockSpec(memory_space=pltpu.SMEM)
    return pl.pallas_call(
        lambda *refs: prep_kernel(*refs, head_dim=head_dim, capacity=capacity),
        out_shape=jax.ShapeDtypeStruct((out_rows, width), jnp.bfloat16),
        in_specs=[smem] * 3 + [vmem] * 9,
        out_specs=vmem,
        scratch_shapes=[
            pltpu.VMEM((tok_rows, width), jnp.bfloat16),
            pltpu.VMEM((out_rows, tok_rows), jnp.bfloat16),
            pltpu.SMEM((lengths.shape[0],), jnp.int32),
        ],
        cost_estimate=pl.CostEstimate(
            flops=2 * tok_rows * features * width + 2 * out_rows * tok_rows * width,
            transcendentals=tok_rows * 8,
            bytes_accessed=hidden.size * 2 + features * width * 2 + out_rows * width * 2,
        ),
    )(
        lengths,
        dealing,
        home,
        hidden,
        norm_gain,
        w_query,
        w_key,
        w_value,
        query_gain[None, :],
        key_gain[None, :],
        cos_full,
        sin_signed,
    )


def attention_kernel(qkv_ref, qpos_ref, kpos_ref, out_ref, *, q_width, k_width, head_dim, blocks):
    rows = qkv_ref.shape[0]
    block = rows // blocks
    kv_heads = k_width // head_dim
    group = q_width // head_dim // kv_heads
    scale = head_dim ** (-0.5)
    for i in range(blocks):
        key_rows = rows
        rows_here = pl.ds(i * block, block)
        allowed = kpos_ref[:, :key_rows] <= qpos_ref[rows_here, :]
        for h in range(kv_heads):
            k_col = q_width + h * head_dim
            v_col = q_width + k_width + h * head_dim
            keys = qkv_ref[:key_rows, k_col : k_col + head_dim]
            values = qkv_ref[:key_rows, v_col : v_col + head_dim]
            for g in range(group):
                q_col = (h * group + g) * head_dim
                queries = qkv_ref[rows_here, q_col : q_col + head_dim]
                scores = lax.dot_general(
                    queries,
                    keys,
                    (((1,), (1,)), ((), ())),
                    preferred_element_type=jnp.float32,
                ) * scale
                scores = jnp.where(allowed, scores, -jnp.inf)
                row_max = jnp.max(scores, axis=-1, keepdims=True)
                weights = jnp.exp(scores - row_max)
                weights = (weights / jnp.sum(weights, axis=-1, keepdims=True)).astype(jnp.bfloat16)
                mixed = jnp.dot(weights, values, preferred_element_type=jnp.float32)
                out_ref[rows_here, q_col : q_col + head_dim] = mixed.astype(out_ref.dtype)


def attend(qkv_slot, query_pos, key_pos, q_width, k_width, head_dim):
    rows = qkv_slot.shape[0]
    blocks = 4
    heads = q_width // head_dim
    causal_pairs = blocks * blocks
    pair_flops = 4 * (rows // blocks) ** 2 * head_dim
    vmem = pl.BlockSpec(memory_space=pltpu.VMEM)
    return pl.pallas_call(
        lambda *refs: attention_kernel(
            *refs, q_width=q_width, k_width=k_width, head_dim=head_dim, blocks=blocks
        ),
        out_shape=jax.ShapeDtypeStruct((rows, q_width), jnp.bfloat16),
        in_specs=[vmem, vmem, vmem],
        out_specs=vmem,
        cost_estimate=pl.CostEstimate(
            flops=heads * causal_pairs * pair_flops,
            transcendentals=heads * causal_pairs * (rows // blocks) ** 2,
            bytes_accessed=qkv_slot.size * 2 + rows * q_width * 2,
        ),
    )(qkv_slot, query_pos[:, None], key_pos[None, :])


def on_device(
    hidden, lengths, dealing, norm_gain, w_query, w_key, w_value, query_gain, key_gain, w_out
):
    devices = lax.axis_size("req")
    home_index = lax.axis_index("req")
    slice_index = lax.axis_index("tp")
    tok_rows, features = hidden.shape
    head_dim = query_gain.shape[0]
    out_width = w_out.shape[1]
    q_width = w_query.shape[1]
    k_width = w_key.shape[1]
    slot_len = 4 * tok_rows
    capacity = slot_len // devices
    prompt_total = lengths.shape[0]
    prompt_ids = jnp.arange(prompt_total, dtype=jnp.int32)
    prompt_ends = jnp.cumsum(lengths)
    starts = prompt_ends - lengths
    packed_ids = jnp.arange(tok_rows, dtype=jnp.int32) * devices + home_index
    segment = jnp.sum((packed_ids[:, None] >= prompt_ends[None, :]).astype(jnp.int32), axis=1)
    seg_onehot = (segment[:, None] == prompt_ids[None, :]).astype(jnp.int32)
    positions = packed_ids - jnp.sum(seg_onehot * starts[None, :], axis=1)
    picked = prepare(
        hidden,
        lengths,
        dealing,
        jnp.reshape(home_index, (1,)).astype(jnp.int32),
        norm_gain,
        w_query,
        w_key,
        w_value,
        query_gain,
        key_gain,
        positions,
        capacity,
    )
    picked, lengths, dealing, starts, seg_onehot = lax.optimization_barrier(
        (picked, lengths, dealing, starts, seg_onehot)
    )
    inverse = jnp.zeros((prompt_total,), jnp.int32).at[dealing].set(prompt_ids)
    deal_hot = (dealing[:, None] == prompt_ids[None, :]).astype(jnp.int32)
    dealt_starts = jnp.sum(deal_hot * starts[None, :], axis=1)
    dealt_lengths = jnp.sum(deal_hot * lengths[None, :], axis=1)
    ranks = jnp.arange(capacity, dtype=jnp.int32)
    my_start = lax.dynamic_index_in_dim(dealt_starts, home_index, 0, keepdims=False)
    my_length = lax.dynamic_index_in_dim(dealt_lengths, home_index, 0, keepdims=False)
    roll_shift = jnp.mod(my_start, devices)
    my_slots = jnp.sum(seg_onehot * inverse[None, :], axis=1)
    back_rows = my_slots * capacity + positions // devices
    arrived = lax.all_to_all(
        picked.reshape(devices, capacity, picked.shape[1]),
        "req",
        split_axis=0,
        concat_axis=0,
        tiled=True,
    )
    source_ids = jnp.arange(devices, dtype=jnp.int32)
    arrived_pos = (
        ranks[None, :] * devices + jnp.mod(source_ids[:, None] - my_start, devices)
    ).reshape(-1)
    key_pos = jnp.where(arrived_pos < my_length, arrived_pos, 1 << 30)
    mixture = attend(
        arrived.reshape(slot_len, arrived.shape[2]), arrived_pos, key_pos, q_width, k_width, head_dim
    )
    returned = lax.all_to_all(
        mixture.reshape(devices, capacity, mixture.shape[1]),
        "req",
        split_axis=0,
        concat_axis=0,
        tiled=True,
    )
    attended = jnp.take(returned.reshape(capacity * devices, -1), back_rows, axis=0)
    kv_rows = (
        jnp.roll(arrived[:, :, q_width:], -roll_shift, axis=0)
        .transpose(1, 0, 2)
        .reshape(slot_len, -1)
    )
    kv_cache = jnp.stack([kv_rows[:, :k_width], kv_rows[:, k_width:]])[:, None]
    tp_size = lax.axis_size("tp")
    w_rows = w_out.shape[0] // tp_size
    summed = jnp.dot(
        attended,
        lax.dynamic_slice_in_dim(w_out, slice_index * w_rows, w_rows, 0),
        preferred_element_type=jnp.float32,
    )
    for shift in range(1, tp_size):
        passed = lax.ppermute(
            attended, "tp", perm=[(i, (i + shift) % tp_size) for i in range(tp_size)]
        )
        source = jnp.mod(slice_index - shift, tp_size)
        summed = summed + jnp.dot(
            passed,
            lax.dynamic_slice_in_dim(w_out, source * w_rows, w_rows, 0),
            preferred_element_type=jnp.float32,
        )
    branch = lax.optimization_barrier(summed.astype(jnp.bfloat16))
    residual = lax.dynamic_slice_in_dim(hidden, slice_index * out_width, out_width, 1)
    hidden_out = (residual.astype(jnp.float32) + branch.astype(jnp.float32)).astype(jnp.bfloat16)
    return (hidden_out, kv_cache)


def solution(mesh):
    in_specs = (
        P("req", None),
        P(),
        P(),
        P(),
        P(None, "tp"),
        P(None, "tp"),
        P(None, "tp"),
        P(),
        P(),
        P(None, "tp"),
    )
    out_specs = (P("req", "tp"), P(None, "req", None, "tp"))
    return jax.shard_map(
        on_device, mesh=mesh, in_specs=in_specs, out_specs=out_specs, check_vma=False
    )
```

```python
import jax
import jax.numpy as jnp
from jax import lax
from jax.experimental import pallas as pl
from jax.experimental.pallas import tpu as pltpu
from jax.sharding import PartitionSpec as P

EPS = 1e-06
THETA = 1000000.0


def rms_rows(values, scale_gain):
    inv_rms = lax.rsqrt(jnp.mean(values * values, axis=-1, keepdims=True) + EPS)
    return values * inv_rms * scale_gain


def rotate(values, positions):
    features = values.shape[-1]
    half_width = features // 2
    frequency = THETA ** (-(jnp.arange(half_width).astype(jnp.float32) * 2.0) / features)
    angles = positions.astype(jnp.float32)[:, None] * frequency[None, :]
    cosine = jnp.cos(angles)[:, None, :]
    sine_part = jnp.sin(angles)[:, None, :]
    first_half = values[..., :half_width]
    second_half = values[..., half_width:]
    return jnp.concatenate(
        [
            first_half * cosine - second_half * sine_part,
            second_half * cosine + first_half * sine_part,
        ],
        axis=-1,
    )


def project(normed, w_query, w_key, w_value, query_gain, key_gain, positions):
    head_dim = query_gain.shape[0]
    row_count = normed.shape[0]
    query_rows = jnp.dot(normed, w_query, preferred_element_type=jnp.float32).reshape(
        row_count, -1, head_dim
    )
    key_rows = jnp.dot(normed, w_key, preferred_element_type=jnp.float32).reshape(
        row_count, -1, head_dim
    )
    value_rows = jnp.dot(normed, w_value, preferred_element_type=jnp.float32).astype(jnp.bfloat16)
    query_rows = rotate(rms_rows(query_rows, query_gain.astype(jnp.float32)), positions).astype(
        jnp.bfloat16
    )
    key_rows = rotate(rms_rows(key_rows, key_gain.astype(jnp.float32)), positions).astype(
        jnp.bfloat16
    )
    return (query_rows.reshape(row_count, -1), key_rows.reshape(row_count, -1), value_rows)


def prep_kernel(
    lengths_ref,
    dealing_ref,
    home_ref,
    hidden_ref,
    norm_gain_ref,
    wq_ref,
    wk_ref,
    wv_ref,
    qgain_ref,
    kgain_ref,
    cos_ref,
    sin_ref,
    out_ref,
    qkv_ref,
    pick_ref,
    starts_ref,
    *,
    head_dim,
    capacity,
):
    devices = dealing_ref.shape[0]
    prompt_total = lengths_ref.shape[0]
    tok_rows = qkv_ref.shape[0]

    def running(p, total):
        starts_ref[p] = total
        return total + lengths_ref[p]

    lax.fori_loop(0, prompt_total, running, jnp.int32(0))
    home = home_ref[0]
    rank_ids = lax.broadcasted_iota(jnp.int32, (capacity, tok_rows), 0)
    row_gap = lax.broadcasted_iota(jnp.int32, (capacity, tok_rows), 1) - rank_ids

    def pick_rows(d, carry):
        prompt = dealing_ref[d]
        start = starts_ref[prompt]
        length = lengths_ref[prompt]
        first = lax.rem(lax.rem(home - start, devices) + devices, devices)
        first_row = lax.div(start + first - home, devices)
        count = jnp.minimum(lax.div(length - first + devices - 1, devices), capacity)
        hits = (row_gap == first_row) & (rank_ids < count)
        pick_ref[pl.ds(pl.multiple_of(d * capacity, capacity), capacity), :] = hits.astype(
            pick_ref.dtype
        )
        return carry

    lax.fori_loop(0, devices, pick_rows, 0)
    values = hidden_ref[...].astype(jnp.float32)
    inv_rms = lax.rsqrt(jnp.mean(values * values, axis=-1, keepdims=True) + EPS)
    normed = (values * inv_rms * norm_gain_ref[...].astype(jnp.float32)[None, :]).astype(
        jnp.bfloat16
    )
    cosine = cos_ref[...]
    sine = sin_ref[...]
    column = 0
    for w_ref, gain_ref in ((wq_ref, qgain_ref), (wk_ref, kgain_ref)):
        rows = jnp.dot(normed, w_ref[...], preferred_element_type=jnp.float32)
        gain = gain_ref[...].astype(jnp.float32)
        for h in range(rows.shape[1] // head_dim):
            head = rows[:, h * head_dim : (h + 1) * head_dim]
            head_inv = lax.rsqrt(jnp.mean(head * head, axis=-1, keepdims=True) + EPS)
            head = head * head_inv * gain
            swapped = pltpu.roll(head, head_dim // 2, 1)
            qkv_ref[:, column : column + head_dim] = (head * cosine + swapped * sine).astype(
                jnp.bfloat16
            )
            column += head_dim
    v_width = wv_ref.shape[1]
    qkv_ref[:, column : column + v_width] = jnp.dot(
        normed, wv_ref[...], preferred_element_type=jnp.float32
    ).astype(jnp.bfloat16)
    qkv = qkv_ref[...]
    out_rows = out_ref.shape[0]
    block = out_rows // 4
    for b in range(4):
        rows_here = pl.ds(b * block, block)
        out_ref[rows_here, :] = jnp.dot(
            pick_ref[rows_here, :], qkv, preferred_element_type=jnp.float32
        ).astype(out_ref.dtype)


def prepare(
    hidden, lengths, dealing, home, norm_gain, w_query, w_key, w_value, query_gain, key_gain,
    positions, capacity,
):
    tok_rows, features = hidden.shape
    head_dim = query_gain.shape[0]
    half_width = head_dim // 2
    width = w_query.shape[1] + w_key.shape[1] + w_value.shape[1]
    devices = dealing.shape[0]
    out_rows = devices * capacity
    frequency = THETA ** (-(jnp.arange(half_width).astype(jnp.float32) * 2.0) / head_dim)
    frequency = jnp.concatenate([frequency, frequency])
    angles = positions.astype(jnp.float32)[:, None] * frequency[None, :]
    sign = jnp.where(jnp.arange(head_dim) < half_width, -1.0, 1.0).astype(jnp.float32)
    cos_full = jnp.cos(angles)
    sin_signed = jnp.sin(angles) * sign[None, :]
    vmem = pl.BlockSpec(memory_space=pltpu.VMEM)
    smem = pl.BlockSpec(memory_space=pltpu.SMEM)
    return pl.pallas_call(
        lambda *refs: prep_kernel(*refs, head_dim=head_dim, capacity=capacity),
        out_shape=jax.ShapeDtypeStruct((out_rows, width), jnp.bfloat16),
        in_specs=[smem] * 3 + [vmem] * 9,
        out_specs=vmem,
        scratch_shapes=[
            pltpu.VMEM((tok_rows, width), jnp.bfloat16),
            pltpu.VMEM((out_rows, tok_rows), jnp.bfloat16),
            pltpu.SMEM((lengths.shape[0],), jnp.int32),
        ],
        cost_estimate=pl.CostEstimate(
            flops=2 * tok_rows * features * width + 2 * out_rows * tok_rows * width,
            transcendentals=tok_rows * 8,
            bytes_accessed=hidden.size * 2 + features * width * 2 + out_rows * width * 2,
        ),
    )(
        lengths,
        dealing,
        home,
        hidden,
        norm_gain,
        w_query,
        w_key,
        w_value,
        query_gain[None, :],
        key_gain[None, :],
        cos_full,
        sin_signed,
    )


def attention_kernel(qkv_ref, qpos_ref, kpos_ref, out_ref, *, q_width, k_width, head_dim, blocks):
    rows = qkv_ref.shape[0]
    block = rows // blocks
    kv_heads = k_width // head_dim
    group = q_width // head_dim // kv_heads
    scale = head_dim ** (-0.5)
    for i in range(blocks):
        key_rows = rows
        rows_here = pl.ds(i * block, block)
        allowed = kpos_ref[:, :key_rows] <= qpos_ref[rows_here, :]
        for h in range(kv_heads):
            k_col = q_width + h * head_dim
            v_col = q_width + k_width + h * head_dim
            keys = qkv_ref[:key_rows, k_col : k_col + head_dim]
            values = qkv_ref[:key_rows, v_col : v_col + head_dim]
            for g in range(group):
                q_col = (h * group + g) * head_dim
                queries = qkv_ref[rows_here, q_col : q_col + head_dim]
                scores = lax.dot_general(
                    queries,
                    keys,
                    (((1,), (1,)), ((), ())),
                    preferred_element_type=jnp.float32,
                ) * scale
                scores = jnp.where(allowed, scores, -jnp.inf)
                row_max = jnp.max(scores, axis=-1, keepdims=True)
                weights = jnp.exp(scores - row_max)
                weights = (weights / jnp.sum(weights, axis=-1, keepdims=True)).astype(jnp.bfloat16)
                mixed = jnp.dot(weights, values, preferred_element_type=jnp.float32)
                out_ref[rows_here, q_col : q_col + head_dim] = mixed.astype(out_ref.dtype)


def attend(qkv_slot, query_pos, key_pos, q_width, k_width, head_dim):
    rows = qkv_slot.shape[0]
    blocks = 2
    heads = q_width // head_dim
    causal_pairs = blocks * blocks
    pair_flops = 4 * (rows // blocks) ** 2 * head_dim
    vmem = pl.BlockSpec(memory_space=pltpu.VMEM)
    return pl.pallas_call(
        lambda *refs: attention_kernel(
            *refs, q_width=q_width, k_width=k_width, head_dim=head_dim, blocks=blocks
        ),
        out_shape=jax.ShapeDtypeStruct((rows, q_width), jnp.bfloat16),
        in_specs=[vmem, vmem, vmem],
        out_specs=vmem,
        cost_estimate=pl.CostEstimate(
            flops=heads * causal_pairs * pair_flops,
            transcendentals=heads * causal_pairs * (rows // blocks) ** 2,
            bytes_accessed=qkv_slot.size * 2 + rows * q_width * 2,
        ),
    )(qkv_slot, query_pos[:, None], key_pos[None, :])


def on_device(
    hidden, lengths, dealing, norm_gain, w_query, w_key, w_value, query_gain, key_gain, w_out
):
    devices = lax.axis_size("req")
    home_index = lax.axis_index("req")
    slice_index = lax.axis_index("tp")
    tok_rows, features = hidden.shape
    head_dim = query_gain.shape[0]
    out_width = w_out.shape[1]
    q_width = w_query.shape[1]
    k_width = w_key.shape[1]
    slot_len = 4 * tok_rows
    capacity = slot_len // devices
    prompt_total = lengths.shape[0]
    prompt_ids = jnp.arange(prompt_total, dtype=jnp.int32)
    prompt_ends = jnp.cumsum(lengths)
    starts = prompt_ends - lengths
    packed_ids = jnp.arange(tok_rows, dtype=jnp.int32) * devices + home_index
    segment = jnp.sum((packed_ids[:, None] >= prompt_ends[None, :]).astype(jnp.int32), axis=1)
    seg_onehot = (segment[:, None] == prompt_ids[None, :]).astype(jnp.int32)
    positions = packed_ids - jnp.sum(seg_onehot * starts[None, :], axis=1)
    picked = prepare(
        hidden,
        lengths,
        dealing,
        jnp.reshape(home_index, (1,)).astype(jnp.int32),
        norm_gain,
        w_query,
        w_key,
        w_value,
        query_gain,
        key_gain,
        positions,
        capacity,
    )
    picked, lengths, dealing, starts, seg_onehot = lax.optimization_barrier(
        (picked, lengths, dealing, starts, seg_onehot)
    )
    inverse = jnp.zeros((prompt_total,), jnp.int32).at[dealing].set(prompt_ids)
    deal_hot = (dealing[:, None] == prompt_ids[None, :]).astype(jnp.int32)
    dealt_starts = jnp.sum(deal_hot * starts[None, :], axis=1)
    dealt_lengths = jnp.sum(deal_hot * lengths[None, :], axis=1)
    ranks = jnp.arange(capacity, dtype=jnp.int32)
    my_start = lax.dynamic_index_in_dim(dealt_starts, home_index, 0, keepdims=False)
    my_length = lax.dynamic_index_in_dim(dealt_lengths, home_index, 0, keepdims=False)
    roll_shift = jnp.mod(my_start, devices)
    my_slots = jnp.sum(seg_onehot * inverse[None, :], axis=1)
    back_rows = my_slots * capacity + positions // devices
    arrived = lax.all_to_all(
        picked.reshape(devices, capacity, picked.shape[1]),
        "req",
        split_axis=0,
        concat_axis=0,
        tiled=True,
    )
    source_ids = jnp.arange(devices, dtype=jnp.int32)
    arrived_pos = (
        ranks[None, :] * devices + jnp.mod(source_ids[:, None] - my_start, devices)
    ).reshape(-1)
    key_pos = jnp.where(arrived_pos < my_length, arrived_pos, 1 << 30)
    mixture = attend(
        arrived.reshape(slot_len, arrived.shape[2]), arrived_pos, key_pos, q_width, k_width, head_dim
    )
    returned = lax.all_to_all(
        mixture.reshape(devices, capacity, mixture.shape[1]),
        "req",
        split_axis=0,
        concat_axis=0,
        tiled=True,
    )
    attended = jnp.take(returned.reshape(capacity * devices, -1), back_rows, axis=0)
    kv_rows = (
        jnp.roll(arrived[:, :, q_width:], -roll_shift, axis=0)
        .transpose(1, 0, 2)
        .reshape(slot_len, -1)
    )
    kv_cache = jnp.stack([kv_rows[:, :k_width], kv_rows[:, k_width:]])[:, None]
    tp_size = lax.axis_size("tp")
    w_rows = w_out.shape[0] // tp_size
    summed = jnp.dot(
        attended,
        lax.dynamic_slice_in_dim(w_out, slice_index * w_rows, w_rows, 0),
        preferred_element_type=jnp.float32,
    )
    for shift in sorted(range(1, tp_size), key=lambda s: min(s, tp_size - s)):
        passed = lax.ppermute(
            attended, "tp", perm=[(i, (i + shift) % tp_size) for i in range(tp_size)]
        )
        source = jnp.mod(slice_index - shift, tp_size)
        summed = summed + jnp.dot(
            passed,
            lax.dynamic_slice_in_dim(w_out, source * w_rows, w_rows, 0),
            preferred_element_type=jnp.float32,
        )
    branch = lax.optimization_barrier(summed.astype(jnp.bfloat16))
    residual = lax.dynamic_slice_in_dim(hidden, slice_index * out_width, out_width, 1)
    hidden_out = (residual.astype(jnp.float32) + branch.astype(jnp.float32)).astype(jnp.bfloat16)
    return (hidden_out, kv_cache)


def solution(mesh):
    in_specs = (
        P("req", None),
        P(),
        P(),
        P(),
        P(None, "tp"),
        P(None, "tp"),
        P(None, "tp"),
        P(),
        P(),
        P(None, "tp"),
    )
    out_specs = (P("req", "tp"), P(None, "req", None, "tp"))
    return jax.shard_map(
        on_device, mesh=mesh, in_specs=in_specs, out_specs=out_specs, check_vma=False
    )
```

```python
import jax
import jax.numpy as jnp
from jax import lax
from jax.experimental import pallas as pl
from jax.experimental.pallas import tpu as pltpu
from jax.sharding import PartitionSpec as P

EPS = 1e-06
THETA = 1000000.0


def rms_rows(values, scale_gain):
    inv_rms = lax.rsqrt(jnp.mean(values * values, axis=-1, keepdims=True) + EPS)
    return values * inv_rms * scale_gain


def rotate(values, positions):
    features = values.shape[-1]
    half_width = features // 2
    frequency = THETA ** (-(jnp.arange(half_width).astype(jnp.float32) * 2.0) / features)
    angles = positions.astype(jnp.float32)[:, None] * frequency[None, :]
    cosine = jnp.cos(angles)[:, None, :]
    sine_part = jnp.sin(angles)[:, None, :]
    first_half = values[..., :half_width]
    second_half = values[..., half_width:]
    return jnp.concatenate(
        [
            first_half * cosine - second_half * sine_part,
            second_half * cosine + first_half * sine_part,
        ],
        axis=-1,
    )


def project(normed, w_query, w_key, w_value, query_gain, key_gain, positions):
    head_dim = query_gain.shape[0]
    row_count = normed.shape[0]
    query_rows = jnp.dot(normed, w_query, preferred_element_type=jnp.float32).reshape(
        row_count, -1, head_dim
    )
    key_rows = jnp.dot(normed, w_key, preferred_element_type=jnp.float32).reshape(
        row_count, -1, head_dim
    )
    value_rows = jnp.dot(normed, w_value, preferred_element_type=jnp.float32).astype(jnp.bfloat16)
    query_rows = rotate(rms_rows(query_rows, query_gain.astype(jnp.float32)), positions).astype(
        jnp.bfloat16
    )
    key_rows = rotate(rms_rows(key_rows, key_gain.astype(jnp.float32)), positions).astype(
        jnp.bfloat16
    )
    return (query_rows.reshape(row_count, -1), key_rows.reshape(row_count, -1), value_rows)


def prep_kernel(
    lengths_ref,
    dealing_ref,
    home_ref,
    hidden_ref,
    norm_gain_ref,
    wq_ref,
    wk_ref,
    wv_ref,
    qgain_ref,
    kgain_ref,
    cos_ref,
    sin_ref,
    out_ref,
    qkv_ref,
    pick_ref,
    starts_ref,
    *,
    head_dim,
    capacity,
):
    devices = dealing_ref.shape[0]
    prompt_total = lengths_ref.shape[0]
    tok_rows = qkv_ref.shape[0]

    def running(p, total):
        starts_ref[p] = total
        return total + lengths_ref[p]

    lax.fori_loop(0, prompt_total, running, jnp.int32(0))
    home = home_ref[0]
    rank_ids = lax.broadcasted_iota(jnp.int32, (capacity, tok_rows), 0)
    row_gap = lax.broadcasted_iota(jnp.int32, (capacity, tok_rows), 1) - rank_ids

    def pick_rows(d, carry):
        prompt = dealing_ref[d]
        start = starts_ref[prompt]
        length = lengths_ref[prompt]
        first = lax.rem(lax.rem(home - start, devices) + devices, devices)
        first_row = lax.div(start + first - home, devices)
        count = jnp.minimum(lax.div(length - first + devices - 1, devices), capacity)
        hits = (row_gap == first_row) & (rank_ids < count)
        pick_ref[pl.ds(pl.multiple_of(d * capacity, capacity), capacity), :] = hits.astype(
            pick_ref.dtype
        )
        return carry

    lax.fori_loop(0, devices, pick_rows, 0)
    values = hidden_ref[...].astype(jnp.float32)
    inv_rms = lax.rsqrt(jnp.mean(values * values, axis=-1, keepdims=True) + EPS)
    normed = (values * inv_rms * norm_gain_ref[...].astype(jnp.float32)[None, :]).astype(
        jnp.bfloat16
    )
    cosine = cos_ref[...]
    sine = sin_ref[...]
    column = 0
    for w_ref, gain_ref in ((wq_ref, qgain_ref), (wk_ref, kgain_ref)):
        rows = jnp.dot(normed, w_ref[...], preferred_element_type=jnp.float32)
        gain = gain_ref[...].astype(jnp.float32)
        for h in range(rows.shape[1] // head_dim):
            head = rows[:, h * head_dim : (h + 1) * head_dim]
            head_inv = lax.rsqrt(jnp.mean(head * head, axis=-1, keepdims=True) + EPS)
            head = head * head_inv * gain
            swapped = pltpu.roll(head, head_dim // 2, 1)
            qkv_ref[:, column : column + head_dim] = (head * cosine + swapped * sine).astype(
                jnp.bfloat16
            )
            column += head_dim
    v_width = wv_ref.shape[1]
    qkv_ref[:, column : column + v_width] = jnp.dot(
        normed, wv_ref[...], preferred_element_type=jnp.float32
    ).astype(jnp.bfloat16)
    qkv = qkv_ref[...]
    out_rows = out_ref.shape[0]
    block = out_rows // 4
    for b in range(4):
        rows_here = pl.ds(b * block, block)
        out_ref[rows_here, :] = jnp.dot(
            pick_ref[rows_here, :], qkv, preferred_element_type=jnp.float32
        ).astype(out_ref.dtype)


def prepare(
    hidden, lengths, dealing, home, norm_gain, w_query, w_key, w_value, query_gain, key_gain,
    positions, capacity,
):
    tok_rows, features = hidden.shape
    head_dim = query_gain.shape[0]
    half_width = head_dim // 2
    width = w_query.shape[1] + w_key.shape[1] + w_value.shape[1]
    devices = dealing.shape[0]
    out_rows = devices * capacity
    frequency = THETA ** (-(jnp.arange(half_width).astype(jnp.float32) * 2.0) / head_dim)
    frequency = jnp.concatenate([frequency, frequency])
    angles = positions.astype(jnp.float32)[:, None] * frequency[None, :]
    sign = jnp.where(jnp.arange(head_dim) < half_width, -1.0, 1.0).astype(jnp.float32)
    cos_full = jnp.cos(angles)
    sin_signed = jnp.sin(angles) * sign[None, :]
    vmem = pl.BlockSpec(memory_space=pltpu.VMEM)
    smem = pl.BlockSpec(memory_space=pltpu.SMEM)
    return pl.pallas_call(
        lambda *refs: prep_kernel(*refs, head_dim=head_dim, capacity=capacity),
        out_shape=jax.ShapeDtypeStruct((out_rows, width), jnp.bfloat16),
        in_specs=[smem] * 3 + [vmem] * 9,
        out_specs=vmem,
        scratch_shapes=[
            pltpu.VMEM((tok_rows, width), jnp.bfloat16),
            pltpu.VMEM((out_rows, tok_rows), jnp.bfloat16),
            pltpu.SMEM((lengths.shape[0],), jnp.int32),
        ],
        cost_estimate=pl.CostEstimate(
            flops=2 * tok_rows * features * width + 2 * out_rows * tok_rows * width,
            transcendentals=tok_rows * 8,
            bytes_accessed=hidden.size * 2 + features * width * 2 + out_rows * width * 2,
        ),
    )(
        lengths,
        dealing,
        home,
        hidden,
        norm_gain,
        w_query,
        w_key,
        w_value,
        query_gain[None, :],
        key_gain[None, :],
        cos_full,
        sin_signed,
    )


def attention_kernel(qkv_ref, qpos_ref, kpos_ref, out_ref, *, q_width, k_width, head_dim, blocks):
    rows = qkv_ref.shape[0]
    block = rows // blocks
    kv_heads = k_width // head_dim
    group = q_width // head_dim // kv_heads
    scale = head_dim ** (-0.5)
    for i in range(blocks):
        key_rows = rows
        rows_here = pl.ds(i * block, block)
        allowed = kpos_ref[:, :key_rows] <= qpos_ref[rows_here, :]
        for h in range(kv_heads):
            k_col = q_width + h * head_dim
            v_col = q_width + k_width + h * head_dim
            keys = qkv_ref[:key_rows, k_col : k_col + head_dim]
            values = qkv_ref[:key_rows, v_col : v_col + head_dim]
            for g in range(group):
                q_col = (h * group + g) * head_dim
                queries = qkv_ref[rows_here, q_col : q_col + head_dim]
                scores = lax.dot_general(
                    queries,
                    keys,
                    (((1,), (1,)), ((), ())),
                    preferred_element_type=jnp.float32,
                ) * scale
                scores = jnp.where(allowed, scores, -jnp.inf)
                row_max = jnp.max(scores, axis=-1, keepdims=True)
                weights = jnp.exp(scores - row_max)
                weights = (weights / jnp.sum(weights, axis=-1, keepdims=True)).astype(jnp.bfloat16)
                mixed = jnp.dot(weights, values, preferred_element_type=jnp.float32)
                out_ref[rows_here, q_col : q_col + head_dim] = mixed.astype(out_ref.dtype)


def attend(qkv_slot, query_pos, key_pos, q_width, k_width, head_dim):
    rows = qkv_slot.shape[0]
    blocks = 2
    heads = q_width // head_dim
    causal_pairs = blocks * blocks
    pair_flops = 4 * (rows // blocks) ** 2 * head_dim
    vmem = pl.BlockSpec(memory_space=pltpu.VMEM)
    return pl.pallas_call(
        lambda *refs: attention_kernel(
            *refs, q_width=q_width, k_width=k_width, head_dim=head_dim, blocks=blocks
        ),
        out_shape=jax.ShapeDtypeStruct((rows, q_width), jnp.bfloat16),
        in_specs=[vmem, vmem, vmem],
        out_specs=vmem,
        cost_estimate=pl.CostEstimate(
            flops=heads * causal_pairs * pair_flops,
            transcendentals=heads * causal_pairs * (rows // blocks) ** 2,
            bytes_accessed=qkv_slot.size * 2 + rows * q_width * 2,
        ),
    )(qkv_slot, query_pos[:, None], key_pos[None, :])


def on_device(
    hidden, lengths, dealing, norm_gain, w_query, w_key, w_value, query_gain, key_gain, w_out
):
    devices = lax.axis_size("req")
    home_index = lax.axis_index("req")
    slice_index = lax.axis_index("tp")
    tok_rows, features = hidden.shape
    head_dim = query_gain.shape[0]
    out_width = w_out.shape[1]
    q_width = w_query.shape[1]
    k_width = w_key.shape[1]
    slot_len = 4 * tok_rows
    capacity = slot_len // devices
    prompt_total = lengths.shape[0]
    prompt_ids = jnp.arange(prompt_total, dtype=jnp.int32)
    prompt_ends = jnp.cumsum(lengths)
    starts = prompt_ends - lengths
    packed_ids = jnp.arange(tok_rows, dtype=jnp.int32) * devices + home_index
    segment = jnp.sum((packed_ids[:, None] >= prompt_ends[None, :]).astype(jnp.int32), axis=1)
    seg_onehot = (segment[:, None] == prompt_ids[None, :]).astype(jnp.int32)
    positions = packed_ids - jnp.sum(seg_onehot * starts[None, :], axis=1)
    picked = prepare(
        hidden,
        lengths,
        dealing,
        jnp.reshape(home_index, (1,)).astype(jnp.int32),
        norm_gain,
        w_query,
        w_key,
        w_value,
        query_gain,
        key_gain,
        positions,
        capacity,
    )
    picked, lengths, dealing, starts, seg_onehot = lax.optimization_barrier(
        (picked, lengths, dealing, starts, seg_onehot)
    )
    inverse = jnp.zeros((prompt_total,), jnp.int32).at[dealing].set(prompt_ids)
    deal_hot = (dealing[:, None] == prompt_ids[None, :]).astype(jnp.int32)
    dealt_starts = jnp.sum(deal_hot * starts[None, :], axis=1)
    dealt_lengths = jnp.sum(deal_hot * lengths[None, :], axis=1)
    ranks = jnp.arange(capacity, dtype=jnp.int32)
    my_start = lax.dynamic_index_in_dim(dealt_starts, home_index, 0, keepdims=False)
    my_length = lax.dynamic_index_in_dim(dealt_lengths, home_index, 0, keepdims=False)
    roll_shift = jnp.mod(my_start, devices)
    my_slots = jnp.sum(seg_onehot * inverse[None, :], axis=1)
    back_rows = my_slots * capacity + positions // devices
    arrived = lax.all_to_all(
        picked.reshape(devices, capacity, picked.shape[1]),
        "req",
        split_axis=0,
        concat_axis=0,
        tiled=True,
    )
    source_ids = jnp.arange(devices, dtype=jnp.int32)
    arrived_pos = (
        ranks[None, :] * devices + jnp.mod(source_ids[:, None] - my_start, devices)
    ).reshape(-1)
    key_pos = jnp.where(arrived_pos < my_length, arrived_pos, 1 << 30)
    mixture = attend(
        arrived.reshape(slot_len, arrived.shape[2]), arrived_pos, key_pos, q_width, k_width, head_dim
    )
    returned = lax.all_to_all(
        mixture.reshape(devices, capacity, mixture.shape[1]),
        "req",
        split_axis=0,
        concat_axis=0,
        tiled=True,
    )
    attended = jnp.take(returned.reshape(capacity * devices, -1), back_rows, axis=0)
    kv_rows = (
        jnp.roll(arrived[:, :, q_width:], -roll_shift, axis=0)
        .transpose(1, 0, 2)
        .reshape(slot_len, -1)
    )
    kv_cache = jnp.stack([kv_rows[:, :k_width], kv_rows[:, k_width:]])[:, None]
    tp_size = lax.axis_size("tp")
    w_rows = w_out.shape[0] // tp_size
    summed = jnp.dot(
        attended,
        lax.dynamic_slice_in_dim(w_out, slice_index * w_rows, w_rows, 0),
        preferred_element_type=jnp.float32,
    )
    for shift in sorted(range(1, tp_size), key=lambda s: (min(s, tp_size - s), -s)):
        passed = lax.ppermute(
            attended, "tp", perm=[(i, (i + shift) % tp_size) for i in range(tp_size)]
        )
        source = jnp.mod(slice_index - shift, tp_size)
        summed = summed + jnp.dot(
            passed,
            lax.dynamic_slice_in_dim(w_out, source * w_rows, w_rows, 0),
            preferred_element_type=jnp.float32,
        )
    branch = lax.optimization_barrier(summed.astype(jnp.bfloat16))
    residual = lax.dynamic_slice_in_dim(hidden, slice_index * out_width, out_width, 1)
    hidden_out = (residual.astype(jnp.float32) + branch.astype(jnp.float32)).astype(jnp.bfloat16)
    return (hidden_out, kv_cache)


def solution(mesh):
    in_specs = (
        P("req", None),
        P(),
        P(),
        P(),
        P(None, "tp"),
        P(None, "tp"),
        P(None, "tp"),
        P(),
        P(),
        P(None, "tp"),
    )
    out_specs = (P("req", "tp"), P(None, "req", None, "tp"))
    return jax.shard_map(
        on_device, mesh=mesh, in_specs=in_specs, out_specs=out_specs, check_vma=False
    )
```

```python
import jax
import jax.numpy as jnp
from jax import lax
from jax.experimental import pallas as pl
from jax.experimental.pallas import tpu as pltpu
from jax.sharding import PartitionSpec as P

EPS = 1e-06
THETA = 1000000.0


def rms_rows(values, scale_gain):
    inv_rms = lax.rsqrt(jnp.mean(values * values, axis=-1, keepdims=True) + EPS)
    return values * inv_rms * scale_gain


def rotate(values, positions):
    features = values.shape[-1]
    half_width = features // 2
    frequency = THETA ** (-(jnp.arange(half_width).astype(jnp.float32) * 2.0) / features)
    angles = positions.astype(jnp.float32)[:, None] * frequency[None, :]
    cosine = jnp.cos(angles)[:, None, :]
    sine_part = jnp.sin(angles)[:, None, :]
    first_half = values[..., :half_width]
    second_half = values[..., half_width:]
    return jnp.concatenate(
        [
            first_half * cosine - second_half * sine_part,
            second_half * cosine + first_half * sine_part,
        ],
        axis=-1,
    )


def project(normed, w_query, w_key, w_value, query_gain, key_gain, positions):
    head_dim = query_gain.shape[0]
    row_count = normed.shape[0]
    query_rows = jnp.dot(normed, w_query, preferred_element_type=jnp.float32).reshape(
        row_count, -1, head_dim
    )
    key_rows = jnp.dot(normed, w_key, preferred_element_type=jnp.float32).reshape(
        row_count, -1, head_dim
    )
    value_rows = jnp.dot(normed, w_value, preferred_element_type=jnp.float32).astype(jnp.bfloat16)
    query_rows = rotate(rms_rows(query_rows, query_gain.astype(jnp.float32)), positions).astype(
        jnp.bfloat16
    )
    key_rows = rotate(rms_rows(key_rows, key_gain.astype(jnp.float32)), positions).astype(
        jnp.bfloat16
    )
    return (query_rows.reshape(row_count, -1), key_rows.reshape(row_count, -1), value_rows)


def prep_kernel(
    lengths_ref,
    dealing_ref,
    home_ref,
    hidden_ref,
    norm_gain_ref,
    wq_ref,
    wk_ref,
    wv_ref,
    qgain_ref,
    kgain_ref,
    cos_ref,
    sin_ref,
    out_ref,
    qkv_ref,
    pick_ref,
    starts_ref,
    *,
    head_dim,
    capacity,
):
    devices = dealing_ref.shape[0]
    prompt_total = lengths_ref.shape[0]
    tok_rows = qkv_ref.shape[0]

    def running(p, total):
        starts_ref[p] = total
        return total + lengths_ref[p]

    lax.fori_loop(0, prompt_total, running, jnp.int32(0))
    home = home_ref[0]
    rank_ids = lax.broadcasted_iota(jnp.int32, (capacity, tok_rows), 0)
    row_gap = lax.broadcasted_iota(jnp.int32, (capacity, tok_rows), 1) - rank_ids

    def pick_rows(d, carry):
        prompt = dealing_ref[d]
        start = starts_ref[prompt]
        length = lengths_ref[prompt]
        first = lax.rem(lax.rem(home - start, devices) + devices, devices)
        first_row = lax.div(start + first - home, devices)
        count = jnp.minimum(lax.div(length - first + devices - 1, devices), capacity)
        hits = (row_gap == first_row) & (rank_ids < count)
        pick_ref[pl.ds(pl.multiple_of(d * capacity, capacity), capacity), :] = hits.astype(
            pick_ref.dtype
        )
        return carry

    lax.fori_loop(0, devices, pick_rows, 0)
    values = hidden_ref[...].astype(jnp.float32)
    inv_rms = lax.rsqrt(jnp.mean(values * values, axis=-1, keepdims=True) + EPS)
    normed = (values * inv_rms * norm_gain_ref[...].astype(jnp.float32)[None, :]).astype(
        jnp.bfloat16
    )
    cosine = cos_ref[...]
    sine = sin_ref[...]
    column = 0
    for w_ref, gain_ref in ((wq_ref, qgain_ref), (wk_ref, kgain_ref)):
        rows = jnp.dot(normed, w_ref[...], preferred_element_type=jnp.float32)
        gain = gain_ref[...].astype(jnp.float32)
        for h in range(rows.shape[1] // head_dim):
            head = rows[:, h * head_dim : (h + 1) * head_dim]
            head_inv = lax.rsqrt(jnp.mean(head * head, axis=-1, keepdims=True) + EPS)
            head = head * head_inv * gain
            swapped = pltpu.roll(head, head_dim // 2, 1)
            qkv_ref[:, column : column + head_dim] = (head * cosine + swapped * sine).astype(
                jnp.bfloat16
            )
            column += head_dim
    v_width = wv_ref.shape[1]
    qkv_ref[:, column : column + v_width] = jnp.dot(
        normed, wv_ref[...], preferred_element_type=jnp.float32
    ).astype(jnp.bfloat16)
    qkv = qkv_ref[...]
    out_rows = out_ref.shape[0]
    block = out_rows // 4
    for b in range(4):
        rows_here = pl.ds(b * block, block)
        out_ref[rows_here, :] = jnp.dot(
            pick_ref[rows_here, :], qkv, preferred_element_type=jnp.float32
        ).astype(out_ref.dtype)


def prepare(
    hidden, lengths, dealing, home, norm_gain, w_query, w_key, w_value, query_gain, key_gain,
    positions, capacity,
):
    tok_rows, features = hidden.shape
    head_dim = query_gain.shape[0]
    half_width = head_dim // 2
    width = w_query.shape[1] + w_key.shape[1] + w_value.shape[1]
    devices = dealing.shape[0]
    out_rows = devices * capacity
    frequency = THETA ** (-(jnp.arange(half_width).astype(jnp.float32) * 2.0) / head_dim)
    frequency = jnp.concatenate([frequency, frequency])
    angles = positions.astype(jnp.float32)[:, None] * frequency[None, :]
    sign = jnp.where(jnp.arange(head_dim) < half_width, -1.0, 1.0).astype(jnp.float32)
    cos_full = jnp.cos(angles)
    sin_signed = jnp.sin(angles) * sign[None, :]
    vmem = pl.BlockSpec(memory_space=pltpu.VMEM)
    smem = pl.BlockSpec(memory_space=pltpu.SMEM)
    return pl.pallas_call(
        lambda *refs: prep_kernel(*refs, head_dim=head_dim, capacity=capacity),
        out_shape=jax.ShapeDtypeStruct((out_rows, width), jnp.bfloat16),
        in_specs=[smem] * 3 + [vmem] * 9,
        out_specs=vmem,
        scratch_shapes=[
            pltpu.VMEM((tok_rows, width), jnp.bfloat16),
            pltpu.VMEM((out_rows, tok_rows), jnp.bfloat16),
            pltpu.SMEM((lengths.shape[0],), jnp.int32),
        ],
        cost_estimate=pl.CostEstimate(
            flops=2 * tok_rows * features * width + 2 * out_rows * tok_rows * width,
            transcendentals=tok_rows * 8,
            bytes_accessed=hidden.size * 2 + features * width * 2 + out_rows * width * 2,
        ),
    )(
        lengths,
        dealing,
        home,
        hidden,
        norm_gain,
        w_query,
        w_key,
        w_value,
        query_gain[None, :],
        key_gain[None, :],
        cos_full,
        sin_signed,
    )


def attention_kernel(qkv_ref, qpos_ref, kpos_ref, out_ref, *, q_width, k_width, head_dim, blocks):
    rows = qkv_ref.shape[0]
    block = rows // blocks
    kv_heads = k_width // head_dim
    group = q_width // head_dim // kv_heads
    scale = head_dim ** (-0.5)
    for i in range(blocks):
        key_rows = rows
        rows_here = pl.ds(i * block, block)
        allowed = kpos_ref[:, :key_rows] <= qpos_ref[rows_here, :]
        for h in range(kv_heads):
            k_col = q_width + h * head_dim
            v_col = q_width + k_width + h * head_dim
            keys = qkv_ref[:key_rows, k_col : k_col + head_dim]
            values = qkv_ref[:key_rows, v_col : v_col + head_dim]
            for g in range(group):
                q_col = (h * group + g) * head_dim
                queries = qkv_ref[rows_here, q_col : q_col + head_dim]
                scores = lax.dot_general(
                    queries,
                    keys,
                    (((1,), (1,)), ((), ())),
                    preferred_element_type=jnp.float32,
                ) * scale
                scores = jnp.where(allowed, scores, -jnp.inf)
                row_max = jnp.max(scores, axis=-1, keepdims=True)
                weights = jnp.exp(scores - row_max)
                weights = (weights / jnp.sum(weights, axis=-1, keepdims=True)).astype(jnp.bfloat16)
                mixed = jnp.dot(weights, values, preferred_element_type=jnp.float32)
                out_ref[rows_here, q_col : q_col + head_dim] = mixed.astype(out_ref.dtype)


def attend(qkv_slot, query_pos, key_pos, q_width, k_width, head_dim):
    rows = qkv_slot.shape[0]
    blocks = 2
    heads = q_width // head_dim
    causal_pairs = blocks * blocks
    pair_flops = 4 * (rows // blocks) ** 2 * head_dim
    vmem = pl.BlockSpec(memory_space=pltpu.VMEM)
    return pl.pallas_call(
        lambda *refs: attention_kernel(
            *refs, q_width=q_width, k_width=k_width, head_dim=head_dim, blocks=blocks
        ),
        out_shape=jax.ShapeDtypeStruct((rows, q_width), jnp.bfloat16),
        in_specs=[vmem, vmem, vmem],
        out_specs=vmem,
        cost_estimate=pl.CostEstimate(
            flops=heads * causal_pairs * pair_flops,
            transcendentals=heads * causal_pairs * (rows // blocks) ** 2,
            bytes_accessed=qkv_slot.size * 2 + rows * q_width * 2,
        ),
    )(qkv_slot, query_pos[:, None], key_pos[None, :])


def on_device(
    hidden, lengths, dealing, norm_gain, w_query, w_key, w_value, query_gain, key_gain, w_out
):
    devices = lax.axis_size("req")
    home_index = lax.axis_index("req")
    slice_index = lax.axis_index("tp")
    tok_rows, features = hidden.shape
    head_dim = query_gain.shape[0]
    out_width = w_out.shape[1]
    q_width = w_query.shape[1]
    k_width = w_key.shape[1]
    slot_len = 4 * tok_rows
    capacity = slot_len // devices
    prompt_total = lengths.shape[0]
    prompt_ids = jnp.arange(prompt_total, dtype=jnp.int32)
    prompt_ends = jnp.cumsum(lengths)
    starts = prompt_ends - lengths
    packed_ids = jnp.arange(tok_rows, dtype=jnp.int32) * devices + home_index
    segment = jnp.sum((packed_ids[:, None] >= prompt_ends[None, :]).astype(jnp.int32), axis=1)
    seg_onehot = (segment[:, None] == prompt_ids[None, :]).astype(jnp.int32)
    positions = packed_ids - jnp.sum(seg_onehot * starts[None, :], axis=1)
    picked = prepare(
        hidden,
        lengths,
        dealing,
        jnp.reshape(home_index, (1,)).astype(jnp.int32),
        norm_gain,
        w_query,
        w_key,
        w_value,
        query_gain,
        key_gain,
        positions,
        capacity,
    )
    picked, lengths, dealing, starts, seg_onehot = lax.optimization_barrier(
        (picked, lengths, dealing, starts, seg_onehot)
    )
    inverse = jnp.zeros((prompt_total,), jnp.int32).at[dealing].set(prompt_ids)
    deal_hot = (dealing[:, None] == prompt_ids[None, :]).astype(jnp.int32)
    dealt_starts = jnp.sum(deal_hot * starts[None, :], axis=1)
    dealt_lengths = jnp.sum(deal_hot * lengths[None, :], axis=1)
    ranks = jnp.arange(capacity, dtype=jnp.int32)
    my_start = lax.dynamic_index_in_dim(dealt_starts, home_index, 0, keepdims=False)
    my_length = lax.dynamic_index_in_dim(dealt_lengths, home_index, 0, keepdims=False)
    roll_shift = jnp.mod(my_start, devices)
    my_slots = jnp.sum(seg_onehot * inverse[None, :], axis=1)
    back_rows = my_slots * capacity + positions // devices
    arrived = lax.all_to_all(
        picked.reshape(devices, capacity, picked.shape[1]),
        "req",
        split_axis=0,
        concat_axis=0,
        tiled=True,
    )
    source_ids = jnp.arange(devices, dtype=jnp.int32)
    arrived_pos = (
        ranks[None, :] * devices + jnp.mod(source_ids[:, None] - my_start, devices)
    ).reshape(-1)
    key_pos = jnp.where(arrived_pos < my_length, arrived_pos, 1 << 30)
    mixture = attend(
        arrived.reshape(slot_len, arrived.shape[2]), arrived_pos, key_pos, q_width, k_width, head_dim
    )
    returned = lax.all_to_all(
        mixture.reshape(devices, capacity, mixture.shape[1]),
        "req",
        split_axis=0,
        concat_axis=0,
        tiled=True,
    )
    attended = jnp.take(returned.reshape(capacity * devices, -1), back_rows, axis=0)
    kv_rows = (
        jnp.roll(arrived[:, :, q_width:], -roll_shift, axis=0)
        .transpose(1, 0, 2)
        .reshape(slot_len, -1)
    )
    kv_cache = jnp.stack([kv_rows[:, :k_width], kv_rows[:, k_width:]])[:, None]
    tp_size = lax.axis_size("tp")
    w_rows = w_out.shape[0] // tp_size
    passes = []
    for shift in sorted(range(1, tp_size), key=lambda s: min(s, tp_size - s)):
        passed = lax.ppermute(
            attended, "tp", perm=[(i, (i + shift) % tp_size) for i in range(tp_size)]
        )
        passes.append((passed, jnp.mod(slice_index - shift, tp_size)))
    passes.append((attended, slice_index))
    summed = None
    for passed, source in passes:
        product = jnp.dot(
            passed,
            lax.dynamic_slice_in_dim(w_out, source * w_rows, w_rows, 0),
            preferred_element_type=jnp.float32,
        )
        summed = product if summed is None else summed + product
    branch = lax.optimization_barrier(summed.astype(jnp.bfloat16))
    residual = lax.dynamic_slice_in_dim(hidden, slice_index * out_width, out_width, 1)
    hidden_out = (residual.astype(jnp.float32) + branch.astype(jnp.float32)).astype(jnp.bfloat16)
    return (hidden_out, kv_cache)


def solution(mesh):
    in_specs = (
        P("req", None),
        P(),
        P(),
        P(),
        P(None, "tp"),
        P(None, "tp"),
        P(None, "tp"),
        P(),
        P(),
        P(None, "tp"),
    )
    out_specs = (P("req", "tp"), P(None, "req", None, "tp"))
    return jax.shard_map(
        on_device, mesh=mesh, in_specs=in_specs, out_specs=out_specs, check_vma=False
    )
```

```python
import jax
import jax.numpy as jnp
from jax import lax
from jax.experimental import pallas as pl
from jax.experimental.pallas import tpu as pltpu
from jax.sharding import PartitionSpec as P

EPS = 1e-06
THETA = 1000000.0


def rms_rows(values, scale_gain):
    inv_rms = lax.rsqrt(jnp.mean(values * values, axis=-1, keepdims=True) + EPS)
    return values * inv_rms * scale_gain


def rotate(values, positions):
    features = values.shape[-1]
    half_width = features // 2
    frequency = THETA ** (-(jnp.arange(half_width).astype(jnp.float32) * 2.0) / features)
    angles = positions.astype(jnp.float32)[:, None] * frequency[None, :]
    cosine = jnp.cos(angles)[:, None, :]
    sine_part = jnp.sin(angles)[:, None, :]
    first_half = values[..., :half_width]
    second_half = values[..., half_width:]
    return jnp.concatenate(
        [
            first_half * cosine - second_half * sine_part,
            second_half * cosine + first_half * sine_part,
        ],
        axis=-1,
    )


def project(normed, w_query, w_key, w_value, query_gain, key_gain, positions):
    head_dim = query_gain.shape[0]
    row_count = normed.shape[0]
    query_rows = jnp.dot(normed, w_query, preferred_element_type=jnp.float32).reshape(
        row_count, -1, head_dim
    )
    key_rows = jnp.dot(normed, w_key, preferred_element_type=jnp.float32).reshape(
        row_count, -1, head_dim
    )
    value_rows = jnp.dot(normed, w_value, preferred_element_type=jnp.float32).astype(jnp.bfloat16)
    query_rows = rotate(rms_rows(query_rows, query_gain.astype(jnp.float32)), positions).astype(
        jnp.bfloat16
    )
    key_rows = rotate(rms_rows(key_rows, key_gain.astype(jnp.float32)), positions).astype(
        jnp.bfloat16
    )
    return (query_rows.reshape(row_count, -1), key_rows.reshape(row_count, -1), value_rows)


def prep_kernel(
    lengths_ref,
    dealing_ref,
    home_ref,
    hidden_ref,
    norm_gain_ref,
    wq_ref,
    wk_ref,
    wv_ref,
    qgain_ref,
    kgain_ref,
    cos_ref,
    sin_ref,
    out_ref,
    qkv_ref,
    pick_ref,
    starts_ref,
    *,
    head_dim,
    capacity,
):
    devices = dealing_ref.shape[0]
    prompt_total = lengths_ref.shape[0]
    tok_rows = qkv_ref.shape[0]

    def running(p, total):
        starts_ref[p] = total
        return total + lengths_ref[p]

    lax.fori_loop(0, prompt_total, running, jnp.int32(0))
    home = home_ref[0]
    rank_ids = lax.broadcasted_iota(jnp.int32, (capacity, tok_rows), 0)
    row_gap = lax.broadcasted_iota(jnp.int32, (capacity, tok_rows), 1) - rank_ids

    def pick_rows(d, carry):
        prompt = dealing_ref[d]
        start = starts_ref[prompt]
        length = lengths_ref[prompt]
        first = lax.rem(lax.rem(home - start, devices) + devices, devices)
        first_row = lax.div(start + first - home, devices)
        count = jnp.minimum(lax.div(length - first + devices - 1, devices), capacity)
        hits = (row_gap == first_row) & (rank_ids < count)
        pick_ref[pl.ds(pl.multiple_of(d * capacity, capacity), capacity), :] = hits.astype(
            pick_ref.dtype
        )
        return carry

    lax.fori_loop(0, devices, pick_rows, 0)
    values = hidden_ref[...].astype(jnp.float32)
    inv_rms = lax.rsqrt(jnp.mean(values * values, axis=-1, keepdims=True) + EPS)
    normed = (values * inv_rms * norm_gain_ref[...].astype(jnp.float32)[None, :]).astype(
        jnp.bfloat16
    )
    cosine = cos_ref[...]
    sine = sin_ref[...]
    column = 0
    for w_ref, gain_ref in ((wq_ref, qgain_ref), (wk_ref, kgain_ref)):
        rows = jnp.dot(normed, w_ref[...], preferred_element_type=jnp.float32)
        gain = gain_ref[...].astype(jnp.float32)
        for h in range(rows.shape[1] // head_dim):
            head = rows[:, h * head_dim : (h + 1) * head_dim]
            head_inv = lax.rsqrt(jnp.mean(head * head, axis=-1, keepdims=True) + EPS)
            head = head * head_inv * gain
            swapped = pltpu.roll(head, head_dim // 2, 1)
            qkv_ref[:, column : column + head_dim] = (head * cosine + swapped * sine).astype(
                jnp.bfloat16
            )
            column += head_dim
    v_width = wv_ref.shape[1]
    qkv_ref[:, column : column + v_width] = jnp.dot(
        normed, wv_ref[...], preferred_element_type=jnp.float32
    ).astype(jnp.bfloat16)
    qkv = qkv_ref[...]
    out_rows = out_ref.shape[0]
    block = out_rows // 4
    for b in range(4):
        rows_here = pl.ds(b * block, block)
        out_ref[rows_here, :] = jnp.dot(
            pick_ref[rows_here, :], qkv, preferred_element_type=jnp.float32
        ).astype(out_ref.dtype)


def prepare(
    hidden, lengths, dealing, home, norm_gain, w_query, w_key, w_value, query_gain, key_gain,
    positions, capacity,
):
    tok_rows, features = hidden.shape
    head_dim = query_gain.shape[0]
    half_width = head_dim // 2
    width = w_query.shape[1] + w_key.shape[1] + w_value.shape[1]
    devices = dealing.shape[0]
    out_rows = devices * capacity
    frequency = THETA ** (-(jnp.arange(half_width).astype(jnp.float32) * 2.0) / head_dim)
    frequency = jnp.concatenate([frequency, frequency])
    angles = positions.astype(jnp.float32)[:, None] * frequency[None, :]
    sign = jnp.where(jnp.arange(head_dim) < half_width, -1.0, 1.0).astype(jnp.float32)
    cos_full = jnp.cos(angles)
    sin_signed = jnp.sin(angles) * sign[None, :]
    vmem = pl.BlockSpec(memory_space=pltpu.VMEM)
    smem = pl.BlockSpec(memory_space=pltpu.SMEM)
    return pl.pallas_call(
        lambda *refs: prep_kernel(*refs, head_dim=head_dim, capacity=capacity),
        out_shape=jax.ShapeDtypeStruct((out_rows, width), jnp.bfloat16),
        in_specs=[smem] * 3 + [vmem] * 9,
        out_specs=vmem,
        scratch_shapes=[
            pltpu.VMEM((tok_rows, width), jnp.bfloat16),
            pltpu.VMEM((out_rows, tok_rows), jnp.bfloat16),
            pltpu.SMEM((lengths.shape[0],), jnp.int32),
        ],
        cost_estimate=pl.CostEstimate(
            flops=2 * tok_rows * features * width + 2 * out_rows * tok_rows * width,
            transcendentals=tok_rows * 8,
            bytes_accessed=hidden.size * 2 + features * width * 2 + out_rows * width * 2,
        ),
    )(
        lengths,
        dealing,
        home,
        hidden,
        norm_gain,
        w_query,
        w_key,
        w_value,
        query_gain[None, :],
        key_gain[None, :],
        cos_full,
        sin_signed,
    )


def attention_kernel(qkv_ref, qpos_ref, kpos_ref, out_ref, *, q_width, k_width, head_dim, blocks):
    rows = qkv_ref.shape[0]
    block = rows // blocks
    kv_heads = k_width // head_dim
    group = q_width // head_dim // kv_heads
    scale = head_dim ** (-0.5)
    for i in range(blocks):
        key_rows = rows
        rows_here = pl.ds(i * block, block)
        allowed = kpos_ref[:, :key_rows] <= qpos_ref[rows_here, :]
        for h in range(kv_heads):
            k_col = q_width + h * head_dim
            v_col = q_width + k_width + h * head_dim
            keys = qkv_ref[:key_rows, k_col : k_col + head_dim]
            values = qkv_ref[:key_rows, v_col : v_col + head_dim]
            for g in range(group):
                q_col = (h * group + g) * head_dim
                queries = qkv_ref[rows_here, q_col : q_col + head_dim]
                scores = lax.dot_general(
                    queries,
                    keys,
                    (((1,), (1,)), ((), ())),
                    preferred_element_type=jnp.float32,
                ) * scale
                scores = jnp.where(allowed, scores, -jnp.inf)
                row_max = jnp.max(scores, axis=-1, keepdims=True)
                weights = jnp.exp(scores - row_max)
                weights = (weights / jnp.sum(weights, axis=-1, keepdims=True)).astype(jnp.bfloat16)
                mixed = jnp.dot(weights, values, preferred_element_type=jnp.float32)
                out_ref[rows_here, q_col : q_col + head_dim] = mixed.astype(out_ref.dtype)


def attend(qkv_slot, query_pos, key_pos, q_width, k_width, head_dim):
    rows = qkv_slot.shape[0]
    blocks = 2
    heads = q_width // head_dim
    causal_pairs = blocks * blocks
    pair_flops = 4 * (rows // blocks) ** 2 * head_dim
    vmem = pl.BlockSpec(memory_space=pltpu.VMEM)
    return pl.pallas_call(
        lambda *refs: attention_kernel(
            *refs, q_width=q_width, k_width=k_width, head_dim=head_dim, blocks=blocks
        ),
        out_shape=jax.ShapeDtypeStruct((rows, q_width), jnp.bfloat16),
        in_specs=[vmem, vmem, vmem],
        out_specs=vmem,
        cost_estimate=pl.CostEstimate(
            flops=heads * causal_pairs * pair_flops,
            transcendentals=heads * causal_pairs * (rows // blocks) ** 2,
            bytes_accessed=qkv_slot.size * 2 + rows * q_width * 2,
        ),
    )(qkv_slot, query_pos[:, None], key_pos[None, :])


def on_device(
    hidden, lengths, dealing, norm_gain, w_query, w_key, w_value, query_gain, key_gain, w_out
):
    devices = lax.axis_size("req")
    home_index = lax.axis_index("req")
    slice_index = lax.axis_index("tp")
    tok_rows, features = hidden.shape
    head_dim = query_gain.shape[0]
    out_width = w_out.shape[1]
    q_width = w_query.shape[1]
    k_width = w_key.shape[1]
    slot_len = 4 * tok_rows
    capacity = slot_len // devices
    prompt_total = lengths.shape[0]
    prompt_ids = jnp.arange(prompt_total, dtype=jnp.int32)
    prompt_ends = jnp.cumsum(lengths)
    starts = prompt_ends - lengths
    packed_ids = jnp.arange(tok_rows, dtype=jnp.int32) * devices + home_index
    segment = jnp.sum((packed_ids[:, None] >= prompt_ends[None, :]).astype(jnp.int32), axis=1)
    seg_onehot = (segment[:, None] == prompt_ids[None, :]).astype(jnp.int32)
    positions = packed_ids - jnp.sum(seg_onehot * starts[None, :], axis=1)
    picked = prepare(
        hidden,
        lengths,
        dealing,
        jnp.reshape(home_index, (1,)).astype(jnp.int32),
        norm_gain,
        w_query,
        w_key,
        w_value,
        query_gain,
        key_gain,
        positions,
        capacity,
    )
    picked, lengths, dealing, starts, seg_onehot = lax.optimization_barrier(
        (picked, lengths, dealing, starts, seg_onehot)
    )
    inverse = jnp.zeros((prompt_total,), jnp.int32).at[dealing].set(prompt_ids)
    deal_hot = (dealing[:, None] == prompt_ids[None, :]).astype(jnp.int32)
    dealt_starts = jnp.sum(deal_hot * starts[None, :], axis=1)
    dealt_lengths = jnp.sum(deal_hot * lengths[None, :], axis=1)
    ranks = jnp.arange(capacity, dtype=jnp.int32)
    my_start = lax.dynamic_index_in_dim(dealt_starts, home_index, 0, keepdims=False)
    my_length = lax.dynamic_index_in_dim(dealt_lengths, home_index, 0, keepdims=False)
    roll_shift = jnp.mod(my_start, devices)
    my_slots = jnp.sum(seg_onehot * inverse[None, :], axis=1)
    back_rows = my_slots * capacity + positions // devices
    arrived = lax.all_to_all(
        picked.reshape(devices, capacity, picked.shape[1]),
        "req",
        split_axis=0,
        concat_axis=0,
        tiled=True,
    )
    source_ids = jnp.arange(devices, dtype=jnp.int32)
    arrived_pos = (
        ranks[None, :] * devices + jnp.mod(source_ids[:, None] - my_start, devices)
    ).reshape(-1)
    key_pos = jnp.where(arrived_pos < my_length, arrived_pos, 1 << 30)
    mixture = attend(
        arrived.reshape(slot_len, arrived.shape[2]), arrived_pos, key_pos, q_width, k_width, head_dim
    )
    returned = lax.all_to_all(
        mixture.reshape(devices, capacity, mixture.shape[1]),
        "req",
        split_axis=0,
        concat_axis=0,
        tiled=True,
    )
    back_hot = (
        back_rows[:, None] == jnp.arange(capacity * devices, dtype=jnp.int32)[None, :]
    ).astype(returned.dtype)
    attended = jnp.dot(
        back_hot, returned.reshape(capacity * devices, -1), preferred_element_type=jnp.float32
    ).astype(returned.dtype)
    kv_rows = (
        jnp.roll(arrived[:, :, q_width:], -roll_shift, axis=0)
        .transpose(1, 0, 2)
        .reshape(slot_len, -1)
    )
    kv_cache = jnp.stack([kv_rows[:, :k_width], kv_rows[:, k_width:]])[:, None]
    tp_size = lax.axis_size("tp")
    w_rows = w_out.shape[0] // tp_size
    passes = []
    for shift in sorted(range(1, tp_size), key=lambda s: min(s, tp_size - s)):
        passed = lax.ppermute(
            attended, "tp", perm=[(i, (i + shift) % tp_size) for i in range(tp_size)]
        )
        passes.append((passed, jnp.mod(slice_index - shift, tp_size)))
    passes.append((attended, slice_index))
    summed = None
    for passed, source in passes:
        product = jnp.dot(
            passed,
            lax.dynamic_slice_in_dim(w_out, source * w_rows, w_rows, 0),
            preferred_element_type=jnp.float32,
        )
        summed = product if summed is None else summed + product
    branch = lax.optimization_barrier(summed.astype(jnp.bfloat16))
    residual = lax.dynamic_slice_in_dim(hidden, slice_index * out_width, out_width, 1)
    hidden_out = (residual.astype(jnp.float32) + branch.astype(jnp.float32)).astype(jnp.bfloat16)
    return (hidden_out, kv_cache)


def solution(mesh):
    in_specs = (
        P("req", None),
        P(),
        P(),
        P(),
        P(None, "tp"),
        P(None, "tp"),
        P(None, "tp"),
        P(),
        P(),
        P(None, "tp"),
    )
    out_specs = (P("req", "tp"), P(None, "req", None, "tp"))
    return jax.shard_map(
        on_device, mesh=mesh, in_specs=in_specs, out_specs=out_specs, check_vma=False
    )
```

```python
import jax
import jax.numpy as jnp
from jax import lax
from jax.experimental import pallas as pl
from jax.experimental.pallas import tpu as pltpu
from jax.sharding import PartitionSpec as P

EPS = 1e-06
THETA = 1000000.0


def rms_rows(values, scale_gain):
    inv_rms = lax.rsqrt(jnp.mean(values * values, axis=-1, keepdims=True) + EPS)
    return values * inv_rms * scale_gain


def rotate(values, positions):
    features = values.shape[-1]
    half_width = features // 2
    frequency = THETA ** (-(jnp.arange(half_width).astype(jnp.float32) * 2.0) / features)
    angles = positions.astype(jnp.float32)[:, None] * frequency[None, :]
    cosine = jnp.cos(angles)[:, None, :]
    sine_part = jnp.sin(angles)[:, None, :]
    first_half = values[..., :half_width]
    second_half = values[..., half_width:]
    return jnp.concatenate(
        [
            first_half * cosine - second_half * sine_part,
            second_half * cosine + first_half * sine_part,
        ],
        axis=-1,
    )


def project(normed, w_query, w_key, w_value, query_gain, key_gain, positions):
    head_dim = query_gain.shape[0]
    row_count = normed.shape[0]
    query_rows = jnp.dot(normed, w_query, preferred_element_type=jnp.float32).reshape(
        row_count, -1, head_dim
    )
    key_rows = jnp.dot(normed, w_key, preferred_element_type=jnp.float32).reshape(
        row_count, -1, head_dim
    )
    value_rows = jnp.dot(normed, w_value, preferred_element_type=jnp.float32).astype(jnp.bfloat16)
    query_rows = rotate(rms_rows(query_rows, query_gain.astype(jnp.float32)), positions).astype(
        jnp.bfloat16
    )
    key_rows = rotate(rms_rows(key_rows, key_gain.astype(jnp.float32)), positions).astype(
        jnp.bfloat16
    )
    return (query_rows.reshape(row_count, -1), key_rows.reshape(row_count, -1), value_rows)


def prep_kernel(
    lengths_ref,
    dealing_ref,
    home_ref,
    hidden_ref,
    norm_gain_ref,
    wq_ref,
    wk_ref,
    wv_ref,
    qgain_ref,
    kgain_ref,
    cos_ref,
    sin_ref,
    out_ref,
    qkv_ref,
    pick_ref,
    starts_ref,
    *,
    head_dim,
    capacity,
):
    devices = dealing_ref.shape[0]
    prompt_total = lengths_ref.shape[0]
    tok_rows = qkv_ref.shape[0]

    def running(p, total):
        starts_ref[p] = total
        return total + lengths_ref[p]

    lax.fori_loop(0, prompt_total, running, jnp.int32(0))
    home = home_ref[0]
    rank_ids = lax.broadcasted_iota(jnp.int32, (capacity, tok_rows), 0)
    row_gap = lax.broadcasted_iota(jnp.int32, (capacity, tok_rows), 1) - rank_ids

    def pick_rows(d, carry):
        prompt = dealing_ref[d]
        start = starts_ref[prompt]
        length = lengths_ref[prompt]
        first = lax.rem(lax.rem(home - start, devices) + devices, devices)
        first_row = lax.div(start + first - home, devices)
        count = jnp.minimum(lax.div(length - first + devices - 1, devices), capacity)
        hits = (row_gap == first_row) & (rank_ids < count)
        pick_ref[pl.ds(pl.multiple_of(d * capacity, capacity), capacity), :] = hits.astype(
            pick_ref.dtype
        )
        return carry

    lax.fori_loop(0, devices, pick_rows, 0)
    values = hidden_ref[...].astype(jnp.float32)
    inv_rms = lax.rsqrt(jnp.mean(values * values, axis=-1, keepdims=True) + EPS)
    normed = (values * inv_rms * norm_gain_ref[...].astype(jnp.float32)[None, :]).astype(
        jnp.bfloat16
    )
    cosine = cos_ref[...]
    sine = sin_ref[...]
    column = 0
    for w_ref, gain_ref in ((wq_ref, qgain_ref), (wk_ref, kgain_ref)):
        rows = jnp.dot(normed, w_ref[...], preferred_element_type=jnp.float32)
        gain = gain_ref[...].astype(jnp.float32)
        for h in range(rows.shape[1] // head_dim):
            head = rows[:, h * head_dim : (h + 1) * head_dim]
            head_inv = lax.rsqrt(jnp.mean(head * head, axis=-1, keepdims=True) + EPS)
            head = head * head_inv * gain
            swapped = pltpu.roll(head, head_dim // 2, 1)
            qkv_ref[:, column : column + head_dim] = (head * cosine + swapped * sine).astype(
                jnp.bfloat16
            )
            column += head_dim
    v_width = wv_ref.shape[1]
    qkv_ref[:, column : column + v_width] = jnp.dot(
        normed, wv_ref[...], preferred_element_type=jnp.float32
    ).astype(jnp.bfloat16)
    qkv = qkv_ref[...]
    out_rows = out_ref.shape[0]
    block = out_rows // 4
    for b in range(4):
        rows_here = pl.ds(b * block, block)
        out_ref[rows_here, :] = jnp.dot(
            pick_ref[rows_here, :], qkv, preferred_element_type=jnp.float32
        ).astype(out_ref.dtype)


def prepare(
    hidden, lengths, dealing, home, norm_gain, w_query, w_key, w_value, query_gain, key_gain,
    positions, capacity,
):
    tok_rows, features = hidden.shape
    head_dim = query_gain.shape[0]
    half_width = head_dim // 2
    width = w_query.shape[1] + w_key.shape[1] + w_value.shape[1]
    devices = dealing.shape[0]
    out_rows = devices * capacity
    frequency = THETA ** (-(jnp.arange(half_width).astype(jnp.float32) * 2.0) / head_dim)
    frequency = jnp.concatenate([frequency, frequency])
    angles = positions.astype(jnp.float32)[:, None] * frequency[None, :]
    sign = jnp.where(jnp.arange(head_dim) < half_width, -1.0, 1.0).astype(jnp.float32)
    cos_full = jnp.cos(angles)
    sin_signed = jnp.sin(angles) * sign[None, :]
    vmem = pl.BlockSpec(memory_space=pltpu.VMEM)
    smem = pl.BlockSpec(memory_space=pltpu.SMEM)
    return pl.pallas_call(
        lambda *refs: prep_kernel(*refs, head_dim=head_dim, capacity=capacity),
        out_shape=jax.ShapeDtypeStruct((out_rows, width), jnp.bfloat16),
        in_specs=[smem] * 3 + [vmem] * 9,
        out_specs=vmem,
        scratch_shapes=[
            pltpu.VMEM((tok_rows, width), jnp.bfloat16),
            pltpu.VMEM((out_rows, tok_rows), jnp.bfloat16),
            pltpu.SMEM((lengths.shape[0],), jnp.int32),
        ],
        cost_estimate=pl.CostEstimate(
            flops=2 * tok_rows * features * width + 2 * out_rows * tok_rows * width,
            transcendentals=tok_rows * 8,
            bytes_accessed=hidden.size * 2 + features * width * 2 + out_rows * width * 2,
        ),
    )(
        lengths,
        dealing,
        home,
        hidden,
        norm_gain,
        w_query,
        w_key,
        w_value,
        query_gain[None, :],
        key_gain[None, :],
        cos_full,
        sin_signed,
    )


def attention_kernel(qkv_ref, qpos_ref, kpos_ref, out_ref, *, q_width, k_width, head_dim, blocks):
    rows = qkv_ref.shape[0]
    block = rows // blocks
    kv_heads = k_width // head_dim
    group = q_width // head_dim // kv_heads
    scale = head_dim ** (-0.5)
    for i in range(blocks):
        key_rows = rows
        rows_here = pl.ds(i * block, block)
        allowed = kpos_ref[:, :key_rows] <= qpos_ref[rows_here, :]
        for h in range(kv_heads):
            k_col = q_width + h * head_dim
            v_col = q_width + k_width + h * head_dim
            keys = qkv_ref[:key_rows, k_col : k_col + head_dim]
            values = qkv_ref[:key_rows, v_col : v_col + head_dim]
            q_cols = [(h * group + g) * head_dim for g in range(group)]
            queries = jnp.concatenate(
                [qkv_ref[rows_here, c : c + head_dim] for c in q_cols], axis=0
            )
            scores = lax.dot_general(
                queries,
                keys,
                (((1,), (1,)), ((), ())),
                preferred_element_type=jnp.float32,
            ) * scale
            scores = jnp.where(jnp.concatenate([allowed] * group, axis=0), scores, -jnp.inf)
            row_max = jnp.max(scores, axis=-1, keepdims=True)
            weights = jnp.exp(scores - row_max)
            weights = (weights / jnp.sum(weights, axis=-1, keepdims=True)).astype(jnp.bfloat16)
            mixed = jnp.dot(weights, values, preferred_element_type=jnp.float32)
            for g, c in enumerate(q_cols):
                out_ref[rows_here, c : c + head_dim] = mixed[g * block : (g + 1) * block].astype(
                    out_ref.dtype
                )


def attend(qkv_slot, query_pos, key_pos, q_width, k_width, head_dim):
    rows = qkv_slot.shape[0]
    blocks = 2
    heads = q_width // head_dim
    causal_pairs = blocks * blocks
    pair_flops = 4 * (rows // blocks) ** 2 * head_dim
    vmem = pl.BlockSpec(memory_space=pltpu.VMEM)
    return pl.pallas_call(
        lambda *refs: attention_kernel(
            *refs, q_width=q_width, k_width=k_width, head_dim=head_dim, blocks=blocks
        ),
        out_shape=jax.ShapeDtypeStruct((rows, q_width), jnp.bfloat16),
        in_specs=[vmem, vmem, vmem],
        out_specs=vmem,
        cost_estimate=pl.CostEstimate(
            flops=heads * causal_pairs * pair_flops,
            transcendentals=heads * causal_pairs * (rows // blocks) ** 2,
            bytes_accessed=qkv_slot.size * 2 + rows * q_width * 2,
        ),
    )(qkv_slot, query_pos[:, None], key_pos[None, :])


def on_device(
    hidden, lengths, dealing, norm_gain, w_query, w_key, w_value, query_gain, key_gain, w_out
):
    devices = lax.axis_size("req")
    home_index = lax.axis_index("req")
    slice_index = lax.axis_index("tp")
    tok_rows, features = hidden.shape
    head_dim = query_gain.shape[0]
    out_width = w_out.shape[1]
    q_width = w_query.shape[1]
    k_width = w_key.shape[1]
    slot_len = 4 * tok_rows
    capacity = slot_len // devices
    prompt_total = lengths.shape[0]
    prompt_ids = jnp.arange(prompt_total, dtype=jnp.int32)
    prompt_ends = jnp.cumsum(lengths)
    starts = prompt_ends - lengths
    packed_ids = jnp.arange(tok_rows, dtype=jnp.int32) * devices + home_index
    segment = jnp.sum((packed_ids[:, None] >= prompt_ends[None, :]).astype(jnp.int32), axis=1)
    seg_onehot = (segment[:, None] == prompt_ids[None, :]).astype(jnp.int32)
    positions = packed_ids - jnp.sum(seg_onehot * starts[None, :], axis=1)
    picked = prepare(
        hidden,
        lengths,
        dealing,
        jnp.reshape(home_index, (1,)).astype(jnp.int32),
        norm_gain,
        w_query,
        w_key,
        w_value,
        query_gain,
        key_gain,
        positions,
        capacity,
    )
    picked, lengths, dealing, starts, seg_onehot = lax.optimization_barrier(
        (picked, lengths, dealing, starts, seg_onehot)
    )
    inverse = jnp.zeros((prompt_total,), jnp.int32).at[dealing].set(prompt_ids)
    deal_hot = (dealing[:, None] == prompt_ids[None, :]).astype(jnp.int32)
    dealt_starts = jnp.sum(deal_hot * starts[None, :], axis=1)
    dealt_lengths = jnp.sum(deal_hot * lengths[None, :], axis=1)
    ranks = jnp.arange(capacity, dtype=jnp.int32)
    my_start = lax.dynamic_index_in_dim(dealt_starts, home_index, 0, keepdims=False)
    my_length = lax.dynamic_index_in_dim(dealt_lengths, home_index, 0, keepdims=False)
    roll_shift = jnp.mod(my_start, devices)
    my_slots = jnp.sum(seg_onehot * inverse[None, :], axis=1)
    back_rows = my_slots * capacity + positions // devices
    arrived = lax.all_to_all(
        picked.reshape(devices, capacity, picked.shape[1]),
        "req",
        split_axis=0,
        concat_axis=0,
        tiled=True,
    )
    source_ids = jnp.arange(devices, dtype=jnp.int32)
    arrived_pos = (
        ranks[None, :] * devices + jnp.mod(source_ids[:, None] - my_start, devices)
    ).reshape(-1)
    key_pos = jnp.where(arrived_pos < my_length, arrived_pos, 1 << 30)
    mixture = attend(
        arrived.reshape(slot_len, arrived.shape[2]), arrived_pos, key_pos, q_width, k_width, head_dim
    )
    returned = lax.all_to_all(
        mixture.reshape(devices, capacity, mixture.shape[1]),
        "req",
        split_axis=0,
        concat_axis=0,
        tiled=True,
    )
    attended = jnp.take(returned.reshape(capacity * devices, -1), back_rows, axis=0)
    kv_rows = (
        jnp.roll(arrived[:, :, q_width:], -roll_shift, axis=0)
        .transpose(1, 0, 2)
        .reshape(slot_len, -1)
    )
    kv_cache = jnp.stack([kv_rows[:, :k_width], kv_rows[:, k_width:]])[:, None]
    tp_size = lax.axis_size("tp")
    w_rows = w_out.shape[0] // tp_size
    passes = []
    for shift in sorted(range(1, tp_size), key=lambda s: min(s, tp_size - s)):
        passed = lax.ppermute(
            attended, "tp", perm=[(i, (i + shift) % tp_size) for i in range(tp_size)]
        )
        passes.append((passed, jnp.mod(slice_index - shift, tp_size)))
    passes.append((attended, slice_index))
    summed = None
    for passed, source in passes:
        product = jnp.dot(
            passed,
            lax.dynamic_slice_in_dim(w_out, source * w_rows, w_rows, 0),
            preferred_element_type=jnp.float32,
        )
        summed = product if summed is None else summed + product
    branch = lax.optimization_barrier(summed.astype(jnp.bfloat16))
    residual = lax.dynamic_slice_in_dim(hidden, slice_index * out_width, out_width, 1)
    hidden_out = (residual.astype(jnp.float32) + branch.astype(jnp.float32)).astype(jnp.bfloat16)
    return (hidden_out, kv_cache)


def solution(mesh):
    in_specs = (
        P("req", None),
        P(),
        P(),
        P(),
        P(None, "tp"),
        P(None, "tp"),
        P(None, "tp"),
        P(),
        P(),
        P(None, "tp"),
    )
    out_specs = (P("req", "tp"), P(None, "req", None, "tp"))
    return jax.shard_map(
        on_device, mesh=mesh, in_specs=in_specs, out_specs=out_specs, check_vma=False
    )
```
